512 devices in a mesh: section: 4 (over x_hi, core), ctx: 32 (over x_lo, z), dp: 4 (over y).
Axes of the slice: x: 4 (x_hi: 2, x_lo: 2; x = x_hi * 2 + x_lo), y: 4, z: 16, core: 2. Of those that a mesh axis runs over, the one named last changes fastest.
Arguments:
- inputs: bfloat16 [4, 8192, 4096], P('section', 'ctx', 'dp'), may hold values from -6 to 6
- upstream: bfloat16 [4, 8192, 4096], P('section', 'ctx', 'dp'), may hold values from -6 to 6
- short_filter: bfloat16 [4, 21, 256], P('section', None, 'dp'), may hold values from -2 to 2
- medium_filter: bfloat16 [4, 128, 256], P('section', None, 'dp'), may hold values from -0.5 to 0.5
Outputs:
- incoming: bfloat16 [4, 8192, 4096], P('section', 'ctx', 'dp')
- grad_short: float32 [4, 21, 256], P('section', None, ('dp', 'ctx'))
- grad_medium: float32 [4, 128, 256], P('section', None, ('dp', 'ctx'))
The draws below stay inside these ranges and needn't reach their ends.
All inputs are finite; a program needn't handle non-finite values.
Results may differ from the reference program's by a relative error of at most 0.0071.
Values may be sent and summed in bfloat16 or wider, within the bound.
No kernel may reach another device: no remote copies, remote signals or barrier semaphores. Data moves between devices by JAX's collectives and lax.ppermute only.
A program may use at most 64 MiB of HBM per device.

```python
import jax
import jax.numpy as jnp
from jax import lax

C = 4096
SK = 7
MK = 128
G = 256
SECTIONS = 4
SEQ = 8192


def raised(drawn, stream_key, source, target, parts, factor):
    owner, partner = [(jnp.arange(drawn.shape[dim]) // (drawn.shape[dim] // parts)).reshape([-1 if axis == dim else 1 for axis in range(drawn.ndim)]) for dim in (source, target)]
    chosen = jax.random.permutation(stream_key, parts)[partner]
    strong = (owner == chosen) | (owner == (partner + parts // 2) % parts)
    return jnp.where(strong, factor * drawn, drawn)


def levels(key, shape, shards, low, largest):
    loudness, own = 1.0, jax.random.fold_in(key, 6)
    for position, blocks in shards:
        heights = jnp.exp(jax.random.uniform(jax.random.fold_in(own, position), (blocks,), jnp.float32, low / len(shards), largest / len(shards)))
        loudness = loudness * jnp.repeat(heights, shape[position] // blocks).reshape([-1 if axis == position else 1 for axis in range(len(shape))])
    return loudness


def gaussian(key, dims, scale, most, cuts=(), kind=jnp.bfloat16):
    entries = jax.random.normal(key, dims, jnp.float32) * scale
    if len(cuts) > 0:
        entries = levels(key, dims, cuts, -0.22, 0.18) * entries
    return jnp.clip(entries, min=-most, max=most).astype(kind)


def bell_draw_with(rng, dims, spread, most, split, heavy, kind=jnp.bfloat16):
    result = spread * jax.random.normal(rng, dims, jnp.float32)
    if split:
        result = result * levels(rng, dims, split, -0.22, 0.18)
    return jnp.clip(raised(result, jax.random.fold_in(rng, 3), *heavy), -most, most).astype(kind)


def setup_inputs(seed: int = 0) -> dict:
    keys = jax.random.split(jax.random.key(seed), 5)
    inputs = gaussian(keys[0], (SECTIONS, SEQ, C), 1.0, 6.0, ((0, 4), (1, 32), (2, 4)))
    upstream = bell_draw_with(keys[1], (SECTIONS, SEQ, C), 1.0, 6.0, ((0, 4), (1, 32), (2, 4)), (1, 2, 32, 2.75))
    short_filter = gaussian(keys[2], (SECTIONS, 3 * SK, G), SK ** -0.5, 2.0, ((0, 4), (2, 4)))
    medium_filter = gaussian(keys[3], (SECTIONS, MK, G), MK ** -0.5, 0.5, ((0, 4), (2, 4)))
    return dict(inputs=inputs, upstream=upstream, short_filter=short_filter, medium_filter=medium_filter)


def causal_mix(signal, taps):
    length = signal.shape[0] + taps.shape[0]
    spectrum = jnp.fft.rfft(signal, n=length, axis=0) * jnp.fft.rfft(taps, n=length, axis=0)
    return jnp.fft.irfft(spectrum, n=length, axis=0)[: signal.shape[0]].astype(signal.dtype)


def lagged(values_in, offset):
    return jnp.pad(values_in, ((offset, 0), (0, 0)))[: values_in.shape[0]]


def leading(values_in, offset):
    return jnp.pad(values_in, ((0, offset), (0, 0)))[offset:]


def one_section(operands):
    signal, grad_out, short_taps, medium_taps = operands
    seq_len, chan_count = signal.shape
    group_count = medium_taps.shape[1]
    group_width = chan_count // group_count
    chan_short = jnp.repeat(short_taps.astype(jnp.float32).reshape(3, SK, group_count), group_width, axis=2)
    chan_medium = jnp.repeat(medium_taps.astype(jnp.float32), group_width, axis=1)
    signal_f = signal.astype(jnp.float32)
    features = []
    for branch in range(3):
        running = jnp.zeros((seq_len, chan_count), jnp.float32)
        for offset in range(SK):
            running = running + chan_short[branch, offset] * lagged(signal_f, offset)
        features.append(running.astype(jnp.bfloat16))
    query_in, key_in, value_in = features
    products = (key_in.astype(jnp.float32) * value_in.astype(jnp.float32)).astype(jnp.bfloat16)
    mixed_out = causal_mix(products.astype(jnp.float32), chan_medium)
    grad_f = grad_out.astype(jnp.float32)
    query_grad = (grad_f * mixed_out).astype(jnp.bfloat16)
    gate_grad = (grad_f * query_in.astype(jnp.float32)).astype(jnp.bfloat16)
    kv_grad = jnp.flip(causal_mix(jnp.flip(gate_grad.astype(jnp.float32), 0), chan_medium), 0)
    key_grad = (kv_grad * value_in.astype(jnp.float32)).astype(jnp.bfloat16)
    value_grad = (kv_grad * key_in.astype(jnp.float32)).astype(jnp.bfloat16)
    input_grad = jnp.zeros((seq_len, chan_count), jnp.float32)
    short_rows = []
    for branch, feature_grad in enumerate([query_grad, key_grad, value_grad]):
        feature_f = feature_grad.astype(jnp.float32)
        for offset in range(SK):
            input_grad = input_grad + chan_short[branch, offset] * leading(feature_f, offset)
            short_rows.append(jnp.sum(feature_f * lagged(signal_f, offset), axis=0))
    short_grad = jnp.stack(short_rows).reshape(3 * SK, group_count, group_width).sum(-1)
    length = seq_len + MK
    spectrum = jnp.fft.rfft(gate_grad.astype(jnp.float32), n=length, axis=0) * jnp.conj(jnp.fft.rfft(products.astype(jnp.float32), n=length, axis=0))
    medium_grad = jnp.fft.irfft(spectrum, n=length, axis=0)[:MK].astype(signal_f.dtype)
    medium_grad = medium_grad.reshape(MK, group_count, group_width).sum(-1)
    return input_grad.astype(jnp.bfloat16), short_grad, medium_grad


def reference(inputs, upstream, short_filter, medium_filter):
    input_grad, short_grad, medium_grad = lax.map(one_section, (inputs, upstream, short_filter, medium_filter))
    incoming = jnp.concatenate([input_grad[1:], jnp.zeros_like(input_grad[:1])], 0)
    return incoming, short_grad, medium_grad
```

```python
from functools import partial

import jax
import jax.numpy as jnp
from jax import lax
from jax.sharding import PartitionSpec as P


def passed_along(block, axis, distance):
    devices = range(lax.axis_size(axis))
    route = [(i - distance, i) for i in devices if i - distance in devices]
    return lax.ppermute(block, axis, route)


def owned_sum(partial_terms, axis):
    axis_len = lax.axis_size(axis)
    row_count, col_count = partial_terms.shape
    blocks = partial_terms.reshape(row_count, axis_len, col_count // axis_len)
    gathered = lax.all_gather(blocks, axis, axis=0, tiled=False)
    mine = lax.dynamic_index_in_dim(gathered, lax.axis_index(axis), axis=2, keepdims=False)
    return jnp.sum(mine, axis=0)


def band_matrix(filter_taps, out_rows):
    tap_count, group_count = filter_taps.shape
    leading = jnp.flip(filter_taps, 0).T
    padded = jnp.concatenate([leading, jnp.zeros((group_count, out_rows), filter_taps.dtype)], 1)
    span_len = out_rows + tap_count - 1
    tiled_rows = jnp.tile(padded, (1, out_rows))[:, : out_rows * span_len]
    return tiled_rows.reshape(group_count, out_rows, span_len)


def diagonal_sums(cross_terms, tap_count):
    group_count, out_rows, span_len = cross_terms.shape
    flat_view = jnp.pad(
        cross_terms.reshape(group_count, out_rows * span_len), ((0, 0), (0, out_rows))
    )
    skewed = flat_view.reshape(group_count, out_rows, span_len + 1)
    return jnp.flip(jnp.sum(skewed[:, :, :tap_count], axis=1), 1)


def short_features(padded, chan_short, out_rows):
    lag_count = chan_short.shape[1]
    running = jnp.zeros((3, out_rows, padded.shape[1]), jnp.float32)
    for offset in range(lag_count):
        first_row = lag_count - 1 - offset
        running = running + chan_short[:, offset, None, :] * padded[
            None, first_row : first_row + out_rows
        ].astype(jnp.float32)
    return running.astype(jnp.bfloat16)


def medium_block(operands, row_block):
    filter_blk, kv_blk, gate_blk = operands
    tap_count = filter_blk.shape[0]
    seq_rows = gate_blk.shape[0] - tap_count + 1
    span_len = row_block + tap_count - 1
    toeplitz = band_matrix(filter_blk, row_block)

    def row_part(start):
        kv_win = lax.dynamic_slice_in_dim(kv_blk, start, span_len, 0)
        gate_win = lax.dynamic_slice_in_dim(gate_blk, start, span_len, 0)
        gate_rows = gate_win[:row_block]
        mixed_out = jnp.einsum("gts,sgc->tgc", toeplitz, kv_win, preferred_element_type=jnp.float32)
        back_out = jnp.flip(
            jnp.einsum(
                "gts,sgc->tgc", toeplitz, jnp.flip(gate_win, 0), preferred_element_type=jnp.float32
            ),
            0,
        )
        cross_terms = jnp.einsum(
            "tgc,sgc->gts", gate_rows, kv_win, preferred_element_type=jnp.float32
        )
        return (mixed_out, back_out, diagonal_sums(cross_terms, tap_count).T)

    starts = jnp.arange(seq_rows // row_block, dtype=jnp.int32) * row_block
    mixed_out, back_out, taps_grad = lax.map(row_part, starts)
    full_shape = (seq_rows,) + mixed_out.shape[2:]
    return (mixed_out.reshape(full_shape), back_out.reshape(full_shape), jnp.sum(taps_grad, 0))


def split_groups(values_in, block_count, group_width):
    length = values_in.shape[0]
    return values_in.reshape(length, block_count, -1, group_width).transpose(1, 0, 2, 3)


def join_groups(blocks):
    block_count, length, block_groups, group_width = blocks.shape
    return blocks.transpose(1, 0, 2, 3).reshape(length, block_count * block_groups * group_width)


def per_device(inputs, upstream, short_filter, medium_filter):
    signal = inputs[0]
    grad_out = upstream[0]
    seq_rows, chan_count = signal.shape
    tap_count = medium_filter.shape[1]
    group_count = medium_filter.shape[2]
    lag_count = short_filter.shape[1] // 3
    group_width = chan_count // group_count
    short_rim = lag_count - 1
    medium_rim = tap_count - 1
    chan_short = jnp.broadcast_to(
        short_filter[0].astype(jnp.float32).reshape(3, lag_count, group_count, 1),
        (3, lag_count, group_count, group_width),
    ).reshape(3, lag_count, chan_count)
    medium_taps = medium_filter[0]
    zero_rim = jnp.zeros((short_rim, chan_count), jnp.bfloat16)
    features_local = short_features(jnp.concatenate([zero_rim, signal], 0), chan_short, seq_rows)
    kv_local = (
        features_local[1].astype(jnp.float32) * features_local[2].astype(jnp.float32)
    ).astype(jnp.bfloat16)
    signal_rim, kv_rim = passed_along(
        (signal[seq_rows - short_rim :], kv_local[seq_rows - medium_rim :]), "ctx", 1
    )
    signal_pad = jnp.concatenate([signal_rim, signal], 0)
    head_features = short_features(signal_pad[: 2 * short_rim], chan_short, short_rim)
    features = jnp.concatenate([head_features, features_local[:, short_rim:]], 1)
    query_in = features[0]
    key_in = features[1]
    value_in = features[2]
    head_products = (
        key_in[:short_rim].astype(jnp.float32) * value_in[:short_rim].astype(jnp.float32)
    ).astype(jnp.bfloat16)
    products = jnp.concatenate([head_products, kv_local[short_rim:]], 0)
    kv_pad = jnp.concatenate([kv_rim, products], 0)
    gate_grad = (grad_out.astype(jnp.float32) * query_in.astype(jnp.float32)).astype(jnp.bfloat16)
    gate_rim = passed_along(gate_grad[:medium_rim], "ctx", -1)
    gate_ext = jnp.concatenate([gate_grad, gate_rim], 0)
    block_groups = 8
    block_count = group_count // block_groups
    row_block = 128
    taps_blocks = medium_taps.reshape(tap_count, block_count, block_groups).transpose(1, 0, 2)
    mixed_blocks, back_blocks, grad_blocks = lax.map(
        partial(medium_block, row_block=row_block),
        (
            taps_blocks,
            split_groups(kv_pad, block_count, group_width),
            split_groups(gate_ext, block_count, group_width),
        ),
    )
    mixed_out = join_groups(mixed_blocks)
    back_out = join_groups(back_blocks)
    taps_grad = grad_blocks.transpose(1, 0, 2).reshape(tap_count, group_count)
    query_grad = (grad_out.astype(jnp.float32) * mixed_out).astype(jnp.bfloat16)
    key_grad = (back_out * value_in.astype(jnp.float32)).astype(jnp.bfloat16)
    value_grad = (back_out * key_in.astype(jnp.float32)).astype(jnp.bfloat16)
    feature_grads = jnp.stack([query_grad, key_grad, value_grad])
    feature_rim = passed_along(feature_grads[:, :short_rim], "ctx", -1)
    grads_pad = jnp.concatenate([feature_grads, feature_rim], 1)
    running = jnp.zeros((seq_rows, chan_count), jnp.float32)
    short_rows = []
    for offset in range(lag_count):
        running = running + jnp.sum(
            chan_short[:, offset, None, :]
            * grads_pad[:, offset : offset + seq_rows].astype(jnp.float32),
            axis=0,
        )
        lag_start = short_rim - offset
        short_rows.append(
            jnp.sum(
                feature_grads.astype(jnp.float32)
                * signal_pad[None, lag_start : lag_start + seq_rows].astype(jnp.float32),
                axis=1,
            )
        )
    input_grad = running.astype(jnp.bfloat16)
    short_grad = jnp.stack(short_rows, 1).reshape(3 * lag_count, group_count, group_width).sum(-1)
    short_part = owned_sum(short_grad, "ctx")[None]
    medium_part = owned_sum(taps_grad, "ctx")[None]
    incoming = passed_along(input_grad[None], "section", -1)
    return (incoming, short_part, medium_part)


def solution(mesh):
    in_specs = (
        P("section", "ctx", "dp"),
        P("section", "ctx", "dp"),
        P("section", None, "dp"),
        P("section", None, "dp"),
    )
    out_specs = (
        P("section", "ctx", "dp"),
        P("section", None, ("dp", "ctx")),
        P("section", None, ("dp", "ctx")),
    )
    return jax.shard_map(
        per_device, mesh=mesh, in_specs=in_specs, out_specs=out_specs, check_vma=False
    )
```

```python
from functools import partial

import jax
import jax.numpy as jnp
from jax import lax
from jax.sharding import PartitionSpec as P


def passed_along(block, axis, distance):
    devices = range(lax.axis_size(axis))
    route = [(i - distance, i) for i in devices if i - distance in devices]
    return lax.ppermute(block, axis, route)


def owned_sum(partial_terms, axis):
    axis_len = lax.axis_size(axis)
    row_count, col_count = partial_terms.shape
    width = col_count // axis_len
    chunks = partial_terms.reshape(row_count, axis_len, width).transpose(1, 2, 0)
    chunks = chunks.reshape(axis_len, width * row_count)
    if axis_len & (axis_len - 1):
        gathered = lax.all_gather(chunks, axis, axis=0, tiled=False)
        return jnp.sum(gathered[:, lax.axis_index(axis)], axis=0).reshape(width, row_count).T
    here = lax.axis_index(axis)
    span = axis_len // 2
    while span >= 1:
        upper = (here // span) % 2
        kept = lax.dynamic_slice_in_dim(chunks, upper * span, span, 0)
        sent = lax.dynamic_slice_in_dim(chunks, (1 - upper) * span, span, 0)
        route = [(i, i ^ span) for i in range(axis_len)]
        chunks = kept + lax.ppermute(sent, axis, route)
        span //= 2
    return chunks[0].reshape(width, row_count).T


def band_matrix(filter_taps, out_rows):
    tap_count, group_count = filter_taps.shape
    leading = jnp.flip(filter_taps, 0).T
    padded = jnp.concatenate([leading, jnp.zeros((group_count, out_rows), filter_taps.dtype)], 1)
    span_len = out_rows + tap_count - 1
    tiled_rows = jnp.tile(padded, (1, out_rows))[:, : out_rows * span_len]
    return tiled_rows.reshape(group_count, out_rows, span_len)


def diagonal_sums(cross_terms, tap_count):
    group_count, out_rows, span_len = cross_terms.shape
    flat_view = jnp.pad(
        cross_terms.reshape(group_count, out_rows * span_len), ((0, 0), (0, out_rows))
    )
    skewed = flat_view.reshape(group_count, out_rows, span_len + 1)
    return jnp.flip(jnp.sum(skewed[:, :, :tap_count], axis=1), 1)


def short_features(padded, chan_short, out_rows):
    lag_count = chan_short.shape[1]
    running = jnp.zeros((3, out_rows, padded.shape[1]), jnp.float32)
    for offset in range(lag_count):
        first_row = lag_count - 1 - offset
        running = running + chan_short[:, offset, None, :] * padded[
            None, first_row : first_row + out_rows
        ].astype(jnp.float32)
    return running.astype(jnp.bfloat16)


def medium_block(operands, row_block):
    filter_blk, kv_blk, gate_blk = operands
    tap_count = filter_blk.shape[0]
    seq_rows = gate_blk.shape[0] - tap_count + 1
    span_len = row_block + tap_count - 1
    toeplitz = band_matrix(filter_blk, row_block)

    def row_part(start):
        kv_win = lax.dynamic_slice_in_dim(kv_blk, start, span_len, 0)
        gate_win = lax.dynamic_slice_in_dim(gate_blk, start, span_len, 0)
        gate_rows = gate_win[:row_block]
        mixed_out = jnp.einsum("gts,sgc->tgc", toeplitz, kv_win, preferred_element_type=jnp.float32)
        back_out = jnp.flip(
            jnp.einsum(
                "gts,sgc->tgc", toeplitz, jnp.flip(gate_win, 0), preferred_element_type=jnp.float32
            ),
            0,
        )
        cross_terms = jnp.einsum(
            "tgc,sgc->gts", gate_rows, kv_win, preferred_element_type=jnp.float32
        )
        return (mixed_out, back_out, diagonal_sums(cross_terms, tap_count).T)

    starts = jnp.arange(seq_rows // row_block, dtype=jnp.int32) * row_block
    mixed_out, back_out, taps_grad = lax.map(row_part, starts)
    full_shape = (seq_rows,) + mixed_out.shape[2:]
    return (mixed_out.reshape(full_shape), back_out.reshape(full_shape), jnp.sum(taps_grad, 0))


def split_groups(values_in, block_count, group_width):
    length = values_in.shape[0]
    return values_in.reshape(length, block_count, -1, group_width).transpose(1, 0, 2, 3)


def join_groups(blocks):
    block_count, length, block_groups, group_width = blocks.shape
    return blocks.transpose(1, 0, 2, 3).reshape(length, block_count * block_groups * group_width)


def per_device(inputs, upstream, short_filter, medium_filter):
    signal = inputs[0]
    grad_out = upstream[0]
    seq_rows, chan_count = signal.shape
    tap_count = medium_filter.shape[1]
    group_count = medium_filter.shape[2]
    lag_count = short_filter.shape[1] // 3
    group_width = chan_count // group_count
    short_rim = lag_count - 1
    medium_rim = tap_count - 1
    chan_short = jnp.broadcast_to(
        short_filter[0].astype(jnp.float32).reshape(3, lag_count, group_count, 1),
        (3, lag_count, group_count, group_width),
    ).reshape(3, lag_count, chan_count)
    medium_taps = medium_filter[0]
    zero_rim = jnp.zeros((short_rim, chan_count), jnp.bfloat16)
    features_local = short_features(jnp.concatenate([zero_rim, signal], 0), chan_short, seq_rows)
    kv_local = (
        features_local[1].astype(jnp.float32) * features_local[2].astype(jnp.float32)
    ).astype(jnp.bfloat16)
    signal_rim, kv_rim = passed_along(
        (signal[seq_rows - short_rim :], kv_local[seq_rows - medium_rim :]), "ctx", 1
    )
    signal_pad = jnp.concatenate([signal_rim, signal], 0)
    head_features = short_features(signal_pad[: 2 * short_rim], chan_short, short_rim)
    features = jnp.concatenate([head_features, features_local[:, short_rim:]], 1)
    query_in = features[0]
    key_in = features[1]
    value_in = features[2]
    head_products = (
        key_in[:short_rim].astype(jnp.float32) * value_in[:short_rim].astype(jnp.float32)
    ).astype(jnp.bfloat16)
    products = jnp.concatenate([head_products, kv_local[short_rim:]], 0)
    kv_pad = jnp.concatenate([kv_rim, products], 0)
    gate_grad = (grad_out.astype(jnp.float32) * query_in.astype(jnp.float32)).astype(jnp.bfloat16)
    gate_rim = passed_along(gate_grad[:medium_rim], "ctx", -1)
    gate_ext = jnp.concatenate([gate_grad, gate_rim], 0)
    block_groups = 8
    block_count = group_count // block_groups
    row_block = 128
    taps_blocks = medium_taps.reshape(tap_count, block_count, block_groups).transpose(1, 0, 2)
    mixed_blocks, back_blocks, grad_blocks = lax.map(
        partial(medium_block, row_block=row_block),
        (
            taps_blocks,
            split_groups(kv_pad, block_count, group_width),
            split_groups(gate_ext, block_count, group_width),
        ),
    )
    mixed_out = join_groups(mixed_blocks)
    back_out = join_groups(back_blocks)
    taps_grad = grad_blocks.transpose(1, 0, 2).reshape(tap_count, group_count)
    query_grad = (grad_out.astype(jnp.float32) * mixed_out).astype(jnp.bfloat16)
    key_grad = (back_out * value_in.astype(jnp.float32)).astype(jnp.bfloat16)
    value_grad = (back_out * key_in.astype(jnp.float32)).astype(jnp.bfloat16)
    feature_grads = jnp.stack([query_grad, key_grad, value_grad])
    feature_rim = passed_along(feature_grads[:, :short_rim], "ctx", -1)
    grads_pad = jnp.concatenate([feature_grads, feature_rim], 1)
    running = jnp.zeros((seq_rows, chan_count), jnp.float32)
    short_rows = []
    for offset in range(lag_count):
        running = running + jnp.sum(
            chan_short[:, offset, None, :]
            * grads_pad[:, offset : offset + seq_rows].astype(jnp.float32),
            axis=0,
        )
        lag_start = short_rim - offset
        short_rows.append(
            jnp.sum(
                feature_grads.astype(jnp.float32)
                * signal_pad[None, lag_start : lag_start + seq_rows].astype(jnp.float32),
                axis=1,
            )
        )
    input_grad = running.astype(jnp.bfloat16)
    short_grad = jnp.stack(short_rows, 1).reshape(3 * lag_count, group_count, group_width).sum(-1)
    short_part = owned_sum(short_grad, "ctx")[None]
    medium_part = owned_sum(taps_grad, "ctx")[None]
    incoming = passed_along(input_grad[None], "section", -1)
    return (incoming, short_part, medium_part)


def solution(mesh):
    in_specs = (
        P("section", "ctx", "dp"),
        P("section", "ctx", "dp"),
        P("section", None, "dp"),
        P("section", None, "dp"),
    )
    out_specs = (
        P("section", "ctx", "dp"),
        P("section", None, ("dp", "ctx")),
        P("section", None, ("dp", "ctx")),
    )
    return jax.shard_map(
        per_device, mesh=mesh, in_specs=in_specs, out_specs=out_specs, check_vma=False
    )
```

```python
import jax
import jax.numpy as jnp
from jax import lax
from jax.sharding import PartitionSpec as P


def passed_along(block, axis, distance):
    devices = range(lax.axis_size(axis))
    route = [(i - distance, i) for i in devices if i - distance in devices]
    return lax.ppermute(block, axis, route)


def owned_sum(partial_terms, axis):
    axis_len = lax.axis_size(axis)
    row_count, col_count = partial_terms.shape
    width = col_count // axis_len
    chunks = partial_terms.reshape(row_count, axis_len, width).transpose(1, 2, 0)
    chunks = chunks.reshape(axis_len, width * row_count)
    if axis_len & (axis_len - 1):
        gathered = lax.all_gather(chunks, axis, axis=0, tiled=False)
        return jnp.sum(gathered[:, lax.axis_index(axis)], axis=0).reshape(width, row_count).T
    here = lax.axis_index(axis)
    span = axis_len // 2
    while span >= 1:
        upper = (here // span) % 2
        kept = lax.dynamic_slice_in_dim(chunks, upper * span, span, 0)
        sent = lax.dynamic_slice_in_dim(chunks, (1 - upper) * span, span, 0)
        route = [(i, i ^ span) for i in range(axis_len)]
        chunks = kept + lax.ppermute(sent, axis, route)
        span //= 2
    return chunks[0].reshape(width, row_count).T


def band_matrix(filter_taps, out_rows):
    tap_count, group_count = filter_taps.shape
    leading = jnp.flip(filter_taps, 0).T
    padded = jnp.concatenate([leading, jnp.zeros((group_count, out_rows), filter_taps.dtype)], 1)
    span_len = out_rows + tap_count - 1
    tiled_rows = jnp.tile(padded, (1, out_rows))[:, : out_rows * span_len]
    return tiled_rows.reshape(group_count, out_rows, span_len)


def diagonal_sums(cross_terms, tap_count):
    group_count, out_rows, span_len = cross_terms.shape
    flat_view = jnp.pad(
        cross_terms.reshape(group_count, out_rows * span_len), ((0, 0), (0, out_rows))
    )
    skewed = flat_view.reshape(group_count, out_rows, span_len + 1)
    return jnp.flip(jnp.sum(skewed[:, :, :tap_count], axis=1), 1)


def short_features(padded, chan_short, out_rows):
    lag_count = chan_short.shape[1]
    running = jnp.zeros((3, out_rows, padded.shape[1]), jnp.float32)
    for offset in range(lag_count):
        first_row = lag_count - 1 - offset
        running = running + chan_short[:, offset, None, :] * padded[
            None, first_row : first_row + out_rows
        ].astype(jnp.float32)
    return running.astype(jnp.bfloat16)


def medium_terms(medium_taps, kv_pad, gate_ext, row_block):
    tap_count, group_count = medium_taps.shape
    seq_rows = gate_ext.shape[0] - tap_count + 1
    chan_count = kv_pad.shape[1]
    group_width = chan_count // group_count
    span_len = row_block + tap_count - 1
    block_count = seq_rows // row_block
    toeplitz = band_matrix(medium_taps, row_block)
    kv_groups = kv_pad.reshape(-1, group_count, group_width)
    gate_groups = gate_ext.reshape(-1, group_count, group_width)
    starts = [b * row_block for b in range(block_count)]
    kv_win = jnp.concatenate([kv_groups[b : b + span_len] for b in starts], axis=2)
    gate_win = jnp.concatenate([gate_groups[b : b + span_len] for b in starts], axis=2)
    mixed_out = jnp.einsum("gts,sgn->tgn", toeplitz, kv_win, preferred_element_type=jnp.float32)
    back_band = jnp.flip(toeplitz, (1, 2))
    back_out = jnp.einsum("gts,sgn->tgn", back_band, gate_win, preferred_element_type=jnp.float32)
    cross_terms = jnp.einsum(
        "tgn,sgn->gts", gate_win[:row_block], kv_win, preferred_element_type=jnp.float32
    )
    taps_grad = diagonal_sums(cross_terms, tap_count).T

    def unblock(values_in):
        split = values_in.reshape(row_block, group_count, block_count, group_width)
        return split.transpose(2, 0, 1, 3).reshape(seq_rows, chan_count)

    return unblock(mixed_out), unblock(back_out), taps_grad


def per_device(inputs, upstream, short_filter, medium_filter):
    signal = inputs[0]
    grad_out = upstream[0]
    seq_rows, chan_count = signal.shape
    tap_count = medium_filter.shape[1]
    group_count = medium_filter.shape[2]
    lag_count = short_filter.shape[1] // 3
    group_width = chan_count // group_count
    short_rim = lag_count - 1
    medium_rim = tap_count - 1
    chan_short = jnp.broadcast_to(
        short_filter[0].astype(jnp.float32).reshape(3, lag_count, group_count, 1),
        (3, lag_count, group_count, group_width),
    ).reshape(3, lag_count, chan_count)
    medium_taps = medium_filter[0]
    zero_rim = jnp.zeros((short_rim, chan_count), jnp.bfloat16)
    features_local = short_features(jnp.concatenate([zero_rim, signal], 0), chan_short, seq_rows)
    kv_local = (
        features_local[1].astype(jnp.float32) * features_local[2].astype(jnp.float32)
    ).astype(jnp.bfloat16)
    signal_rim, kv_rim = passed_along(
        (signal[seq_rows - short_rim :], kv_local[seq_rows - medium_rim :]), "ctx", 1
    )
    signal_pad = jnp.concatenate([signal_rim, signal], 0)
    head_features = short_features(signal_pad[: 2 * short_rim], chan_short, short_rim)
    features = jnp.concatenate([head_features, features_local[:, short_rim:]], 1)
    query_in = features[0]
    key_in = features[1]
    value_in = features[2]
    head_products = (
        key_in[:short_rim].astype(jnp.float32) * value_in[:short_rim].astype(jnp.float32)
    ).astype(jnp.bfloat16)
    products = jnp.concatenate([head_products, kv_local[short_rim:]], 0)
    kv_pad = jnp.concatenate([kv_rim, products], 0)
    gate_grad = (grad_out.astype(jnp.float32) * query_in.astype(jnp.float32)).astype(jnp.bfloat16)
    gate_rim = passed_along(gate_grad[:medium_rim], "ctx", -1)
    gate_ext = jnp.concatenate([gate_grad, gate_rim], 0)
    mixed_out, back_out, taps_grad = medium_terms(medium_taps, kv_pad, gate_ext, 128)
    query_grad = (grad_out.astype(jnp.float32) * mixed_out).astype(jnp.bfloat16)
    key_grad = (back_out * value_in.astype(jnp.float32)).astype(jnp.bfloat16)
    value_grad = (back_out * key_in.astype(jnp.float32)).astype(jnp.bfloat16)
    feature_grads = jnp.stack([query_grad, key_grad, value_grad])
    feature_rim = passed_along(feature_grads[:, :short_rim], "ctx", -1)
    grads_pad = jnp.concatenate([feature_grads, feature_rim], 1)
    running = jnp.zeros((seq_rows, chan_count), jnp.float32)
    short_rows = []
    for offset in range(lag_count):
        running = running + jnp.sum(
            chan_short[:, offset, None, :]
            * grads_pad[:, offset : offset + seq_rows].astype(jnp.float32),
            axis=0,
        )
        lag_start = short_rim - offset
        short_rows.append(
            jnp.sum(
                feature_grads.astype(jnp.float32)
                * signal_pad[None, lag_start : lag_start + seq_rows].astype(jnp.float32),
                axis=1,
            )
        )
    input_grad = running.astype(jnp.bfloat16)
    short_grad = jnp.stack(short_rows, 1).reshape(3 * lag_count, group_count, group_width).sum(-1)
    short_part = owned_sum(short_grad, "ctx")[None]
    medium_part = owned_sum(taps_grad, "ctx")[None]
    incoming = passed_along(input_grad[None], "section", -1)
    return (incoming, short_part, medium_part)


def solution(mesh):
    in_specs = (
        P("section", "ctx", "dp"),
        P("section", "ctx", "dp"),
        P("section", None, "dp"),
        P("section", None, "dp"),
    )
    out_specs = (
        P("section", "ctx", "dp"),
        P("section", None, ("dp", "ctx")),
        P("section", None, ("dp", "ctx")),
    )
    return jax.shard_map(
        per_device, mesh=mesh, in_specs=in_specs, out_specs=out_specs, check_vma=False
    )
```

```python
import jax
import jax.numpy as jnp
from jax import lax
from jax.sharding import PartitionSpec as P


def passed_along(block, axis, distance):
    devices = range(lax.axis_size(axis))
    route = [(i - distance, i) for i in devices if i - distance in devices]
    return lax.ppermute(block, axis, route)


def owned_sum(partial_terms, axis):
    axis_len = lax.axis_size(axis)
    row_count, col_count = partial_terms.shape
    width = col_count // axis_len
    chunks = partial_terms.reshape(row_count, axis_len, width).transpose(1, 2, 0)
    chunks = chunks.reshape(axis_len, width * row_count)
    if axis_len & (axis_len - 1):
        gathered = lax.all_gather(chunks, axis, axis=0, tiled=False)
        return jnp.sum(gathered[:, lax.axis_index(axis)], axis=0).reshape(width, row_count).T
    here = lax.axis_index(axis)
    span = axis_len // 2
    while span >= 1:
        upper = (here // span) % 2
        kept = lax.dynamic_slice_in_dim(chunks, upper * span, span, 0)
        sent = lax.dynamic_slice_in_dim(chunks, (1 - upper) * span, span, 0)
        route = [(i, i ^ span) for i in range(axis_len)]
        chunks = kept + lax.ppermute(sent, axis, route)
        span //= 2
    return chunks[0].reshape(width, row_count).T


def band_matrix(filter_taps, out_rows):
    tap_count, group_count = filter_taps.shape
    leading = jnp.flip(filter_taps, 0).T
    padded = jnp.concatenate([leading, jnp.zeros((group_count, out_rows), filter_taps.dtype)], 1)
    span_len = out_rows + tap_count - 1
    tiled_rows = jnp.tile(padded, (1, out_rows))[:, : out_rows * span_len]
    return tiled_rows.reshape(group_count, out_rows, span_len)


def diagonal_sums(cross_terms, tap_count):
    group_count, out_rows, span_len = cross_terms.shape
    flat_view = jnp.pad(
        cross_terms.reshape(group_count, out_rows * span_len), ((0, 0), (0, out_rows))
    )
    skewed = flat_view.reshape(group_count, out_rows, span_len + 1)
    return jnp.flip(jnp.sum(skewed[:, :, :tap_count], axis=1), 1)


def short_features(padded, chan_short, out_rows):
    lag_count = chan_short.shape[1]
    running = jnp.zeros((3, out_rows, padded.shape[1]), jnp.float32)
    for offset in range(lag_count):
        first_row = lag_count - 1 - offset
        running = running + chan_short[:, offset, None, :] * padded[
            None, first_row : first_row + out_rows
        ].astype(jnp.float32)
    return running.astype(jnp.bfloat16)


def medium_terms(medium_taps, kv_pad, gate_ext, row_block):
    tap_count, group_count = medium_taps.shape
    seq_rows = gate_ext.shape[0] - tap_count + 1
    chan_count = kv_pad.shape[1]
    group_width = chan_count // group_count
    span_len = row_block + tap_count - 1
    block_count = seq_rows // row_block
    toeplitz = band_matrix(medium_taps, row_block)
    kv_groups = kv_pad.reshape(-1, group_count, group_width)
    gate_groups = gate_ext.reshape(-1, group_count, group_width)
    starts = [b * row_block for b in range(block_count)]
    kv_win = jnp.concatenate([kv_groups[b : b + span_len] for b in starts], axis=2)
    gate_win = jnp.concatenate([gate_groups[b : b + span_len] for b in starts], axis=2)
    mixed_out = jnp.einsum("gts,sgn->tgn", toeplitz, kv_win, preferred_element_type=jnp.float32)
    back_out = jnp.flip(
        jnp.einsum(
            "gts,sgn->tgn", toeplitz, jnp.flip(gate_win, 0), preferred_element_type=jnp.float32
        ),
        0,
    )
    cross_terms = jnp.einsum(
        "tgn,sgn->gts", gate_win[:row_block], kv_win, preferred_element_type=jnp.float32
    )
    taps_grad = diagonal_sums(cross_terms, tap_count).T

    def unblock(values_in):
        split = values_in.reshape(row_block, group_count, block_count, group_width)
        return split.transpose(2, 0, 1, 3).reshape(seq_rows, chan_count)

    return unblock(mixed_out), unblock(back_out), taps_grad


def per_device(inputs, upstream, short_filter, medium_filter):
    signal = inputs[0]
    grad_out = upstream[0]
    seq_rows, chan_count = signal.shape
    tap_count = medium_filter.shape[1]
    group_count = medium_filter.shape[2]
    lag_count = short_filter.shape[1] // 3
    group_width = chan_count // group_count
    short_rim = lag_count - 1
    medium_rim = tap_count - 1
    chan_short = jnp.broadcast_to(
        short_filter[0].astype(jnp.float32).reshape(3, lag_count, group_count, 1),
        (3, lag_count, group_count, group_width),
    ).reshape(3, lag_count, chan_count)
    medium_taps = medium_filter[0]
    zero_rim = jnp.zeros((short_rim, chan_count), jnp.bfloat16)
    features_local = short_features(jnp.concatenate([zero_rim, signal], 0), chan_short, seq_rows)
    kv_local = (
        features_local[1].astype(jnp.float32) * features_local[2].astype(jnp.float32)
    ).astype(jnp.bfloat16)
    signal_rim, kv_rim = passed_along(
        (signal[seq_rows - short_rim :], kv_local[seq_rows - medium_rim :]), "ctx", 1
    )
    signal_pad = jnp.concatenate([signal_rim, signal], 0)
    head_features = short_features(signal_pad[: 2 * short_rim], chan_short, short_rim)
    features = jnp.concatenate([head_features, features_local[:, short_rim:]], 1)
    query_in = features[0]
    key_in = features[1]
    value_in = features[2]
    head_products = (
        key_in[:short_rim].astype(jnp.float32) * value_in[:short_rim].astype(jnp.float32)
    ).astype(jnp.bfloat16)
    products = jnp.concatenate([head_products, kv_local[short_rim:]], 0)
    kv_pad = jnp.concatenate([kv_rim, products], 0)
    gate_grad = (grad_out.astype(jnp.float32) * query_in.astype(jnp.float32)).astype(jnp.bfloat16)
    gate_rim = passed_along(gate_grad[:medium_rim], "ctx", -1)
    gate_ext = jnp.concatenate([gate_grad, gate_rim], 0)
    mixed_out, back_out, taps_grad = medium_terms(medium_taps, kv_pad, gate_ext, 128)
    query_grad = (grad_out.astype(jnp.float32) * mixed_out).astype(jnp.bfloat16)
    key_grad = (back_out * value_in.astype(jnp.float32)).astype(jnp.bfloat16)
    value_grad = (back_out * key_in.astype(jnp.float32)).astype(jnp.bfloat16)
    feature_grads = jnp.stack([query_grad, key_grad, value_grad])
    feature_rim = passed_along(feature_grads[:, :short_rim], "ctx", -1)
    grads_pad = jnp.concatenate([feature_grads, feature_rim], 1)
    running = jnp.zeros((seq_rows, chan_count), jnp.float32)
    short_rows = []
    for offset in range(lag_count):
        running = running + jnp.sum(
            chan_short[:, offset, None, :]
            * grads_pad[:, offset : offset + seq_rows].astype(jnp.float32),
            axis=0,
        )
        lag_start = short_rim - offset
        short_rows.append(
            jnp.sum(
                feature_grads.astype(jnp.float32)
                * signal_pad[None, lag_start : lag_start + seq_rows].astype(jnp.float32),
                axis=1,
            )
        )
    input_grad = running.astype(jnp.bfloat16)
    short_grad = jnp.stack(short_rows, 1).reshape(3 * lag_count, group_count, group_width).sum(-1)
    short_part = owned_sum(short_grad, "ctx")[None]
    medium_part = owned_sum(taps_grad, "ctx")[None]
    incoming = passed_along(input_grad[None], "section", -1)
    return (incoming, short_part, medium_part)


def solution(mesh):
    in_specs = (
        P("section", "ctx", "dp"),
        P("section", "ctx", "dp"),
        P("section", None, "dp"),
        P("section", None, "dp"),
    )
    out_specs = (
        P("section", "ctx", "dp"),
        P("section", None, ("dp", "ctx")),
        P("section", None, ("dp", "ctx")),
    )
    return jax.shard_map(
        per_device, mesh=mesh, in_specs=in_specs, out_specs=out_specs, check_vma=False
    )
```

```python
import jax
import jax.numpy as jnp
from jax import lax
from jax.sharding import PartitionSpec as P


def passed_along(block, axis, distance):
    devices = range(lax.axis_size(axis))
    route = [(i - distance, i) for i in devices if i - distance in devices]
    return lax.ppermute(block, axis, route)


def owned_sum(partial_terms, axis):
    axis_len = lax.axis_size(axis)
    row_count, col_count = partial_terms.shape
    width = col_count // axis_len
    chunks = partial_terms.reshape(row_count, axis_len, width).transpose(1, 0, 2)
    return jnp.sum(lax.all_to_all(chunks, axis, 0, 0, tiled=False), axis=0)


def band_matrix(filter_taps, out_rows):
    tap_count, group_count = filter_taps.shape
    leading = jnp.flip(filter_taps, 0).T
    padded = jnp.concatenate([leading, jnp.zeros((group_count, out_rows), filter_taps.dtype)], 1)
    span_len = out_rows + tap_count - 1
    tiled_rows = jnp.tile(padded, (1, out_rows))[:, : out_rows * span_len]
    return tiled_rows.reshape(group_count, out_rows, span_len)


def diagonal_sums(cross_terms, tap_count):
    group_count, out_rows, span_len = cross_terms.shape
    flat_view = jnp.pad(
        cross_terms.reshape(group_count, out_rows * span_len), ((0, 0), (0, out_rows))
    )
    skewed = flat_view.reshape(group_count, out_rows, span_len + 1)
    return jnp.flip(jnp.sum(skewed[:, :, :tap_count], axis=1), 1)


def short_features(padded, chan_short, out_rows):
    lag_count = chan_short.shape[1]
    running = jnp.zeros((3, out_rows, padded.shape[1]), jnp.float32)
    for offset in range(lag_count):
        first_row = lag_count - 1 - offset
        running = running + chan_short[:, offset, None, :] * padded[
            None, first_row : first_row + out_rows
        ].astype(jnp.float32)
    return running.astype(jnp.bfloat16)


def medium_terms(medium_taps, kv_pad, gate_ext, row_block):
    tap_count, group_count = medium_taps.shape
    seq_rows = gate_ext.shape[0] - tap_count + 1
    chan_count = kv_pad.shape[1]
    group_width = chan_count // group_count
    span_len = row_block + tap_count - 1
    block_count = seq_rows // row_block
    toeplitz = band_matrix(medium_taps, row_block)
    kv_groups = kv_pad.reshape(-1, group_count, group_width)
    gate_groups = gate_ext.reshape(-1, group_count, group_width)
    starts = [b * row_block for b in range(block_count)]
    kv_win = jnp.concatenate([kv_groups[b : b + span_len] for b in starts], axis=2)
    gate_win = jnp.concatenate([gate_groups[b : b + span_len] for b in starts], axis=2)
    mixed_out = jnp.einsum("gts,sgn->tgn", toeplitz, kv_win, preferred_element_type=jnp.float32)
    back_out = jnp.flip(
        jnp.einsum(
            "gts,sgn->tgn", toeplitz, jnp.flip(gate_win, 0), preferred_element_type=jnp.float32
        ),
        0,
    )
    cross_terms = jnp.einsum(
        "tgn,sgn->gts", gate_win[:row_block], kv_win, preferred_element_type=jnp.float32
    )
    taps_grad = diagonal_sums(cross_terms, tap_count).T

    def unblock(values_in):
        split = values_in.reshape(row_block, group_count, block_count, group_width)
        return split.transpose(2, 0, 1, 3).reshape(seq_rows, chan_count)

    return unblock(mixed_out), unblock(back_out), taps_grad


def per_device(inputs, upstream, short_filter, medium_filter):
    signal = inputs[0]
    grad_out = upstream[0]
    seq_rows, chan_count = signal.shape
    tap_count = medium_filter.shape[1]
    group_count = medium_filter.shape[2]
    lag_count = short_filter.shape[1] // 3
    group_width = chan_count // group_count
    short_rim = lag_count - 1
    medium_rim = tap_count - 1
    chan_short = jnp.broadcast_to(
        short_filter[0].astype(jnp.float32).reshape(3, lag_count, group_count, 1),
        (3, lag_count, group_count, group_width),
    ).reshape(3, lag_count, chan_count)
    medium_taps = medium_filter[0]
    zero_rim = jnp.zeros((short_rim, chan_count), jnp.bfloat16)
    features_local = short_features(jnp.concatenate([zero_rim, signal], 0), chan_short, seq_rows)
    kv_local = (
        features_local[1].astype(jnp.float32) * features_local[2].astype(jnp.float32)
    ).astype(jnp.bfloat16)
    signal_rim, kv_rim = passed_along(
        (signal[seq_rows - short_rim :], kv_local[seq_rows - medium_rim :]), "ctx", 1
    )
    signal_pad = jnp.concatenate([signal_rim, signal], 0)
    head_features = short_features(signal_pad[: 2 * short_rim], chan_short, short_rim)
    features = jnp.concatenate([head_features, features_local[:, short_rim:]], 1)
    query_in = features[0]
    key_in = features[1]
    value_in = features[2]
    head_products = (
        key_in[:short_rim].astype(jnp.float32) * value_in[:short_rim].astype(jnp.float32)
    ).astype(jnp.bfloat16)
    products = jnp.concatenate([head_products, kv_local[short_rim:]], 0)
    kv_pad = jnp.concatenate([kv_rim, products], 0)
    gate_grad = (grad_out.astype(jnp.float32) * query_in.astype(jnp.float32)).astype(jnp.bfloat16)
    gate_rim = passed_along(gate_grad[:medium_rim], "ctx", -1)
    gate_ext = jnp.concatenate([gate_grad, gate_rim], 0)
    mixed_out, back_out, taps_grad = medium_terms(medium_taps, kv_pad, gate_ext, 128)
    query_grad = (grad_out.astype(jnp.float32) * mixed_out).astype(jnp.bfloat16)
    key_grad = (back_out * value_in.astype(jnp.float32)).astype(jnp.bfloat16)
    value_grad = (back_out * key_in.astype(jnp.float32)).astype(jnp.bfloat16)
    feature_grads = jnp.stack([query_grad, key_grad, value_grad])
    feature_rim = passed_along(feature_grads[:, :short_rim], "ctx", -1)
    grads_pad = jnp.concatenate([feature_grads, feature_rim], 1)
    running = jnp.zeros((seq_rows, chan_count), jnp.float32)
    short_rows = []
    for offset in range(lag_count):
        running = running + jnp.sum(
            chan_short[:, offset, None, :]
            * grads_pad[:, offset : offset + seq_rows].astype(jnp.float32),
            axis=0,
        )
        lag_start = short_rim - offset
        short_rows.append(
            jnp.sum(
                feature_grads.astype(jnp.float32)
                * signal_pad[None, lag_start : lag_start + seq_rows].astype(jnp.float32),
                axis=1,
            )
        )
    input_grad = running.astype(jnp.bfloat16)
    short_grad = jnp.stack(short_rows, 1).reshape(3 * lag_count, group_count, group_width).sum(-1)
    short_count = short_grad.shape[0]
    both_part = owned_sum(jnp.concatenate([short_grad, taps_grad], 0), "ctx")
    short_part = both_part[None, :short_count]
    medium_part = both_part[None, short_count:]
    incoming = passed_along(input_grad[None], "section", -1)
    return (incoming, short_part, medium_part)


def solution(mesh):
    in_specs = (
        P("section", "ctx", "dp"),
        P("section", "ctx", "dp"),
        P("section", None, "dp"),
        P("section", None, "dp"),
    )
    out_specs = (
        P("section", "ctx", "dp"),
        P("section", None, ("dp", "ctx")),
        P("section", None, ("dp", "ctx")),
    )
    return jax.shard_map(
        per_device, mesh=mesh, in_specs=in_specs, out_specs=out_specs, check_vma=False
    )
```

```python
import jax
import jax.numpy as jnp
from jax import lax
from jax.sharding import PartitionSpec as P


def passed_along(block, axis, distance):
    devices = range(lax.axis_size(axis))
    route = [(i - distance, i) for i in devices if i - distance in devices]
    return lax.ppermute(block, axis, route)


def owned_sum(partial_terms, axis):
    axis_len = lax.axis_size(axis)
    row_count, col_count = partial_terms.shape
    width = col_count // axis_len
    chunks = partial_terms.reshape(row_count, axis_len, width).transpose(1, 0, 2)
    return jnp.sum(lax.all_to_all(chunks, axis, 0, 0, tiled=False), axis=0)


def band_matrix(filter_taps, out_rows):
    tap_count, group_count = filter_taps.shape
    leading = jnp.flip(filter_taps, 0).T
    padded = jnp.concatenate([leading, jnp.zeros((group_count, out_rows), filter_taps.dtype)], 1)
    span_len = out_rows + tap_count - 1
    tiled_rows = jnp.tile(padded, (1, out_rows))[:, : out_rows * span_len]
    return tiled_rows.reshape(group_count, out_rows, span_len)


def diagonal_sums(cross_terms, tap_count):
    group_count, out_rows, span_len = cross_terms.shape
    flat_view = jnp.pad(
        cross_terms.reshape(group_count, out_rows * span_len), ((0, 0), (0, out_rows))
    )
    skewed = flat_view.reshape(group_count, out_rows, span_len + 1)
    return jnp.flip(jnp.sum(skewed[:, :, :tap_count], axis=1), 1)


def short_features(padded, chan_short, out_rows):
    lag_count = chan_short.shape[1]
    running = jnp.zeros((3, out_rows, padded.shape[1]), jnp.float32)
    for offset in range(lag_count):
        first_row = lag_count - 1 - offset
        running = running + chan_short[:, offset, None, :] * padded[
            None, first_row : first_row + out_rows
        ].astype(jnp.float32)
    return running.astype(jnp.bfloat16)


def medium_terms(medium_taps, kv_pad, gate_ext, row_block):
    tap_count, group_count = medium_taps.shape
    seq_rows = gate_ext.shape[0] - tap_count + 1
    chan_count = kv_pad.shape[1]
    group_width = chan_count // group_count
    span_len = row_block + tap_count - 1
    block_count = seq_rows // row_block
    toeplitz = band_matrix(medium_taps, row_block)
    kv_groups = kv_pad.reshape(-1, group_count, group_width)
    gate_groups = gate_ext.reshape(-1, group_count, group_width)
    starts = [b * row_block for b in range(block_count)]
    kv_win = jnp.concatenate([kv_groups[b : b + span_len] for b in starts], axis=2)
    gate_win = jnp.concatenate([gate_groups[b : b + span_len] for b in starts], axis=2)
    mixed_out = jnp.einsum("gts,sgn->tgn", toeplitz, kv_win, preferred_element_type=jnp.float32)
    back_out = jnp.flip(
        jnp.einsum(
            "gts,sgn->tgn", toeplitz, jnp.flip(gate_win, 0), preferred_element_type=jnp.float32
        ),
        0,
    )
    cross_terms = jnp.einsum(
        "tgn,sgn->gts", gate_win[:row_block], kv_win, preferred_element_type=jnp.float32
    )
    taps_grad = diagonal_sums(cross_terms, tap_count).T

    def unblock(values_in):
        split = values_in.reshape(row_block, group_count, block_count, group_width)
        return split.transpose(2, 0, 1, 3).reshape(seq_rows, chan_count)

    return unblock(mixed_out), unblock(back_out), taps_grad


def per_device(inputs, upstream, short_filter, medium_filter):
    signal = inputs[0]
    grad_out = upstream[0]
    seq_rows, chan_count = signal.shape
    tap_count = medium_filter.shape[1]
    group_count = medium_filter.shape[2]
    lag_count = short_filter.shape[1] // 3
    group_width = chan_count // group_count
    short_rim = lag_count - 1
    medium_rim = tap_count - 1
    chan_short = jnp.broadcast_to(
        short_filter[0].astype(jnp.float32).reshape(3, lag_count, group_count, 1),
        (3, lag_count, group_count, group_width),
    ).reshape(3, lag_count, chan_count)
    medium_taps = medium_filter[0]
    zero_rim = jnp.zeros((short_rim, chan_count), jnp.bfloat16)
    features_local = short_features(jnp.concatenate([zero_rim, signal], 0), chan_short, seq_rows)
    kv_local = (
        features_local[1].astype(jnp.float32) * features_local[2].astype(jnp.float32)
    ).astype(jnp.bfloat16)
    signal_rim, kv_rim = passed_along(
        (signal[seq_rows - short_rim :], kv_local[seq_rows - medium_rim :]), "ctx", 1
    )
    signal_pad = jnp.concatenate([signal_rim, signal], 0)
    head_features = short_features(signal_pad[: 2 * short_rim], chan_short, short_rim)
    features = jnp.concatenate([head_features, features_local[:, short_rim:]], 1)
    query_in = features[0]
    key_in = features[1]
    value_in = features[2]
    head_products = (
        key_in[:short_rim].astype(jnp.float32) * value_in[:short_rim].astype(jnp.float32)
    ).astype(jnp.bfloat16)
    products = jnp.concatenate([head_products, kv_local[short_rim:]], 0)
    kv_pad = jnp.concatenate([kv_rim, products], 0)
    gate_grad = (grad_out.astype(jnp.float32) * query_in.astype(jnp.float32)).astype(jnp.bfloat16)
    gate_rim = passed_along(gate_grad[:medium_rim], "ctx", -1)
    gate_ext = jnp.concatenate([gate_grad, gate_rim], 0)
    mixed_out, back_out, taps_grad = medium_terms(medium_taps, kv_pad, gate_ext, 128)
    query_grad = (grad_out.astype(jnp.float32) * mixed_out).astype(jnp.bfloat16)
    key_grad = (back_out * value_in.astype(jnp.float32)).astype(jnp.bfloat16)
    value_grad = (back_out * key_in.astype(jnp.float32)).astype(jnp.bfloat16)
    feature_grads = jnp.stack([query_grad, key_grad, value_grad])
    feature_rim = passed_along(feature_grads[:, :short_rim], "ctx", -1)
    grads_pad = jnp.concatenate([feature_grads, feature_rim], 1)
    running = jnp.zeros((seq_rows, chan_count), jnp.float32)
    for offset in range(lag_count):
        running = running + jnp.sum(
            chan_short[:, offset, None, :]
            * grads_pad[:, offset : offset + seq_rows].astype(jnp.float32),
            axis=0,
        )
    input_grad = running.astype(jnp.bfloat16)
    lag_windows = jnp.stack(
        [signal_pad[short_rim - offset : short_rim - offset + seq_rows] for offset in range(lag_count)],
        1,
    ).reshape(seq_rows, lag_count, group_count, group_width)
    grad_groups = feature_grads.reshape(3, seq_rows, group_count, group_width)
    cross_short = jnp.einsum(
        "ftgc,tigd->gficd", grad_groups, lag_windows, preferred_element_type=jnp.float32
    )
    same_chan = jnp.eye(group_width, dtype=jnp.float32)
    short_grad = jnp.sum(cross_short * same_chan, axis=(3, 4)).transpose(1, 2, 0)
    short_grad = short_grad.reshape(3 * lag_count, group_count)
    short_count = short_grad.shape[0]
    both_part = owned_sum(jnp.concatenate([short_grad, taps_grad], 0), "ctx")
    short_part = both_part[None, :short_count]
    medium_part = both_part[None, short_count:]
    incoming = passed_along(input_grad[None], "section", -1)
    return (incoming, short_part, medium_part)


def solution(mesh):
    in_specs = (
        P("section", "ctx", "dp"),
        P("section", "ctx", "dp"),
        P("section", None, "dp"),
        P("section", None, "dp"),
    )
    out_specs = (
        P("section", "ctx", "dp"),
        P("section", None, ("dp", "ctx")),
        P("section", None, ("dp", "ctx")),
    )
    return jax.shard_map(
        per_device, mesh=mesh, in_specs=in_specs, out_specs=out_specs, check_vma=False
    )
```

```python
import jax
import jax.numpy as jnp
from jax import lax
from jax.experimental import pallas as pl
from jax.experimental.pallas import tpu as pltpu
from jax.sharding import PartitionSpec as P

LANE_BLOCK = 128


def passed_along(block, axis, distance):
    devices = range(lax.axis_size(axis))
    route = [(i - distance, i) for i in devices if i - distance in devices]
    return lax.ppermute(block, axis, route)


def owned_sum(partial_terms, axis):
    axis_len = lax.axis_size(axis)
    row_count, col_count = partial_terms.shape
    width = col_count // axis_len
    chunks = partial_terms.reshape(row_count, axis_len, width).transpose(1, 0, 2)
    return jnp.sum(lax.all_to_all(chunks, axis, 0, 0, tiled=False), axis=0)


def front_kernel(taps_ref, sig_ref, gy_ref, q_ref, k_ref, v_ref, kv_ref, gate_ref, xs_ref):
    rows = q_ref.shape[0]
    rim = sig_ref.shape[0] - rows
    lags = rim + 1
    xs_ref[pl.ds(0, rows + rim), :] = sig_ref[...].astype(jnp.float32)
    for branch, out_ref in enumerate((q_ref, k_ref, v_ref)):
        acc = None
        for offset in range(lags):
            term = taps_ref[pl.ds(branch * lags + offset, 1), :] * xs_ref[pl.ds(rim - offset, rows), :]
            acc = term if acc is None else acc + term
        out_ref[...] = acc.astype(jnp.bfloat16)
    kv_ref[...] = (k_ref[...].astype(jnp.float32) * v_ref[...].astype(jnp.float32)).astype(
        jnp.bfloat16
    )
    gate_ref[...] = (gy_ref[...].astype(jnp.float32) * q_ref[...].astype(jnp.float32)).astype(
        jnp.bfloat16
    )


def short_front(taps, signal_pad, grad_out):
    padded_rows, chan_count = signal_pad.shape
    rows = grad_out.shape[0]
    tap_rows = taps.shape[0]
    row_spec = pl.BlockSpec((rows, LANE_BLOCK), lambda j: (0, j))
    shape = jax.ShapeDtypeStruct((rows, chan_count), jnp.bfloat16)
    return pl.pallas_call(
        front_kernel,
        grid=(chan_count // LANE_BLOCK,),
        in_specs=[
            pl.BlockSpec((tap_rows, LANE_BLOCK), lambda j: (0, j)),
            pl.BlockSpec((padded_rows, LANE_BLOCK), lambda j: (0, j)),
            row_spec,
        ],
        out_specs=[row_spec] * 5,
        out_shape=[shape] * 5,
        scratch_shapes=[pltpu.VMEM((padded_rows + 8, LANE_BLOCK), jnp.float32)],
    )(taps, signal_pad, grad_out)


def back_kernel(taps_ref, sig_ref, grads_ref, ig_ref, sp_ref, xs_ref, gs_ref):
    rows = ig_ref.shape[0]
    rim = sig_ref.shape[0] - rows
    lags = rim + 1
    branches = grads_ref.shape[0]
    xs_ref[pl.ds(0, rows + rim), :] = sig_ref[...].astype(jnp.float32)
    for branch in range(branches):
        gs_ref[branch, pl.ds(0, rows + rim), :] = grads_ref[branch].astype(jnp.float32)
    acc = None
    for branch in range(branches):
        for offset in range(lags):
            term = taps_ref[pl.ds(branch * lags + offset, 1), :] * gs_ref[branch, pl.ds(offset, rows), :]
            acc = term if acc is None else acc + term
    ig_ref[...] = acc.astype(jnp.bfloat16)
    for branch in range(branches):
        grads_f = gs_ref[branch, pl.ds(0, rows), :]
        for offset in range(lags):
            prod = grads_f * xs_ref[pl.ds(rim - offset, rows), :]
            sp_ref[pl.ds(branch * lags + offset, 1), :] = jnp.sum(prod, axis=0, keepdims=True)


def short_back(taps, signal_pad, grads_pad):
    padded_rows, chan_count = signal_pad.shape
    branches = grads_pad.shape[0]
    tap_rows = taps.shape[0]
    rows = padded_rows - (tap_rows // branches - 1)
    return pl.pallas_call(
        back_kernel,
        grid=(chan_count // LANE_BLOCK,),
        in_specs=[
            pl.BlockSpec((tap_rows, LANE_BLOCK), lambda j: (0, j)),
            pl.BlockSpec((padded_rows, LANE_BLOCK), lambda j: (0, j)),
            pl.BlockSpec((branches, padded_rows, LANE_BLOCK), lambda j: (0, 0, j)),
        ],
        out_specs=[
            pl.BlockSpec((rows, LANE_BLOCK), lambda j: (0, j)),
            pl.BlockSpec((tap_rows, LANE_BLOCK), lambda j: (0, j)),
        ],
        out_shape=[
            jax.ShapeDtypeStruct((rows, chan_count), jnp.bfloat16),
            jax.ShapeDtypeStruct((tap_rows, chan_count), jnp.float32),
        ],
        scratch_shapes=[
            pltpu.VMEM((padded_rows + 8, LANE_BLOCK), jnp.float32),
            pltpu.VMEM((branches, padded_rows + 8, LANE_BLOCK), jnp.float32),
        ],
    )(taps, signal_pad, grads_pad)


def band_matrix(filter_taps, out_rows):
    tap_count, group_count = filter_taps.shape
    leading = jnp.flip(filter_taps, 0).T
    padded = jnp.concatenate([leading, jnp.zeros((group_count, out_rows), filter_taps.dtype)], 1)
    span_len = out_rows + tap_count - 1
    tiled_rows = jnp.tile(padded, (1, out_rows))[:, : out_rows * span_len]
    return tiled_rows.reshape(group_count, out_rows, span_len)


def diagonal_sums(cross_terms, tap_count):
    group_count, out_rows, span_len = cross_terms.shape
    flat_view = jnp.pad(
        cross_terms.reshape(group_count, out_rows * span_len), ((0, 0), (0, out_rows))
    )
    skewed = flat_view.reshape(group_count, out_rows, span_len + 1)
    return jnp.flip(jnp.sum(skewed[:, :, :tap_count], axis=1), 1)


def short_features(padded, chan_short, out_rows):
    lag_count = chan_short.shape[1]
    running = jnp.zeros((3, out_rows, padded.shape[1]), jnp.float32)
    for offset in range(lag_count):
        first_row = lag_count - 1 - offset
        running = running + chan_short[:, offset, None, :] * padded[
            None, first_row : first_row + out_rows
        ].astype(jnp.float32)
    return running.astype(jnp.bfloat16)


def medium_terms(medium_taps, kv_pad, gate_ext, row_block):
    tap_count, group_count = medium_taps.shape
    seq_rows = gate_ext.shape[0] - tap_count + 1
    chan_count = kv_pad.shape[1]
    group_width = chan_count // group_count
    span_len = row_block + tap_count - 1
    block_count = seq_rows // row_block
    toeplitz = band_matrix(medium_taps, row_block)
    kv_groups = kv_pad.reshape(-1, group_count, group_width)
    gate_groups = gate_ext.reshape(-1, group_count, group_width)
    starts = [b * row_block for b in range(block_count)]
    kv_win = jnp.concatenate([kv_groups[b : b + span_len] for b in starts], axis=2)
    gate_win = jnp.concatenate([gate_groups[b : b + span_len] for b in starts], axis=2)
    mixed_out = jnp.einsum("gts,sgn->tgn", toeplitz, kv_win, preferred_element_type=jnp.float32)
    back_out = jnp.flip(
        jnp.einsum(
            "gts,sgn->tgn", toeplitz, jnp.flip(gate_win, 0), preferred_element_type=jnp.float32
        ),
        0,
    )
    cross_terms = jnp.einsum(
        "tgn,sgn->gts", gate_win[:row_block], kv_win, preferred_element_type=jnp.float32
    )
    taps_grad = diagonal_sums(cross_terms, tap_count).T

    def unblock(values_in):
        split = values_in.reshape(row_block, group_count, block_count, group_width)
        return split.transpose(2, 0, 1, 3).reshape(seq_rows, chan_count)

    return unblock(mixed_out), unblock(back_out), taps_grad


def per_device(inputs, upstream, short_filter, medium_filter):
    signal = inputs[0]
    grad_out = upstream[0]
    seq_rows, chan_count = signal.shape
    tap_count = medium_filter.shape[1]
    group_count = medium_filter.shape[2]
    lag_count = short_filter.shape[1] // 3
    group_width = chan_count // group_count
    short_rim = lag_count - 1
    medium_rim = tap_count - 1
    chan_short = jnp.broadcast_to(
        short_filter[0].astype(jnp.float32).reshape(3, lag_count, group_count, 1),
        (3, lag_count, group_count, group_width),
    ).reshape(3, lag_count, chan_count)
    medium_taps = medium_filter[0]
    tap_table = chan_short.reshape(3 * lag_count, chan_count)
    signal_rim = passed_along(signal[seq_rows - short_rim :], "ctx", 1)
    signal_pad = jnp.concatenate([signal_rim, signal], 0)
    query_in, key_in, value_in, products, gate_grad = short_front(tap_table, signal_pad, grad_out)
    kv_rim, gate_rim = passed_along(products[seq_rows - medium_rim :], "ctx", 1), passed_along(
        gate_grad[:medium_rim], "ctx", -1
    )
    kv_pad = jnp.concatenate([kv_rim, products], 0)
    gate_ext = jnp.concatenate([gate_grad, gate_rim], 0)
    mixed_out, back_out, taps_grad = medium_terms(medium_taps, kv_pad, gate_ext, 128)
    query_grad = (grad_out.astype(jnp.float32) * mixed_out).astype(jnp.bfloat16)
    key_grad = (back_out * value_in.astype(jnp.float32)).astype(jnp.bfloat16)
    value_grad = (back_out * key_in.astype(jnp.float32)).astype(jnp.bfloat16)
    feature_grads = jnp.stack([query_grad, key_grad, value_grad])
    feature_rim = passed_along(feature_grads[:, :short_rim], "ctx", -1)
    grads_pad = jnp.concatenate([feature_grads, feature_rim], 1)
    input_grad, short_terms = short_back(tap_table, signal_pad, grads_pad)
    short_grad = short_terms.reshape(3 * lag_count, group_count, group_width).sum(-1)
    short_count = short_grad.shape[0]
    both_part = owned_sum(jnp.concatenate([short_grad, taps_grad], 0), "ctx")
    short_part = both_part[None, :short_count]
    medium_part = both_part[None, short_count:]
    incoming = passed_along(input_grad[None], "section", -1)
    return (incoming, short_part, medium_part)


def solution(mesh):
    in_specs = (
        P("section", "ctx", "dp"),
        P("section", "ctx", "dp"),
        P("section", None, "dp"),
        P("section", None, "dp"),
    )
    out_specs = (
        P("section", "ctx", "dp"),
        P("section", None, ("dp", "ctx")),
        P("section", None, ("dp", "ctx")),
    )
    return jax.shard_map(
        per_device, mesh=mesh, in_specs=in_specs, out_specs=out_specs, check_vma=False
    )
```

```python
import jax
import jax.numpy as jnp
from jax import lax
from jax.experimental import pallas as pl
from jax.experimental.pallas import tpu as pltpu
from jax.sharding import PartitionSpec as P

LANE_BLOCK = 128


def passed_along(block, axis, distance):
    devices = range(lax.axis_size(axis))
    route = [(i - distance, i) for i in devices if i - distance in devices]
    return lax.ppermute(block, axis, route)


def owned_sum(partial_terms, axis):
    axis_len = lax.axis_size(axis)
    row_count, col_count = partial_terms.shape
    width = col_count // axis_len
    chunks = partial_terms.reshape(row_count, axis_len, width).transpose(1, 0, 2)
    return jnp.sum(lax.all_to_all(chunks, axis, 0, 0, tiled=False), axis=0)


def front_kernel(taps_ref, sig_ref, gy_ref, q_ref, k_ref, v_ref, kv_ref, gate_ref, xs_ref):
    rows = q_ref.shape[0]
    rim = sig_ref.shape[0] - rows
    lags = rim + 1
    xs_ref[pl.ds(0, rows + rim), :] = sig_ref[...].astype(jnp.float32)
    for branch, out_ref in enumerate((q_ref, k_ref, v_ref)):
        acc = None
        for offset in range(lags):
            term = taps_ref[pl.ds(branch * lags + offset, 1), :] * xs_ref[pl.ds(rim - offset, rows), :]
            acc = term if acc is None else acc + term
        out_ref[...] = acc.astype(jnp.bfloat16)
    kv_ref[...] = (k_ref[...].astype(jnp.float32) * v_ref[...].astype(jnp.float32)).astype(
        jnp.bfloat16
    )
    gate_ref[...] = (gy_ref[...].astype(jnp.float32) * q_ref[...].astype(jnp.float32)).astype(
        jnp.bfloat16
    )


def short_front(taps, signal_pad, grad_out):
    padded_rows, chan_count = signal_pad.shape
    rows = grad_out.shape[0]
    tap_rows = taps.shape[0]
    row_spec = pl.BlockSpec((rows, LANE_BLOCK), lambda j: (0, j))
    shape = jax.ShapeDtypeStruct((rows, chan_count), jnp.bfloat16)
    return pl.pallas_call(
        front_kernel,
        grid=(chan_count // LANE_BLOCK,),
        in_specs=[
            pl.BlockSpec((tap_rows, LANE_BLOCK), lambda j: (0, j)),
            pl.BlockSpec((padded_rows, LANE_BLOCK), lambda j: (0, j)),
            row_spec,
        ],
        out_specs=[row_spec] * 5,
        out_shape=[shape] * 5,
        scratch_shapes=[pltpu.VMEM((padded_rows + 8, LANE_BLOCK), jnp.float32)],
    )(taps, signal_pad, grad_out)


def back_kernel(taps_ref, sig_ref, grads_ref, ig_ref, sp_ref, xs_ref, gs_ref):
    rows = ig_ref.shape[0]
    rim = sig_ref.shape[0] - rows
    lags = rim + 1
    branches = grads_ref.shape[0]
    xs_ref[pl.ds(0, rows + rim), :] = sig_ref[...].astype(jnp.float32)
    for branch in range(branches):
        gs_ref[branch, pl.ds(0, rows + rim), :] = grads_ref[branch].astype(jnp.float32)
    acc = None
    for branch in range(branches):
        for offset in range(lags):
            term = taps_ref[pl.ds(branch * lags + offset, 1), :] * gs_ref[branch, pl.ds(offset, rows), :]
            acc = term if acc is None else acc + term
    ig_ref[...] = acc.astype(jnp.bfloat16)
    for branch in range(branches):
        grads_f = gs_ref[branch, pl.ds(0, rows), :]
        for offset in range(lags):
            prod = grads_f * xs_ref[pl.ds(rim - offset, rows), :]
            sp_ref[pl.ds(branch * lags + offset, 1), :] = jnp.sum(prod, axis=0, keepdims=True)


def short_back(taps, signal_pad, grads_pad):
    padded_rows, chan_count = signal_pad.shape
    branches = grads_pad.shape[0]
    tap_rows = taps.shape[0]
    rows = padded_rows - (tap_rows // branches - 1)
    return pl.pallas_call(
        back_kernel,
        grid=(chan_count // LANE_BLOCK,),
        in_specs=[
            pl.BlockSpec((tap_rows, LANE_BLOCK), lambda j: (0, j)),
            pl.BlockSpec((padded_rows, LANE_BLOCK), lambda j: (0, j)),
            pl.BlockSpec((branches, padded_rows, LANE_BLOCK), lambda j: (0, 0, j)),
        ],
        out_specs=[
            pl.BlockSpec((rows, LANE_BLOCK), lambda j: (0, j)),
            pl.BlockSpec((tap_rows, LANE_BLOCK), lambda j: (0, j)),
        ],
        out_shape=[
            jax.ShapeDtypeStruct((rows, chan_count), jnp.bfloat16),
            jax.ShapeDtypeStruct((tap_rows, chan_count), jnp.float32),
        ],
        scratch_shapes=[
            pltpu.VMEM((padded_rows + 8, LANE_BLOCK), jnp.float32),
            pltpu.VMEM((branches, padded_rows + 8, LANE_BLOCK), jnp.float32),
        ],
    )(taps, signal_pad, grads_pad)


def band_kernel(taps_ref, out_ref):
    group_block, rows, span = out_ref.shape
    for group in range(group_block):
        row = jnp.broadcast_to(taps_ref[pl.ds(group, 1), :], (rows, span))
        out_ref[group] = pltpu.roll(row, 0, 1, stride=1, stride_axis=0).astype(out_ref.dtype)


def band_matrix(filter_taps, out_rows):
    tap_count, group_count = filter_taps.shape
    span = out_rows + tap_count
    leading = jnp.flip(filter_taps, 0).T.astype(jnp.float32)
    padded = jnp.concatenate([leading, jnp.zeros((group_count, out_rows), jnp.float32)], 1)
    group_block = 8
    return pl.pallas_call(
        band_kernel,
        grid=(group_count // group_block,),
        in_specs=[pl.BlockSpec((group_block, span), lambda j: (j, 0))],
        out_specs=pl.BlockSpec((group_block, out_rows, span), lambda j: (j, 0, 0)),
        out_shape=jax.ShapeDtypeStruct((group_count, out_rows, span), filter_taps.dtype),
    )(padded)


def diagonal_kernel(cross_ref, out_ref):
    group_block, rows, span = cross_ref.shape
    for group in range(group_block):
        rolled = pltpu.roll(cross_ref[group], 0, 1, stride=1, stride_axis=0)
        out_ref[pl.ds(group, 1), :] = jnp.sum(rolled[:, span - rows :], axis=0, keepdims=True)


def diagonal_sums(cross_flipped):
    group_count, rows, span = cross_flipped.shape
    group_block = 8
    return pl.pallas_call(
        diagonal_kernel,
        grid=(group_count // group_block,),
        in_specs=[pl.BlockSpec((group_block, rows, span), lambda j: (j, 0, 0))],
        out_specs=pl.BlockSpec((group_block, rows), lambda j: (j, 0)),
        out_shape=jax.ShapeDtypeStruct((group_count, rows), jnp.float32),
    )(cross_flipped)


def medium_terms(medium_taps, kv_pad, gate_ext, row_block):
    tap_count, group_count = medium_taps.shape
    seq_rows = gate_ext.shape[0] - tap_count + 1
    chan_count = kv_pad.shape[1]
    group_width = chan_count // group_count
    span_len = row_block + tap_count
    block_count = seq_rows // row_block
    toeplitz = band_matrix(medium_taps, row_block)
    zero_row = jnp.zeros((1, chan_count), kv_pad.dtype)
    kv_groups = jnp.concatenate([kv_pad, zero_row], 0).reshape(-1, group_count, group_width)
    gate_groups = jnp.concatenate([zero_row, gate_ext], 0).reshape(-1, group_count, group_width)
    row_groups = gate_ext.reshape(-1, group_count, group_width)
    starts = [b * row_block for b in range(block_count)]
    kv_win = jnp.concatenate([kv_groups[b : b + span_len] for b in starts], axis=2)
    gate_win = jnp.concatenate([gate_groups[b : b + span_len] for b in starts], axis=2)
    gate_rows = jnp.concatenate([row_groups[b : b + row_block] for b in starts], axis=2)
    mixed_out = jnp.einsum("gts,sgn->tgn", toeplitz, kv_win, preferred_element_type=jnp.float32)
    back_out = jnp.flip(
        jnp.einsum(
            "gts,sgn->tgn", toeplitz, jnp.flip(gate_win, 0), preferred_element_type=jnp.float32
        ),
        0,
    )
    cross_flipped = jnp.einsum(
        "tgn,sgn->gts", gate_rows, jnp.flip(kv_win, 0), preferred_element_type=jnp.float32
    )
    taps_grad = diagonal_sums(cross_flipped).T

    def unblock(values_in):
        split = values_in.reshape(row_block, group_count, block_count, group_width)
        return split.transpose(2, 0, 1, 3).reshape(seq_rows, chan_count)

    return unblock(mixed_out), unblock(back_out), taps_grad


def per_device(inputs, upstream, short_filter, medium_filter):
    signal = inputs[0]
    grad_out = upstream[0]
    seq_rows, chan_count = signal.shape
    tap_count = medium_filter.shape[1]
    group_count = medium_filter.shape[2]
    lag_count = short_filter.shape[1] // 3
    group_width = chan_count // group_count
    short_rim = lag_count - 1
    medium_rim = tap_count - 1
    chan_short = jnp.broadcast_to(
        short_filter[0].astype(jnp.float32).reshape(3, lag_count, group_count, 1),
        (3, lag_count, group_count, group_width),
    ).reshape(3, lag_count, chan_count)
    medium_taps = medium_filter[0]
    tap_table = chan_short.reshape(3 * lag_count, chan_count)
    signal_rim = passed_along(signal[seq_rows - short_rim :], "ctx", 1)
    signal_pad = jnp.concatenate([signal_rim, signal], 0)
    query_in, key_in, value_in, products, gate_grad = short_front(tap_table, signal_pad, grad_out)
    kv_rim, gate_rim = passed_along(products[seq_rows - medium_rim :], "ctx", 1), passed_along(
        gate_grad[:medium_rim], "ctx", -1
    )
    kv_pad = jnp.concatenate([kv_rim, products], 0)
    gate_ext = jnp.concatenate([gate_grad, gate_rim], 0)
    mixed_out, back_out, taps_grad = medium_terms(medium_taps, kv_pad, gate_ext, 128)
    query_grad = (grad_out.astype(jnp.float32) * mixed_out).astype(jnp.bfloat16)
    key_grad = (back_out * value_in.astype(jnp.float32)).astype(jnp.bfloat16)
    value_grad = (back_out * key_in.astype(jnp.float32)).astype(jnp.bfloat16)
    feature_grads = jnp.stack([query_grad, key_grad, value_grad])
    feature_rim = passed_along(feature_grads[:, :short_rim], "ctx", -1)
    grads_pad = jnp.concatenate([feature_grads, feature_rim], 1)
    input_grad, short_terms = short_back(tap_table, signal_pad, grads_pad)
    short_grad = short_terms.reshape(3 * lag_count, group_count, group_width).sum(-1)
    short_count = short_grad.shape[0]
    both_part = owned_sum(jnp.concatenate([short_grad, taps_grad], 0), "ctx")
    short_part = both_part[None, :short_count]
    medium_part = both_part[None, short_count:]
    incoming = passed_along(input_grad[None], "section", -1)
    return (incoming, short_part, medium_part)


def solution(mesh):
    in_specs = (
        P("section", "ctx", "dp"),
        P("section", "ctx", "dp"),
        P("section", None, "dp"),
        P("section", None, "dp"),
    )
    out_specs = (
        P("section", "ctx", "dp"),
        P("section", None, ("dp", "ctx")),
        P("section", None, ("dp", "ctx")),
    )
    return jax.shard_map(
        per_device, mesh=mesh, in_specs=in_specs, out_specs=out_specs, check_vma=False
    )
```

```python
import jax
import jax.numpy as jnp
from jax import lax
from jax.experimental import pallas as pl
from jax.experimental.pallas import tpu as pltpu
from jax.sharding import PartitionSpec as P

LANE_BLOCK = 128


def passed_along(block, axis, distance):
    devices = range(lax.axis_size(axis))
    route = [(i - distance, i) for i in devices if i - distance in devices]
    return lax.ppermute(block, axis, route)


def owned_sum(partial_terms, axis):
    axis_len = lax.axis_size(axis)
    row_count, col_count = partial_terms.shape
    width = col_count // axis_len
    chunks = partial_terms.reshape(row_count, axis_len, width).transpose(1, 0, 2)
    return jnp.sum(lax.all_to_all(chunks, axis, 0, 0, tiled=False), axis=0)


def front_kernel(taps_ref, sig_ref, gy_ref, q_ref, k_ref, v_ref, kv_ref, gate_ref, xs_ref):
    rows = q_ref.shape[0]
    rim = sig_ref.shape[0] - rows
    lags = rim + 1
    xs_ref[pl.ds(0, rows + rim), :] = sig_ref[...].astype(jnp.float32)
    for branch, out_ref in enumerate((q_ref, k_ref, v_ref)):
        acc = None
        for offset in range(lags):
            term = taps_ref[pl.ds(branch * lags + offset, 1), :] * xs_ref[pl.ds(rim - offset, rows), :]
            acc = term if acc is None else acc + term
        out_ref[...] = acc.astype(jnp.bfloat16)
    kv_ref[...] = (k_ref[...].astype(jnp.float32) * v_ref[...].astype(jnp.float32)).astype(
        jnp.bfloat16
    )
    gate_ref[...] = (gy_ref[...].astype(jnp.float32) * q_ref[...].astype(jnp.float32)).astype(
        jnp.bfloat16
    )


def short_front(taps, signal_pad, grad_out):
    padded_rows, chan_count = signal_pad.shape
    rows = grad_out.shape[0]
    tap_rows = taps.shape[0]
    row_spec = pl.BlockSpec((rows, LANE_BLOCK), lambda j: (0, j))
    shape = jax.ShapeDtypeStruct((rows, chan_count), jnp.bfloat16)
    return pl.pallas_call(
        front_kernel,
        grid=(chan_count // LANE_BLOCK,),
        in_specs=[
            pl.BlockSpec((tap_rows, LANE_BLOCK), lambda j: (0, j)),
            pl.BlockSpec((padded_rows, LANE_BLOCK), lambda j: (0, j)),
            row_spec,
        ],
        out_specs=[row_spec] * 5,
        out_shape=[shape] * 5,
        scratch_shapes=[pltpu.VMEM((padded_rows + 8, LANE_BLOCK), jnp.float32)],
    )(taps, signal_pad, grad_out)


def back_kernel(taps_ref, sig_ref, grads_ref, ig_ref, sp_ref, xs_ref, gs_ref):
    rows = ig_ref.shape[0]
    rim = sig_ref.shape[0] - rows
    lags = rim + 1
    branches = grads_ref.shape[0]
    xs_ref[pl.ds(0, rows + rim), :] = sig_ref[...].astype(jnp.float32)
    for branch in range(branches):
        gs_ref[branch, pl.ds(0, rows + rim), :] = grads_ref[branch].astype(jnp.float32)
    acc = None
    for branch in range(branches):
        for offset in range(lags):
            term = taps_ref[pl.ds(branch * lags + offset, 1), :] * gs_ref[branch, pl.ds(offset, rows), :]
            acc = term if acc is None else acc + term
    ig_ref[...] = acc.astype(jnp.bfloat16)
    for branch in range(branches):
        grads_f = gs_ref[branch, pl.ds(0, rows), :]
        for offset in range(lags):
            prod = grads_f * xs_ref[pl.ds(rim - offset, rows), :]
            sp_ref[pl.ds(branch * lags + offset, 1), :] = jnp.sum(prod, axis=0, keepdims=True)


def short_back(taps, signal_pad, grads_pad):
    padded_rows, chan_count = signal_pad.shape
    branches = grads_pad.shape[0]
    tap_rows = taps.shape[0]
    rows = padded_rows - (tap_rows // branches - 1)
    return pl.pallas_call(
        back_kernel,
        grid=(chan_count // LANE_BLOCK,),
        in_specs=[
            pl.BlockSpec((tap_rows, LANE_BLOCK), lambda j: (0, j)),
            pl.BlockSpec((padded_rows, LANE_BLOCK), lambda j: (0, j)),
            pl.BlockSpec((branches, padded_rows, LANE_BLOCK), lambda j: (0, 0, j)),
        ],
        out_specs=[
            pl.BlockSpec((rows, LANE_BLOCK), lambda j: (0, j)),
            pl.BlockSpec((tap_rows, LANE_BLOCK), lambda j: (0, j)),
        ],
        out_shape=[
            jax.ShapeDtypeStruct((rows, chan_count), jnp.bfloat16),
            jax.ShapeDtypeStruct((tap_rows, chan_count), jnp.float32),
        ],
        scratch_shapes=[
            pltpu.VMEM((padded_rows + 8, LANE_BLOCK), jnp.float32),
            pltpu.VMEM((branches, padded_rows + 8, LANE_BLOCK), jnp.float32),
        ],
    )(taps, signal_pad, grads_pad)


def medium_kernel(fwd_ref, bwd_ref, kv_ref, kvf_ref, gate_ref, mixed_ref, back_ref, taps_ref):
    group_block, span = fwd_ref.shape
    rows = taps_ref.shape[1]
    block_count = mixed_ref.shape[0] // rows
    lanes = mixed_ref.shape[1]
    group_width = lanes // group_block
    lane_group = lax.broadcasted_iota(jnp.int32, (1, lanes), 1) // group_width
    mixed_ref[...] = jnp.zeros(mixed_ref.shape, mixed_ref.dtype)
    back_ref[...] = jnp.zeros(back_ref.shape, back_ref.dtype)
    for group in range(group_block):
        in_group = lane_group == group
        fwd = jnp.broadcast_to(fwd_ref[pl.ds(group, 1), :], (rows, span))
        bwd = jnp.broadcast_to(bwd_ref[pl.ds(group, 1), :], (rows, span))
        fwd_band = pltpu.roll(fwd, 0, 1, stride=1, stride_axis=0).astype(jnp.bfloat16)
        bwd_band = pltpu.roll(bwd, 0, 1, stride=1, stride_axis=0).astype(jnp.bfloat16)
        cross = None
        for blk in range(block_count):
            out_rows = pl.ds(blk * rows, rows)
            mixed = jnp.dot(fwd_band, kv_ref[pl.ds(blk * rows, span), :], preferred_element_type=jnp.float32)
            mixed_ref[out_rows, :] = jnp.where(in_group, mixed, mixed_ref[out_rows, :])
            back = jnp.dot(bwd_band, gate_ref[pl.ds(blk * rows, span), :], preferred_element_type=jnp.float32)
            back_ref[out_rows, :] = jnp.where(in_group, back, back_ref[out_rows, :])
            gate_rows = jnp.where(in_group, gate_ref[out_rows, :], jnp.zeros((), gate_ref.dtype))
            flipped = kvf_ref[pl.ds((block_count - 1 - blk) * rows, span), :]
            part = lax.dot_general(
                gate_rows, flipped, (((1,), (1,)), ((), ())), preferred_element_type=jnp.float32
            )
            cross = part if cross is None else cross + part
        rolled = pltpu.roll(cross, 0, 1, stride=1, stride_axis=0)
        taps_ref[pl.ds(group, 1), :] = jnp.sum(rolled[:, span - rows :], axis=0, keepdims=True)


def medium_terms(medium_taps, kv_pad, gate_ext, row_block):
    tap_count, group_count = medium_taps.shape
    seq_rows = gate_ext.shape[0] - tap_count + 1
    chan_count = kv_pad.shape[1]
    group_width = chan_count // group_count
    span = row_block + tap_count
    group_block = LANE_BLOCK // group_width
    zero_taps = jnp.zeros((group_count, span - tap_count), jnp.float32)
    fwd_taps = jnp.concatenate([jnp.flip(medium_taps, 0).T.astype(jnp.float32), zero_taps], 1)
    bwd_taps = jnp.concatenate([medium_taps.T.astype(jnp.float32), zero_taps], 1)
    zero_row = jnp.zeros((1, chan_count), kv_pad.dtype)
    kv_full = jnp.concatenate([kv_pad, zero_row], 0)
    gate_full = jnp.concatenate([gate_ext, zero_row], 0)
    padded_rows = kv_full.shape[0]
    taps_spec = pl.BlockSpec((group_block, span), lambda j: (j, 0))
    full_spec = pl.BlockSpec((padded_rows, LANE_BLOCK), lambda j: (0, j))
    out_spec = pl.BlockSpec((seq_rows, LANE_BLOCK), lambda j: (0, j))
    mixed_out, back_out, taps_grad = pl.pallas_call(
        medium_kernel,
        grid=(chan_count // LANE_BLOCK,),
        in_specs=[taps_spec, taps_spec, full_spec, full_spec, full_spec],
        out_specs=[out_spec, out_spec, pl.BlockSpec((group_block, tap_count), lambda j: (j, 0))],
        out_shape=[
            jax.ShapeDtypeStruct((seq_rows, chan_count), jnp.float32),
            jax.ShapeDtypeStruct((seq_rows, chan_count), jnp.float32),
            jax.ShapeDtypeStruct((group_count, tap_count), jnp.float32),
        ],
    )(fwd_taps, bwd_taps, kv_full, jnp.flip(kv_full, 0), gate_full)
    return mixed_out, back_out, taps_grad.T


def per_device(inputs, upstream, short_filter, medium_filter):
    signal = inputs[0]
    grad_out = upstream[0]
    seq_rows, chan_count = signal.shape
    tap_count = medium_filter.shape[1]
    group_count = medium_filter.shape[2]
    lag_count = short_filter.shape[1] // 3
    group_width = chan_count // group_count
    short_rim = lag_count - 1
    medium_rim = tap_count - 1
    chan_short = jnp.broadcast_to(
        short_filter[0].astype(jnp.float32).reshape(3, lag_count, group_count, 1),
        (3, lag_count, group_count, group_width),
    ).reshape(3, lag_count, chan_count)
    medium_taps = medium_filter[0]
    tap_table = chan_short.reshape(3 * lag_count, chan_count)
    signal_rim = passed_along(signal[seq_rows - short_rim :], "ctx", 1)
    signal_pad = jnp.concatenate([signal_rim, signal], 0)
    query_in, key_in, value_in, products, gate_grad = short_front(tap_table, signal_pad, grad_out)
    kv_rim, gate_rim = passed_along(products[seq_rows - medium_rim :], "ctx", 1), passed_along(
        gate_grad[:medium_rim], "ctx", -1
    )
    kv_pad = jnp.concatenate([kv_rim, products], 0)
    gate_ext = jnp.concatenate([gate_grad, gate_rim], 0)
    mixed_out, back_out, taps_grad = medium_terms(medium_taps, kv_pad, gate_ext, 128)
    query_grad = (grad_out.astype(jnp.float32) * mixed_out).astype(jnp.bfloat16)
    key_grad = (back_out * value_in.astype(jnp.float32)).astype(jnp.bfloat16)
    value_grad = (back_out * key_in.astype(jnp.float32)).astype(jnp.bfloat16)
    feature_grads = jnp.stack([query_grad, key_grad, value_grad])
    feature_rim = passed_along(feature_grads[:, :short_rim], "ctx", -1)
    grads_pad = jnp.concatenate([feature_grads, feature_rim], 1)
    input_grad, short_terms = short_back(tap_table, signal_pad, grads_pad)
    short_grad = short_terms.reshape(3 * lag_count, group_count, group_width).sum(-1)
    short_count = short_grad.shape[0]
    both_part = owned_sum(jnp.concatenate([short_grad, taps_grad], 0), "ctx")
    short_part = both_part[None, :short_count]
    medium_part = both_part[None, short_count:]
    incoming = passed_along(input_grad[None], "section", -1)
    return (incoming, short_part, medium_part)


def solution(mesh):
    in_specs = (
        P("section", "ctx", "dp"),
        P("section", "ctx", "dp"),
        P("section", None, "dp"),
        P("section", None, "dp"),
    )
    out_specs = (
        P("section", "ctx", "dp"),
        P("section", None, ("dp", "ctx")),
        P("section", None, ("dp", "ctx")),
    )
    return jax.shard_map(
        per_device, mesh=mesh, in_specs=in_specs, out_specs=out_specs, check_vma=False
    )
```

```python
import jax
import jax.numpy as jnp
from jax import lax
from jax.experimental import pallas as pl
from jax.experimental.pallas import tpu as pltpu
from jax.sharding import PartitionSpec as P

LANE_BLOCK = 128


def passed_along(block, axis, distance):
    devices = range(lax.axis_size(axis))
    route = [(i - distance, i) for i in devices if i - distance in devices]
    return lax.ppermute(block, axis, route)


def owned_sum(partial_terms, axis):
    axis_len = lax.axis_size(axis)
    row_count, col_count = partial_terms.shape
    width = col_count // axis_len
    chunks = partial_terms.reshape(row_count, axis_len, width).transpose(1, 0, 2)
    return jnp.sum(lax.all_to_all(chunks, axis, 0, 0, tiled=False), axis=0)


def front_kernel(taps_ref, sig_ref, gy_ref, q_ref, k_ref, v_ref, kv_ref, gate_ref, xs_ref):
    rows = q_ref.shape[0]
    rim = sig_ref.shape[0] - rows
    lags = rim + 1
    xs_ref[pl.ds(0, rows + rim), :] = sig_ref[...].astype(jnp.float32)
    for branch, out_ref in enumerate((q_ref, k_ref, v_ref)):
        acc = None
        for offset in range(lags):
            term = taps_ref[pl.ds(branch * lags + offset, 1), :] * xs_ref[pl.ds(rim - offset, rows), :]
            acc = term if acc is None else acc + term
        out_ref[...] = acc.astype(jnp.bfloat16)
    kv_ref[...] = (k_ref[...].astype(jnp.float32) * v_ref[...].astype(jnp.float32)).astype(
        jnp.bfloat16
    )
    gate_ref[...] = (gy_ref[...].astype(jnp.float32) * q_ref[...].astype(jnp.float32)).astype(
        jnp.bfloat16
    )


def short_front(taps, signal_pad, grad_out):
    padded_rows, chan_count = signal_pad.shape
    rows = grad_out.shape[0]
    tap_rows = taps.shape[0]
    row_spec = pl.BlockSpec((rows, LANE_BLOCK), lambda j: (0, j))
    shape = jax.ShapeDtypeStruct((rows, chan_count), jnp.bfloat16)
    return pl.pallas_call(
        front_kernel,
        grid=(chan_count // LANE_BLOCK,),
        in_specs=[
            pl.BlockSpec((tap_rows, LANE_BLOCK), lambda j: (0, j)),
            pl.BlockSpec((padded_rows, LANE_BLOCK), lambda j: (0, j)),
            row_spec,
        ],
        out_specs=[row_spec] * 5,
        out_shape=[shape] * 5,
        scratch_shapes=[pltpu.VMEM((padded_rows + 8, LANE_BLOCK), jnp.float32)],
    )(taps, signal_pad, grad_out)


def back_kernel(taps_ref, sig_ref, grads_ref, ig_ref, sp_ref, xs_ref, gs_ref):
    rows = ig_ref.shape[0]
    rim = sig_ref.shape[0] - rows
    lags = rim + 1
    branches = grads_ref.shape[0]
    xs_ref[pl.ds(0, rows + rim), :] = sig_ref[...].astype(jnp.float32)
    for branch in range(branches):
        gs_ref[branch, pl.ds(0, rows + rim), :] = grads_ref[branch].astype(jnp.float32)
    acc = None
    for branch in range(branches):
        for offset in range(lags):
            term = taps_ref[pl.ds(branch * lags + offset, 1), :] * gs_ref[branch, pl.ds(offset, rows), :]
            acc = term if acc is None else acc + term
    ig_ref[...] = acc.astype(jnp.bfloat16)
    for branch in range(branches):
        grads_f = gs_ref[branch, pl.ds(0, rows), :]
        for offset in range(lags):
            prod = grads_f * xs_ref[pl.ds(rim - offset, rows), :]
            sp_ref[pl.ds(branch * lags + offset, 1), :] = jnp.sum(prod, axis=0, keepdims=True)


def short_back(taps, signal_pad, grads_pad):
    padded_rows, chan_count = signal_pad.shape
    branches = grads_pad.shape[0]
    tap_rows = taps.shape[0]
    rows = padded_rows - (tap_rows // branches - 1)
    return pl.pallas_call(
        back_kernel,
        grid=(chan_count // LANE_BLOCK,),
        in_specs=[
            pl.BlockSpec((tap_rows, LANE_BLOCK), lambda j: (0, j)),
            pl.BlockSpec((padded_rows, LANE_BLOCK), lambda j: (0, j)),
            pl.BlockSpec((branches, padded_rows, LANE_BLOCK), lambda j: (0, 0, j)),
        ],
        out_specs=[
            pl.BlockSpec((rows, LANE_BLOCK), lambda j: (0, j)),
            pl.BlockSpec((tap_rows, LANE_BLOCK), lambda j: (0, j)),
        ],
        out_shape=[
            jax.ShapeDtypeStruct((rows, chan_count), jnp.bfloat16),
            jax.ShapeDtypeStruct((tap_rows, chan_count), jnp.float32),
        ],
        scratch_shapes=[
            pltpu.VMEM((padded_rows + 8, LANE_BLOCK), jnp.float32),
            pltpu.VMEM((branches, padded_rows + 8, LANE_BLOCK), jnp.float32),
        ],
    )(taps, signal_pad, grads_pad)


def medium_kernel(fwd_ref, bwd_ref, kv_ref, gate_ref, mixed_ref, back_ref, taps_ref):
    group_block, span = fwd_ref.shape
    padded_rows = kv_ref.shape[0]
    row_id = lax.broadcasted_iota(jnp.int32, (padded_rows, padded_rows), 0)
    col_id = lax.broadcasted_iota(jnp.int32, (padded_rows, padded_rows), 1)
    reversal = (row_id + col_id == padded_rows - 1).astype(kv_ref.dtype)
    kv_flipped = jnp.dot(reversal, kv_ref[...], preferred_element_type=jnp.float32).astype(
        kv_ref.dtype
    )
    rows = taps_ref.shape[1]
    block_count = mixed_ref.shape[0] // rows
    lanes = mixed_ref.shape[1]
    group_width = lanes // group_block
    lane_group = lax.broadcasted_iota(jnp.int32, (1, lanes), 1) // group_width
    mixed_ref[...] = jnp.zeros(mixed_ref.shape, mixed_ref.dtype)
    back_ref[...] = jnp.zeros(back_ref.shape, back_ref.dtype)
    for group in range(group_block):
        in_group = lane_group == group
        fwd = jnp.broadcast_to(fwd_ref[pl.ds(group, 1), :], (rows, span))
        bwd = jnp.broadcast_to(bwd_ref[pl.ds(group, 1), :], (rows, span))
        fwd_band = pltpu.roll(fwd, 0, 1, stride=1, stride_axis=0).astype(jnp.bfloat16)
        bwd_band = pltpu.roll(bwd, 0, 1, stride=1, stride_axis=0).astype(jnp.bfloat16)
        cross = None
        for blk in range(block_count):
            out_rows = pl.ds(blk * rows, rows)
            mixed = jnp.dot(fwd_band, kv_ref[pl.ds(blk * rows, span), :], preferred_element_type=jnp.float32)
            mixed_ref[out_rows, :] = jnp.where(in_group, mixed, mixed_ref[out_rows, :])
            back = jnp.dot(bwd_band, gate_ref[pl.ds(blk * rows, span), :], preferred_element_type=jnp.float32)
            back_ref[out_rows, :] = jnp.where(in_group, back, back_ref[out_rows, :])
            gate_rows = jnp.where(in_group, gate_ref[out_rows, :], jnp.zeros((), gate_ref.dtype))
            flip_start = (block_count - 1 - blk) * rows
            flipped = kv_flipped[flip_start : flip_start + span]
            part = lax.dot_general(
                gate_rows, flipped, (((1,), (1,)), ((), ())), preferred_element_type=jnp.float32
            )
            cross = part if cross is None else cross + part
        rolled = pltpu.roll(cross, 0, 1, stride=1, stride_axis=0)
        taps_ref[pl.ds(group, 1), :] = jnp.sum(rolled[:, span - rows :], axis=0, keepdims=True)


def medium_terms(medium_taps, kv_pad, gate_ext, row_block):
    tap_count, group_count = medium_taps.shape
    seq_rows = gate_ext.shape[0] - tap_count + 1
    chan_count = kv_pad.shape[1]
    group_width = chan_count // group_count
    span = row_block + tap_count
    group_block = LANE_BLOCK // group_width
    zero_taps = jnp.zeros((group_count, span - tap_count), jnp.float32)
    fwd_taps = jnp.concatenate([jnp.flip(medium_taps, 0).T.astype(jnp.float32), zero_taps], 1)
    bwd_taps = jnp.concatenate([medium_taps.T.astype(jnp.float32), zero_taps], 1)
    zero_row = jnp.zeros((1, chan_count), kv_pad.dtype)
    kv_full = jnp.concatenate([kv_pad, zero_row], 0)
    gate_full = jnp.concatenate([gate_ext, zero_row], 0)
    padded_rows = kv_full.shape[0]
    taps_spec = pl.BlockSpec((group_block, span), lambda j: (j, 0))
    full_spec = pl.BlockSpec((padded_rows, LANE_BLOCK), lambda j: (0, j))
    out_spec = pl.BlockSpec((seq_rows, LANE_BLOCK), lambda j: (0, j))
    mixed_out, back_out, taps_grad = pl.pallas_call(
        medium_kernel,
        grid=(chan_count // LANE_BLOCK,),
        in_specs=[taps_spec, taps_spec, full_spec, full_spec],
        out_specs=[out_spec, out_spec, pl.BlockSpec((group_block, tap_count), lambda j: (j, 0))],
        out_shape=[
            jax.ShapeDtypeStruct((seq_rows, chan_count), jnp.float32),
            jax.ShapeDtypeStruct((seq_rows, chan_count), jnp.float32),
            jax.ShapeDtypeStruct((group_count, tap_count), jnp.float32),
        ],
    )(fwd_taps, bwd_taps, kv_full, gate_full)
    return mixed_out, back_out, taps_grad.T


def per_device(inputs, upstream, short_filter, medium_filter):
    signal = inputs[0]
    grad_out = upstream[0]
    seq_rows, chan_count = signal.shape
    tap_count = medium_filter.shape[1]
    group_count = medium_filter.shape[2]
    lag_count = short_filter.shape[1] // 3
    group_width = chan_count // group_count
    short_rim = lag_count - 1
    medium_rim = tap_count - 1
    chan_short = jnp.broadcast_to(
        short_filter[0].astype(jnp.float32).reshape(3, lag_count, group_count, 1),
        (3, lag_count, group_count, group_width),
    ).reshape(3, lag_count, chan_count)
    medium_taps = medium_filter[0]
    tap_table = chan_short.reshape(3 * lag_count, chan_count)
    signal_rim = passed_along(signal[seq_rows - short_rim :], "ctx", 1)
    signal_pad = jnp.concatenate([signal_rim, signal], 0)
    query_in, key_in, value_in, products, gate_grad = short_front(tap_table, signal_pad, grad_out)
    kv_rim, gate_rim = passed_along(products[seq_rows - medium_rim :], "ctx", 1), passed_along(
        gate_grad[:medium_rim], "ctx", -1
    )
    kv_pad = jnp.concatenate([kv_rim, products], 0)
    gate_ext = jnp.concatenate([gate_grad, gate_rim], 0)
    mixed_out, back_out, taps_grad = medium_terms(medium_taps, kv_pad, gate_ext, 128)
    query_grad = (grad_out.astype(jnp.float32) * mixed_out).astype(jnp.bfloat16)
    key_grad = (back_out * value_in.astype(jnp.float32)).astype(jnp.bfloat16)
    value_grad = (back_out * key_in.astype(jnp.float32)).astype(jnp.bfloat16)
    feature_grads = jnp.stack([query_grad, key_grad, value_grad])
    feature_rim = passed_along(feature_grads[:, :short_rim], "ctx", -1)
    grads_pad = jnp.concatenate([feature_grads, feature_rim], 1)
    input_grad, short_terms = short_back(tap_table, signal_pad, grads_pad)
    short_grad = short_terms.reshape(3 * lag_count, group_count, group_width).sum(-1)
    short_count = short_grad.shape[0]
    both_part = owned_sum(jnp.concatenate([short_grad, taps_grad], 0), "ctx")
    short_part = both_part[None, :short_count]
    medium_part = both_part[None, short_count:]
    incoming = passed_along(input_grad[None], "section", -1)
    return (incoming, short_part, medium_part)


def solution(mesh):
    in_specs = (
        P("section", "ctx", "dp"),
        P("section", "ctx", "dp"),
        P("section", None, "dp"),
        P("section", None, "dp"),
    )
    out_specs = (
        P("section", "ctx", "dp"),
        P("section", None, ("dp", "ctx")),
        P("section", None, ("dp", "ctx")),
    )
    return jax.shard_map(
        per_device, mesh=mesh, in_specs=in_specs, out_specs=out_specs, check_vma=False
    )
```

```python
import jax
import jax.numpy as jnp
from jax import lax
from jax.experimental import pallas as pl
from jax.experimental.pallas import tpu as pltpu
from jax.sharding import PartitionSpec as P

LANE_BLOCK = 128


def passed_along(block, axis, distance):
    devices = range(lax.axis_size(axis))
    route = [(i - distance, i) for i in devices if i - distance in devices]
    return lax.ppermute(block, axis, route)


def owned_sum(partial_terms, axis):
    axis_len = lax.axis_size(axis)
    row_count, col_count = partial_terms.shape
    width = col_count // axis_len
    chunks = partial_terms.reshape(row_count, axis_len, width).transpose(1, 0, 2)
    return jnp.sum(lax.all_to_all(chunks, axis, 0, 0, tiled=False), axis=0)


def front_kernel(taps_ref, sig_ref, gy_ref, q_ref, k_ref, v_ref, kv_ref, gate_ref, xs_ref):
    rows = q_ref.shape[0]
    rim = sig_ref.shape[0] - rows
    lags = rim + 1
    xs_ref[pl.ds(0, rows + rim), :] = sig_ref[...].astype(jnp.float32)
    for branch, out_ref in enumerate((q_ref, k_ref, v_ref)):
        acc = None
        for offset in range(lags):
            term = taps_ref[pl.ds(branch * lags + offset, 1), :] * xs_ref[pl.ds(rim - offset, rows), :]
            acc = term if acc is None else acc + term
        out_ref[...] = acc.astype(jnp.bfloat16)
    kv_ref[...] = (k_ref[...].astype(jnp.float32) * v_ref[...].astype(jnp.float32)).astype(
        jnp.bfloat16
    )
    gate_ref[...] = (gy_ref[...].astype(jnp.float32) * q_ref[...].astype(jnp.float32)).astype(
        jnp.bfloat16
    )


def short_front(taps, signal_pad, grad_out):
    padded_rows, chan_count = signal_pad.shape
    rows = grad_out.shape[0]
    tap_rows = taps.shape[0]
    row_spec = pl.BlockSpec((rows, LANE_BLOCK), lambda j: (0, j))
    shape = jax.ShapeDtypeStruct((rows, chan_count), jnp.bfloat16)
    return pl.pallas_call(
        front_kernel,
        grid=(chan_count // LANE_BLOCK,),
        in_specs=[
            pl.BlockSpec((tap_rows, LANE_BLOCK), lambda j: (0, j)),
            pl.BlockSpec((padded_rows, LANE_BLOCK), lambda j: (0, j)),
            row_spec,
        ],
        out_specs=[row_spec] * 5,
        out_shape=[shape] * 5,
        scratch_shapes=[pltpu.VMEM((padded_rows + 8, LANE_BLOCK), jnp.float32)],
    )(taps, signal_pad, grad_out)


def input_grad_kernel(taps_ref, grads_ref, rim_ref, ig_ref, gs_ref):
    branches, rows, lanes = grads_ref.shape
    rim = rim_ref.shape[1]
    lags = rim + 1
    for branch in range(branches):
        gs_ref[branch, pl.ds(0, rows), :] = grads_ref[branch].astype(jnp.float32)
        gs_ref[branch, pl.ds(rows, rim), :] = rim_ref[branch].astype(jnp.float32)
    acc = None
    for branch in range(branches):
        for offset in range(lags):
            term = taps_ref[pl.ds(branch * lags + offset, 1), :] * gs_ref[branch, pl.ds(offset, rows), :]
            acc = term if acc is None else acc + term
    ig_ref[...] = acc.astype(jnp.bfloat16)


def short_partial_kernel(sig_ref, grads_ref, sp_ref, xs_ref):
    branches, rows, lanes = grads_ref.shape
    rim = sig_ref.shape[0] - rows
    lags = rim + 1
    xs_ref[pl.ds(0, rows + rim), :] = sig_ref[...].astype(jnp.float32)
    for branch in range(branches):
        grads_f = grads_ref[branch].astype(jnp.float32)
        for offset in range(lags):
            prod = grads_f * xs_ref[pl.ds(rim - offset, rows), :]
            sp_ref[pl.ds(branch * lags + offset, 1), :] = jnp.sum(prod, axis=0, keepdims=True)


def short_partials(signal_pad, feature_grads):
    padded_rows, chan_count = signal_pad.shape
    branches, rows, _ = feature_grads.shape
    tap_rows = branches * (padded_rows - rows + 1)
    return pl.pallas_call(
        short_partial_kernel,
        grid=(chan_count // LANE_BLOCK,),
        in_specs=[
            pl.BlockSpec((padded_rows, LANE_BLOCK), lambda j: (0, j)),
            pl.BlockSpec((branches, rows, LANE_BLOCK), lambda j: (0, 0, j)),
        ],
        out_specs=pl.BlockSpec((tap_rows, LANE_BLOCK), lambda j: (0, j)),
        out_shape=jax.ShapeDtypeStruct((tap_rows, chan_count), jnp.float32),
        scratch_shapes=[pltpu.VMEM((padded_rows + 8, LANE_BLOCK), jnp.float32)],
    )(signal_pad, feature_grads)


def input_grads(taps, feature_grads, feature_rim):
    branches, rows, chan_count = feature_grads.shape
    rim = feature_rim.shape[1]
    return pl.pallas_call(
        input_grad_kernel,
        grid=(chan_count // LANE_BLOCK,),
        in_specs=[
            pl.BlockSpec((taps.shape[0], LANE_BLOCK), lambda j: (0, j)),
            pl.BlockSpec((branches, rows, LANE_BLOCK), lambda j: (0, 0, j)),
            pl.BlockSpec((branches, rim, LANE_BLOCK), lambda j: (0, 0, j)),
        ],
        out_specs=pl.BlockSpec((rows, LANE_BLOCK), lambda j: (0, j)),
        out_shape=jax.ShapeDtypeStruct((rows, chan_count), jnp.bfloat16),
        scratch_shapes=[pltpu.VMEM((branches, rows + rim + 2, LANE_BLOCK), jnp.float32)],
    )(taps, feature_grads, feature_rim)


def medium_kernel(
    fwd_ref, bwd_ref, kv_rim_ref, prod_ref, gate_ref, gate_rim_ref, gy_ref, key_ref, value_ref,
    grads_ref, taps_ref, kv_s, gate_s, mixed_s, back_s,
):
    group_block, span = fwd_ref.shape
    rows = taps_ref.shape[1]
    seq_rows, lanes = gy_ref.shape
    block_count = seq_rows // rows
    rim = kv_rim_ref.shape[0]
    padded_rows = kv_s.shape[0]
    kv_s[pl.ds(0, rim), :] = kv_rim_ref[...].astype(jnp.float32)
    kv_s[pl.ds(rim, seq_rows), :] = prod_ref[...].astype(jnp.float32)
    kv_s[pl.ds(rim + seq_rows, padded_rows - rim - seq_rows), :] = jnp.zeros(
        (padded_rows - rim - seq_rows, lanes), jnp.float32
    )
    gate_s[pl.ds(0, seq_rows), :] = gate_ref[...].astype(jnp.float32)
    gate_s[pl.ds(seq_rows, rim), :] = gate_rim_ref[...].astype(jnp.float32)
    gate_s[pl.ds(rim + seq_rows, padded_rows - rim - seq_rows), :] = jnp.zeros(
        (padded_rows - rim - seq_rows, lanes), jnp.float32
    )
    kv_all = kv_s[...].astype(jnp.bfloat16)
    gate_all = gate_s[...].astype(jnp.bfloat16)
    row_id = lax.broadcasted_iota(jnp.int32, (padded_rows, padded_rows), 0)
    col_id = lax.broadcasted_iota(jnp.int32, (padded_rows, padded_rows), 1)
    reversal = (row_id + col_id == padded_rows - 1).astype(jnp.bfloat16)
    kv_flipped = jnp.dot(reversal, kv_all, preferred_element_type=jnp.float32).astype(jnp.bfloat16)
    group_width = lanes // group_block
    lane_group = lax.broadcasted_iota(jnp.int32, (1, lanes), 1) // group_width
    mixed_s[...] = jnp.zeros(mixed_s.shape, mixed_s.dtype)
    back_s[...] = jnp.zeros(back_s.shape, back_s.dtype)
    for group in range(group_block):
        in_group = lane_group == group
        fwd = jnp.broadcast_to(fwd_ref[pl.ds(group, 1), :], (rows, span))
        bwd = jnp.broadcast_to(bwd_ref[pl.ds(group, 1), :], (rows, span))
        fwd_band = pltpu.roll(fwd, 0, 1, stride=1, stride_axis=0).astype(jnp.bfloat16)
        bwd_band = pltpu.roll(bwd, 0, 1, stride=1, stride_axis=0).astype(jnp.bfloat16)
        cross = None
        for blk in range(block_count):
            start = blk * rows
            out_rows = pl.ds(start, rows)
            mixed = jnp.dot(fwd_band, kv_all[start : start + span], preferred_element_type=jnp.float32)
            mixed_s[out_rows, :] = jnp.where(in_group, mixed, mixed_s[out_rows, :])
            back = jnp.dot(bwd_band, gate_all[start : start + span], preferred_element_type=jnp.float32)
            back_s[out_rows, :] = jnp.where(in_group, back, back_s[out_rows, :])
            gate_rows = jnp.where(in_group, gate_all[start : start + rows], jnp.zeros((), jnp.bfloat16))
            flip_start = (block_count - 1 - blk) * rows
            part = lax.dot_general(
                gate_rows,
                kv_flipped[flip_start : flip_start + span],
                (((1,), (1,)), ((), ())),
                preferred_element_type=jnp.float32,
            )
            cross = part if cross is None else cross + part
        rolled = pltpu.roll(cross, 0, 1, stride=1, stride_axis=0)
        taps_ref[pl.ds(group, 1), :] = jnp.sum(rolled[:, span - rows :], axis=0, keepdims=True)
    back_all = back_s[...]
    grads_ref[0] = (gy_ref[...].astype(jnp.float32) * mixed_s[...]).astype(jnp.bfloat16)
    grads_ref[1] = (back_all * value_ref[...].astype(jnp.float32)).astype(jnp.bfloat16)
    grads_ref[2] = (back_all * key_ref[...].astype(jnp.float32)).astype(jnp.bfloat16)


def medium_terms(medium_taps, kv_rim, products, gate_grad, gate_rim, grad_out, key_in, value_in):
    tap_count, group_count = medium_taps.shape
    seq_rows, chan_count = products.shape
    group_width = chan_count // group_count
    row_block = tap_count
    span = row_block + tap_count
    padded_rows = seq_rows + tap_count
    group_block = LANE_BLOCK // group_width
    zero_taps = jnp.zeros((group_count, span - tap_count), jnp.float32)
    fwd_taps = jnp.concatenate([jnp.flip(medium_taps, 0).T.astype(jnp.float32), zero_taps], 1)
    bwd_taps = jnp.concatenate([medium_taps.T.astype(jnp.float32), zero_taps], 1)
    taps_spec = pl.BlockSpec((group_block, span), lambda j: (j, 0))
    rim_spec = pl.BlockSpec((kv_rim.shape[0], LANE_BLOCK), lambda j: (0, j))
    row_spec = pl.BlockSpec((seq_rows, LANE_BLOCK), lambda j: (0, j))
    grads, taps_grad = pl.pallas_call(
        medium_kernel,
        grid=(chan_count // LANE_BLOCK,),
        in_specs=[taps_spec, taps_spec, rim_spec, row_spec, row_spec, rim_spec, row_spec, row_spec, row_spec],
        out_specs=[
            pl.BlockSpec((3, seq_rows, LANE_BLOCK), lambda j: (0, 0, j)),
            pl.BlockSpec((group_block, tap_count), lambda j: (j, 0)),
        ],
        out_shape=[
            jax.ShapeDtypeStruct((3, seq_rows, chan_count), jnp.bfloat16),
            jax.ShapeDtypeStruct((group_count, tap_count), jnp.float32),
        ],
        scratch_shapes=[
            pltpu.VMEM((padded_rows, LANE_BLOCK), jnp.float32),
            pltpu.VMEM((padded_rows, LANE_BLOCK), jnp.float32),
            pltpu.VMEM((seq_rows, LANE_BLOCK), jnp.float32),
            pltpu.VMEM((seq_rows, LANE_BLOCK), jnp.float32),
        ],
    )(fwd_taps, bwd_taps, kv_rim, products, gate_grad, gate_rim, grad_out, key_in, value_in)
    return grads, taps_grad.T


def per_device(inputs, upstream, short_filter, medium_filter):
    signal = inputs[0]
    grad_out = upstream[0]
    seq_rows, chan_count = signal.shape
    tap_count = medium_filter.shape[1]
    group_count = medium_filter.shape[2]
    lag_count = short_filter.shape[1] // 3
    group_width = chan_count // group_count
    short_rim = lag_count - 1
    medium_rim = tap_count - 1
    chan_short = jnp.broadcast_to(
        short_filter[0].astype(jnp.float32).reshape(3, lag_count, group_count, 1),
        (3, lag_count, group_count, group_width),
    ).reshape(3, lag_count, chan_count)
    medium_taps = medium_filter[0]
    tap_table = chan_short.reshape(3 * lag_count, chan_count)
    signal_rim = passed_along(signal[seq_rows - short_rim :], "ctx", 1)
    signal_pad = jnp.concatenate([signal_rim, signal], 0)
    query_in, key_in, value_in, products, gate_grad = short_front(tap_table, signal_pad, grad_out)
    kv_rim, gate_rim = passed_along(products[seq_rows - medium_rim :], "ctx", 1), passed_along(
        gate_grad[:medium_rim], "ctx", -1
    )
    feature_grads, taps_grad = medium_terms(
        medium_taps, kv_rim, products, gate_grad, gate_rim, grad_out, key_in, value_in
    )
    feature_rim = passed_along(feature_grads[:, :short_rim], "ctx", -1)
    short_terms = short_partials(signal_pad, feature_grads)
    input_grad = input_grads(tap_table, feature_grads, feature_rim)
    short_grad = short_terms.reshape(3 * lag_count, group_count, group_width).sum(-1)
    short_count = short_grad.shape[0]
    both_part = owned_sum(jnp.concatenate([short_grad, taps_grad], 0), "ctx")
    short_part = both_part[None, :short_count]
    medium_part = both_part[None, short_count:]
    incoming = passed_along(input_grad[None], "section", -1)
    return (incoming, short_part, medium_part)


def solution(mesh):
    in_specs = (
        P("section", "ctx", "dp"),
        P("section", "ctx", "dp"),
        P("section", None, "dp"),
        P("section", None, "dp"),
    )
    out_specs = (
        P("section", "ctx", "dp"),
        P("section", None, ("dp", "ctx")),
        P("section", None, ("dp", "ctx")),
    )
    return jax.shard_map(
        per_device, mesh=mesh, in_specs=in_specs, out_specs=out_specs, check_vma=False
    )
```

```python
import jax
import jax.numpy as jnp
from jax import lax
from jax.experimental import pallas as pl
from jax.experimental.pallas import tpu as pltpu
from jax.sharding import PartitionSpec as P

LANE_BLOCK = 128


def passed_along(block, axis, distance):
    devices = range(lax.axis_size(axis))
    route = [(i - distance, i) for i in devices if i - distance in devices]
    return lax.ppermute(block, axis, route)


def owned_sum(partial_terms, axis):
    axis_len = lax.axis_size(axis)
    row_count, col_count = partial_terms.shape
    width = col_count // axis_len
    chunks = partial_terms.reshape(row_count, axis_len, width).transpose(1, 0, 2)
    return jnp.sum(lax.all_to_all(chunks, axis, 0, 0, tiled=False), axis=0)


def front_kernel(taps_ref, sig_ref, gy_ref, q_ref, k_ref, v_ref, kv_ref, gate_ref, xs_ref):
    rows = q_ref.shape[0]
    rim = sig_ref.shape[0] - rows
    lags = rim + 1
    xs_ref[pl.ds(0, rows + rim), :] = sig_ref[...].astype(jnp.float32)
    for branch, out_ref in enumerate((q_ref, k_ref, v_ref)):
        acc = None
        for offset in range(lags):
            term = taps_ref[pl.ds(branch * lags + offset, 1), :] * xs_ref[pl.ds(rim - offset, rows), :]
            acc = term if acc is None else acc + term
        out_ref[...] = acc.astype(jnp.bfloat16)
    kv_ref[...] = (k_ref[...].astype(jnp.float32) * v_ref[...].astype(jnp.float32)).astype(
        jnp.bfloat16
    )
    gate_ref[...] = (gy_ref[...].astype(jnp.float32) * q_ref[...].astype(jnp.float32)).astype(
        jnp.bfloat16
    )


def short_front(taps, signal_pad, grad_out):
    padded_rows, chan_count = signal_pad.shape
    rows = grad_out.shape[0]
    tap_rows = taps.shape[0]
    row_spec = pl.BlockSpec((rows, LANE_BLOCK), lambda j: (0, j))
    shape = jax.ShapeDtypeStruct((rows, chan_count), jnp.bfloat16)
    return pl.pallas_call(
        front_kernel,
        grid=(chan_count // LANE_BLOCK,),
        in_specs=[
            pl.BlockSpec((tap_rows, LANE_BLOCK), lambda j: (0, j)),
            pl.BlockSpec((padded_rows, LANE_BLOCK), lambda j: (0, j)),
            row_spec,
        ],
        out_specs=[row_spec] * 5,
        out_shape=[shape] * 5,
        scratch_shapes=[pltpu.VMEM((padded_rows + 8, LANE_BLOCK), jnp.float32)],
    )(taps, signal_pad, grad_out)


def input_grad_kernel(taps_ref, grads_ref, rim_ref, ig_ref, gs_ref):
    branches, rows, lanes = grads_ref.shape
    rim = rim_ref.shape[1]
    lags = rim + 1
    for branch in range(branches):
        gs_ref[branch, pl.ds(0, rows), :] = grads_ref[branch].astype(jnp.float32)
        gs_ref[branch, pl.ds(rows, rim), :] = rim_ref[branch].astype(jnp.float32)
    acc = None
    for branch in range(branches):
        for offset in range(lags):
            term = taps_ref[pl.ds(branch * lags + offset, 1), :] * gs_ref[branch, pl.ds(offset, rows), :]
            acc = term if acc is None else acc + term
    ig_ref[...] = acc.astype(jnp.bfloat16)


def short_partial_kernel(sig_ref, grads_ref, sp_ref, xs_ref):
    branches, rows, lanes = grads_ref.shape
    rim = sig_ref.shape[0] - rows
    lags = rim + 1
    xs_ref[pl.ds(0, rows + rim), :] = sig_ref[...].astype(jnp.float32)
    for branch in range(branches):
        grads_f = grads_ref[branch].astype(jnp.float32)
        for offset in range(lags):
            prod = grads_f * xs_ref[pl.ds(rim - offset, rows), :]
            sp_ref[pl.ds(branch * lags + offset, 1), :] = jnp.sum(prod, axis=0, keepdims=True)


def short_partials(signal_pad, feature_grads):
    padded_rows, chan_count = signal_pad.shape
    branches, rows, _ = feature_grads.shape
    tap_rows = branches * (padded_rows - rows + 1)
    return pl.pallas_call(
        short_partial_kernel,
        grid=(chan_count // LANE_BLOCK,),
        in_specs=[
            pl.BlockSpec((padded_rows, LANE_BLOCK), lambda j: (0, j)),
            pl.BlockSpec((branches, rows, LANE_BLOCK), lambda j: (0, 0, j)),
        ],
        out_specs=pl.BlockSpec((tap_rows, LANE_BLOCK), lambda j: (0, j)),
        out_shape=jax.ShapeDtypeStruct((tap_rows, chan_count), jnp.float32),
        scratch_shapes=[pltpu.VMEM((padded_rows + 8, LANE_BLOCK), jnp.float32)],
    )(signal_pad, feature_grads)


def input_grads(taps, feature_grads, feature_rim):
    branches, rows, chan_count = feature_grads.shape
    rim = feature_rim.shape[1]
    return pl.pallas_call(
        input_grad_kernel,
        grid=(chan_count // LANE_BLOCK,),
        in_specs=[
            pl.BlockSpec((taps.shape[0], LANE_BLOCK), lambda j: (0, j)),
            pl.BlockSpec((branches, rows, LANE_BLOCK), lambda j: (0, 0, j)),
            pl.BlockSpec((branches, rim, LANE_BLOCK), lambda j: (0, 0, j)),
        ],
        out_specs=pl.BlockSpec((rows, LANE_BLOCK), lambda j: (0, j)),
        out_shape=jax.ShapeDtypeStruct((rows, chan_count), jnp.bfloat16),
        scratch_shapes=[pltpu.VMEM((branches, rows + rim + 2, LANE_BLOCK), jnp.float32)],
    )(taps, feature_grads, feature_rim)


def medium_kernel(
    fwd_ref, bwd_ref, kv_rim_ref, prod_ref, gate_ref, gate_rim_ref, gy_ref, key_ref, value_ref,
    grads_ref, taps_ref, kv_s, gate_s, mixed_s, back_s,
):
    group_block, span = fwd_ref.shape
    rows = taps_ref.shape[1]
    seq_rows, lanes = gy_ref.shape
    block_count = seq_rows // rows
    rim = kv_rim_ref.shape[0]
    padded_rows = kv_s.shape[0]
    kv_s[pl.ds(0, rim), :] = kv_rim_ref[...].astype(jnp.float32)
    kv_s[pl.ds(rim, seq_rows), :] = prod_ref[...].astype(jnp.float32)
    kv_s[pl.ds(rim + seq_rows, padded_rows - rim - seq_rows), :] = jnp.zeros(
        (padded_rows - rim - seq_rows, lanes), jnp.float32
    )
    gate_s[pl.ds(0, seq_rows), :] = gate_ref[...].astype(jnp.float32)
    gate_s[pl.ds(seq_rows, rim), :] = gate_rim_ref[...].astype(jnp.float32)
    gate_s[pl.ds(rim + seq_rows, padded_rows - rim - seq_rows), :] = jnp.zeros(
        (padded_rows - rim - seq_rows, lanes), jnp.float32
    )
    kv_all = kv_s[...].astype(jnp.bfloat16)
    gate_all = gate_s[...].astype(jnp.bfloat16)
    row_id = lax.broadcasted_iota(jnp.int32, (padded_rows, padded_rows), 0)
    col_id = lax.broadcasted_iota(jnp.int32, (padded_rows, padded_rows), 1)
    reversal = (row_id + col_id == padded_rows - 1).astype(jnp.bfloat16)
    kv_flipped = jnp.dot(reversal, kv_all, preferred_element_type=jnp.float32).astype(jnp.bfloat16)
    group_width = lanes // group_block
    lane_group = lax.broadcasted_iota(jnp.int32, (1, lanes), 1) // group_width
    mixed_s[...] = jnp.zeros(mixed_s.shape, mixed_s.dtype)
    back_s[...] = jnp.zeros(back_s.shape, back_s.dtype)
    for group in range(group_block):
        in_group = lane_group == group
        fwd = jnp.broadcast_to(fwd_ref[pl.ds(group, 1), :], (rows, span))
        bwd = jnp.broadcast_to(bwd_ref[pl.ds(group, 1), :], (rows, span))
        fwd_band = pltpu.roll(fwd, 0, 1, stride=1, stride_axis=0).astype(jnp.bfloat16)
        bwd_band = pltpu.roll(bwd, 0, 1, stride=1, stride_axis=0).astype(jnp.bfloat16)
        cross = None
        for blk in range(block_count):
            start = blk * rows
            out_rows = pl.ds(start, rows)
            mixed = jnp.dot(fwd_band, kv_all[start : start + span], preferred_element_type=jnp.float32)
            mixed_s[out_rows, :] = jnp.where(in_group, mixed, mixed_s[out_rows, :])
            back = jnp.dot(bwd_band, gate_all[start : start + span], preferred_element_type=jnp.float32)
            back_s[out_rows, :] = jnp.where(in_group, back, back_s[out_rows, :])
            gate_rows = jnp.where(in_group, gate_all[start : start + rows], jnp.zeros((), jnp.bfloat16))
            flip_start = (block_count - 1 - blk) * rows
            part = lax.dot_general(
                gate_rows,
                kv_flipped[flip_start : flip_start + span],
                (((1,), (1,)), ((), ())),
                preferred_element_type=jnp.float32,
            )
            cross = part if cross is None else cross + part
        rolled = pltpu.roll(cross, 0, 1, stride=1, stride_axis=0)
        taps_ref[pl.ds(group, 1), :] = jnp.sum(rolled[:, span - rows :], axis=0, keepdims=True)
    back_all = back_s[...]
    grads_ref[0] = (gy_ref[...].astype(jnp.float32) * mixed_s[...]).astype(jnp.bfloat16)
    grads_ref[1] = (back_all * value_ref[...].astype(jnp.float32)).astype(jnp.bfloat16)
    grads_ref[2] = (back_all * key_ref[...].astype(jnp.float32)).astype(jnp.bfloat16)


def medium_terms(medium_taps, kv_rim, products, gate_grad, gate_rim, grad_out, key_in, value_in):
    tap_count, group_count = medium_taps.shape
    seq_rows, chan_count = products.shape
    group_width = chan_count // group_count
    row_block = tap_count
    span = row_block + tap_count
    padded_rows = seq_rows + tap_count
    group_block = LANE_BLOCK // group_width
    zero_taps = jnp.zeros((group_count, span - tap_count), jnp.float32)
    fwd_taps = jnp.concatenate([jnp.flip(medium_taps, 0).T.astype(jnp.float32), zero_taps], 1)
    bwd_taps = jnp.concatenate([medium_taps.T.astype(jnp.float32), zero_taps], 1)
    taps_spec = pl.BlockSpec((group_block, span), lambda j: (j, 0))
    rim_spec = pl.BlockSpec((kv_rim.shape[0], LANE_BLOCK), lambda j: (0, j))
    row_spec = pl.BlockSpec((seq_rows, LANE_BLOCK), lambda j: (0, j))
    grads, taps_grad = pl.pallas_call(
        medium_kernel,
        grid=(chan_count // LANE_BLOCK,),
        in_specs=[taps_spec, taps_spec, rim_spec, row_spec, row_spec, rim_spec, row_spec, row_spec, row_spec],
        out_specs=[
            pl.BlockSpec((3, seq_rows, LANE_BLOCK), lambda j: (0, 0, j)),
            pl.BlockSpec((group_block, tap_count), lambda j: (j, 0)),
        ],
        out_shape=[
            jax.ShapeDtypeStruct((3, seq_rows, chan_count), jnp.bfloat16),
            jax.ShapeDtypeStruct((group_count, tap_count), jnp.float32),
        ],
        scratch_shapes=[
            pltpu.VMEM((padded_rows, LANE_BLOCK), jnp.float32),
            pltpu.VMEM((padded_rows, LANE_BLOCK), jnp.float32),
            pltpu.VMEM((seq_rows, LANE_BLOCK), jnp.float32),
            pltpu.VMEM((seq_rows, LANE_BLOCK), jnp.float32),
        ],
    )(fwd_taps, bwd_taps, kv_rim, products, gate_grad, gate_rim, grad_out, key_in, value_in)
    return grads, taps_grad.T


def per_device(inputs, upstream, short_filter, medium_filter):
    signal = inputs[0]
    grad_out = upstream[0]
    seq_rows, chan_count = signal.shape
    tap_count = medium_filter.shape[1]
    group_count = medium_filter.shape[2]
    lag_count = short_filter.shape[1] // 3
    group_width = chan_count // group_count
    short_rim = lag_count - 1
    medium_rim = tap_count - 1
    chan_short = jnp.broadcast_to(
        short_filter[0].astype(jnp.float32).reshape(3, lag_count, group_count, 1),
        (3, lag_count, group_count, group_width),
    ).reshape(3, lag_count, chan_count)
    medium_taps = medium_filter[0]
    tap_table = chan_short.reshape(3 * lag_count, chan_count)
    signal_rim = passed_along(signal[seq_rows - short_rim :], "ctx", 1)
    signal_pad = jnp.concatenate([signal_rim, signal], 0)
    query_in, key_in, value_in, products, gate_grad = short_front(tap_table, signal_pad, grad_out)
    kv_rim, gate_rim = passed_along(products[seq_rows - medium_rim :], "ctx", 1), passed_along(
        gate_grad[:medium_rim], "ctx", -1
    )
    feature_grads, taps_grad = medium_terms(
        medium_taps, kv_rim, products, gate_grad, gate_rim, grad_out, key_in, value_in
    )
    feature_rim = passed_along(feature_grads[:, :short_rim], "ctx", -1)
    short_terms = short_partials(signal_pad, feature_grads)
    input_grad = input_grads(tap_table, feature_grads, feature_rim)
    short_grad = short_terms.reshape(3 * lag_count, group_count, group_width).sum(-1)
    short_count = short_grad.shape[0]
    local_terms = jnp.concatenate([short_grad, taps_grad], 0)
    input_grad, local_terms = lax.optimization_barrier((input_grad, local_terms))
    both_part = owned_sum(local_terms, "ctx")
    short_part = both_part[None, :short_count]
    medium_part = both_part[None, short_count:]
    incoming = passed_along(input_grad[None], "section", -1)
    return (incoming, short_part, medium_part)


def solution(mesh):
    in_specs = (
        P("section", "ctx", "dp"),
        P("section", "ctx", "dp"),
        P("section", None, "dp"),
        P("section", None, "dp"),
    )
    out_specs = (
        P("section", "ctx", "dp"),
        P("section", None, ("dp", "ctx")),
        P("section", None, ("dp", "ctx")),
    )
    return jax.shard_map(
        per_device, mesh=mesh, in_specs=in_specs, out_specs=out_specs, check_vma=False
    )
```

```python
import jax
import jax.numpy as jnp
from jax import lax
from jax.experimental import pallas as pl
from jax.experimental.pallas import tpu as pltpu
from jax.sharding import PartitionSpec as P

LANE_BLOCK = 128


def passed_along(block, axis, distance):
    devices = range(lax.axis_size(axis))
    route = [(i - distance, i) for i in devices if i - distance in devices]
    return lax.ppermute(block, axis, route)


def owned_sum(partial_terms, axis):
    axis_len = lax.axis_size(axis)
    row_count, col_count = partial_terms.shape
    width = col_count // axis_len
    chunks = partial_terms.reshape(row_count, axis_len, width).transpose(1, 0, 2)
    return jnp.sum(lax.all_to_all(chunks, axis, 0, 0, tiled=False), axis=0)


def front_kernel(taps_ref, sig_ref, gy_ref, q_ref, k_ref, v_ref, kv_ref, gate_ref, xs_ref):
    rows = q_ref.shape[0]
    rim = sig_ref.shape[0] - rows
    lags = rim + 1
    xs_ref[pl.ds(0, rows + rim), :] = sig_ref[...].astype(jnp.float32)
    for branch, out_ref in enumerate((q_ref, k_ref, v_ref)):
        acc = None
        for offset in range(lags):
            term = taps_ref[pl.ds(branch * lags + offset, 1), :] * xs_ref[pl.ds(rim - offset, rows), :]
            acc = term if acc is None else acc + term
        out_ref[...] = acc.astype(jnp.bfloat16)
    kv_ref[...] = (k_ref[...].astype(jnp.float32) * v_ref[...].astype(jnp.float32)).astype(
        jnp.bfloat16
    )
    gate_ref[...] = (gy_ref[...].astype(jnp.float32) * q_ref[...].astype(jnp.float32)).astype(
        jnp.bfloat16
    )


def short_front(taps, signal_pad, grad_out):
    padded_rows, chan_count = signal_pad.shape
    rows = grad_out.shape[0]
    tap_rows = taps.shape[0]
    row_spec = pl.BlockSpec((rows, LANE_BLOCK), lambda j: (0, j))
    shape = jax.ShapeDtypeStruct((rows, chan_count), jnp.bfloat16)
    return pl.pallas_call(
        front_kernel,
        grid=(chan_count // LANE_BLOCK,),
        in_specs=[
            pl.BlockSpec((tap_rows, LANE_BLOCK), lambda j: (0, j)),
            pl.BlockSpec((padded_rows, LANE_BLOCK), lambda j: (0, j)),
            row_spec,
        ],
        out_specs=[row_spec] * 5,
        out_shape=[shape] * 5,
        scratch_shapes=[pltpu.VMEM((padded_rows + 8, LANE_BLOCK), jnp.float32)],
    )(taps, signal_pad, grad_out)


def input_grad_kernel(taps_ref, grads_ref, rim_ref, ig_ref, gs_ref):
    branches, rows, lanes = grads_ref.shape
    rim = rim_ref.shape[1]
    lags = rim + 1
    for branch in range(branches):
        gs_ref[branch, pl.ds(0, rows), :] = grads_ref[branch].astype(jnp.float32)
        gs_ref[branch, pl.ds(rows, rim), :] = rim_ref[branch].astype(jnp.float32)
    acc = None
    for branch in range(branches):
        for offset in range(lags):
            term = taps_ref[pl.ds(branch * lags + offset, 1), :] * gs_ref[branch, pl.ds(offset, rows), :]
            acc = term if acc is None else acc + term
    ig_ref[...] = acc.astype(jnp.bfloat16)


def short_partial_kernel(sig_ref, grads_ref, sp_ref, xs_ref):
    branches, rows, lanes = grads_ref.shape
    rim = sig_ref.shape[0] - rows
    lags = rim + 1
    xs_ref[pl.ds(0, rows + rim), :] = sig_ref[...].astype(jnp.float32)
    for branch in range(branches):
        grads_f = grads_ref[branch].astype(jnp.float32)
        for offset in range(lags):
            prod = grads_f * xs_ref[pl.ds(rim - offset, rows), :]
            sp_ref[pl.ds(branch * lags + offset, 1), :] = jnp.sum(prod, axis=0, keepdims=True)


def short_partials(signal_pad, feature_grads):
    padded_rows, chan_count = signal_pad.shape
    branches, rows, _ = feature_grads.shape
    tap_rows = branches * (padded_rows - rows + 1)
    return pl.pallas_call(
        short_partial_kernel,
        grid=(chan_count // LANE_BLOCK,),
        in_specs=[
            pl.BlockSpec((padded_rows, LANE_BLOCK), lambda j: (0, j)),
            pl.BlockSpec((branches, rows, LANE_BLOCK), lambda j: (0, 0, j)),
        ],
        out_specs=pl.BlockSpec((tap_rows, LANE_BLOCK), lambda j: (0, j)),
        out_shape=jax.ShapeDtypeStruct((tap_rows, chan_count), jnp.float32),
        scratch_shapes=[pltpu.VMEM((padded_rows + 8, LANE_BLOCK), jnp.float32)],
    )(signal_pad, feature_grads)


def input_grads(taps, feature_grads, feature_rim):
    branches, rows, chan_count = feature_grads.shape
    rim = feature_rim.shape[1]
    return pl.pallas_call(
        input_grad_kernel,
        grid=(chan_count // LANE_BLOCK,),
        in_specs=[
            pl.BlockSpec((taps.shape[0], LANE_BLOCK), lambda j: (0, j)),
            pl.BlockSpec((branches, rows, LANE_BLOCK), lambda j: (0, 0, j)),
            pl.BlockSpec((branches, rim, LANE_BLOCK), lambda j: (0, 0, j)),
        ],
        out_specs=pl.BlockSpec((rows, LANE_BLOCK), lambda j: (0, j)),
        out_shape=jax.ShapeDtypeStruct((rows, chan_count), jnp.bfloat16),
        scratch_shapes=[pltpu.VMEM((branches, rows + rim + 2, LANE_BLOCK), jnp.float32)],
    )(taps, feature_grads, feature_rim)


def medium_kernel(
    fwd_ref, bwd_ref, kv_rim_ref, prod_ref, gate_ref, gate_rim_ref, gy_ref, key_ref, value_ref,
    grads_ref, taps_ref, kv_s, gate_s, mixed_s, back_s,
):
    group_block, span = fwd_ref.shape
    rows = taps_ref.shape[1]
    seq_rows, lanes = gy_ref.shape
    block_count = seq_rows // rows
    rim = kv_rim_ref.shape[0]
    padded_rows = kv_s.shape[0]
    kv_s[pl.ds(0, rim), :] = kv_rim_ref[...].astype(jnp.float32)
    kv_s[pl.ds(rim, seq_rows), :] = prod_ref[...].astype(jnp.float32)
    kv_s[pl.ds(rim + seq_rows, padded_rows - rim - seq_rows), :] = jnp.zeros(
        (padded_rows - rim - seq_rows, lanes), jnp.float32
    )
    gate_s[pl.ds(0, seq_rows), :] = gate_ref[...].astype(jnp.float32)
    gate_s[pl.ds(seq_rows, rim), :] = gate_rim_ref[...].astype(jnp.float32)
    gate_s[pl.ds(rim + seq_rows, padded_rows - rim - seq_rows), :] = jnp.zeros(
        (padded_rows - rim - seq_rows, lanes), jnp.float32
    )
    kv_all = kv_s[...].astype(jnp.bfloat16)
    gate_all = gate_s[...].astype(jnp.bfloat16)
    row_id = lax.broadcasted_iota(jnp.int32, (padded_rows, padded_rows), 0)
    col_id = lax.broadcasted_iota(jnp.int32, (padded_rows, padded_rows), 1)
    reversal = (row_id + col_id == padded_rows - 1).astype(jnp.bfloat16)
    kv_flipped = jnp.dot(reversal, kv_all, preferred_element_type=jnp.float32).astype(jnp.bfloat16)
    group_width = lanes // group_block
    lane_group = lax.broadcasted_iota(jnp.int32, (1, lanes), 1) // group_width
    mixed_s[...] = jnp.zeros(mixed_s.shape, mixed_s.dtype)
    back_s[...] = jnp.zeros(back_s.shape, back_s.dtype)
    for group in range(group_block):
        in_group = lane_group == group
        fwd = jnp.broadcast_to(fwd_ref[pl.ds(group, 1), :], (rows, span))
        bwd = jnp.broadcast_to(bwd_ref[pl.ds(group, 1), :], (rows, span))
        fwd_band = pltpu.roll(fwd, 0, 1, stride=1, stride_axis=0).astype(jnp.bfloat16)
        bwd_band = pltpu.roll(bwd, 0, 1, stride=1, stride_axis=0).astype(jnp.bfloat16)
        cross = None
        for blk in range(block_count):
            start = blk * rows
            out_rows = pl.ds(start, rows)
            mixed = jnp.dot(fwd_band, kv_all[start : start + span], preferred_element_type=jnp.float32)
            mixed_s[out_rows, :] = jnp.where(in_group, mixed, mixed_s[out_rows, :])
            back = jnp.dot(bwd_band, gate_all[start : start + span], preferred_element_type=jnp.float32)
            back_s[out_rows, :] = jnp.where(in_group, back, back_s[out_rows, :])
            gate_rows = jnp.where(in_group, gate_all[start : start + rows], jnp.zeros((), jnp.bfloat16))
            flip_start = (block_count - 1 - blk) * rows
            part = lax.dot_general(
                gate_rows,
                kv_flipped[flip_start : flip_start + span],
                (((1,), (1,)), ((), ())),
                preferred_element_type=jnp.float32,
            )
            cross = part if cross is None else cross + part
        rolled = pltpu.roll(cross, 0, 1, stride=1, stride_axis=0)
        taps_ref[pl.ds(group, 1), :] = jnp.sum(rolled[:, span - rows :], axis=0, keepdims=True)
    back_all = back_s[...]
    grads_ref[0] = (gy_ref[...].astype(jnp.float32) * mixed_s[...]).astype(jnp.bfloat16)
    grads_ref[1] = (back_all * value_ref[...].astype(jnp.float32)).astype(jnp.bfloat16)
    grads_ref[2] = (back_all * key_ref[...].astype(jnp.float32)).astype(jnp.bfloat16)


def medium_terms(medium_taps, kv_rim, products, gate_grad, gate_rim, grad_out, key_in, value_in):
    tap_count, group_count = medium_taps.shape
    seq_rows, chan_count = products.shape
    group_width = chan_count // group_count
    row_block = tap_count
    span = row_block + tap_count
    padded_rows = seq_rows + tap_count
    group_block = LANE_BLOCK // group_width
    zero_taps = jnp.zeros((group_count, span - tap_count), jnp.float32)
    fwd_taps = jnp.concatenate([jnp.flip(medium_taps, 0).T.astype(jnp.float32), zero_taps], 1)
    bwd_taps = jnp.concatenate([medium_taps.T.astype(jnp.float32), zero_taps], 1)
    taps_spec = pl.BlockSpec((group_block, span), lambda j: (j, 0))
    rim_spec = pl.BlockSpec((kv_rim.shape[0], LANE_BLOCK), lambda j: (0, j))
    row_spec = pl.BlockSpec((seq_rows, LANE_BLOCK), lambda j: (0, j))
    grads, taps_grad = pl.pallas_call(
        medium_kernel,
        grid=(chan_count // LANE_BLOCK,),
        in_specs=[taps_spec, taps_spec, rim_spec, row_spec, row_spec, rim_spec, row_spec, row_spec, row_spec],
        out_specs=[
            pl.BlockSpec((3, seq_rows, LANE_BLOCK), lambda j: (0, 0, j)),
            pl.BlockSpec((group_block, tap_count), lambda j: (j, 0)),
        ],
        out_shape=[
            jax.ShapeDtypeStruct((3, seq_rows, chan_count), jnp.bfloat16),
            jax.ShapeDtypeStruct((group_count, tap_count), jnp.float32),
        ],
        scratch_shapes=[
            pltpu.VMEM((padded_rows, LANE_BLOCK), jnp.float32),
            pltpu.VMEM((padded_rows, LANE_BLOCK), jnp.float32),
            pltpu.VMEM((seq_rows, LANE_BLOCK), jnp.float32),
            pltpu.VMEM((seq_rows, LANE_BLOCK), jnp.float32),
        ],
    )(fwd_taps, bwd_taps, kv_rim, products, gate_grad, gate_rim, grad_out, key_in, value_in)
    return grads, taps_grad.T


def per_device(inputs, upstream, short_filter, medium_filter):
    signal = inputs[0]
    grad_out = upstream[0]
    seq_rows, chan_count = signal.shape
    tap_count = medium_filter.shape[1]
    group_count = medium_filter.shape[2]
    lag_count = short_filter.shape[1] // 3
    group_width = chan_count // group_count
    short_rim = lag_count - 1
    medium_rim = tap_count - 1
    chan_short = jnp.broadcast_to(
        short_filter[0].astype(jnp.float32).reshape(3, lag_count, group_count, 1),
        (3, lag_count, group_count, group_width),
    ).reshape(3, lag_count, chan_count)
    medium_taps = medium_filter[0]
    tap_table = chan_short.reshape(3 * lag_count, chan_count)
    prev_rows = passed_along(signal[seq_rows - medium_rim - short_rim :], "ctx", 1)
    next_rows, next_grad = passed_along(
        (signal[:medium_rim], grad_out[:medium_rim]), "ctx", -1
    )
    signal_rim = passed_along(signal[seq_rows - short_rim :], "ctx", 1)
    signal_pad = jnp.concatenate([signal_rim, signal], 0)
    query_in, key_in, value_in, products, gate_grad = short_front(tap_table, signal_pad, grad_out)
    kv_rim = short_front(tap_table, prev_rows, jnp.zeros_like(next_grad))[3]
    next_pad = jnp.concatenate([signal[seq_rows - short_rim :], next_rows], 0)
    gate_rim = short_front(tap_table, next_pad, next_grad)[4]
    feature_grads, taps_grad = medium_terms(
        medium_taps, kv_rim, products, gate_grad, gate_rim, grad_out, key_in, value_in
    )
    feature_rim = passed_along(feature_grads[:, :short_rim], "ctx", -1)
    short_terms = short_partials(signal_pad, feature_grads)
    input_grad = input_grads(tap_table, feature_grads, feature_rim)
    short_grad = short_terms.reshape(3 * lag_count, group_count, group_width).sum(-1)
    short_count = short_grad.shape[0]
    both_part = owned_sum(jnp.concatenate([short_grad, taps_grad], 0), "ctx")
    short_part = both_part[None, :short_count]
    medium_part = both_part[None, short_count:]
    incoming = passed_along(input_grad[None], "section", -1)
    return (incoming, short_part, medium_part)


def solution(mesh):
    in_specs = (
        P("section", "ctx", "dp"),
        P("section", "ctx", "dp"),
        P("section", None, "dp"),
        P("section", None, "dp"),
    )
    out_specs = (
        P("section", "ctx", "dp"),
        P("section", None, ("dp", "ctx")),
        P("section", None, ("dp", "ctx")),
    )
    return jax.shard_map(
        per_device, mesh=mesh, in_specs=in_specs, out_specs=out_specs, check_vma=False
    )
```

```python
import jax
import jax.numpy as jnp
from jax import lax
from jax.experimental import pallas as pl
from jax.experimental.pallas import tpu as pltpu
from jax.sharding import PartitionSpec as P

LANE_BLOCK = 128
SHORT_BLOCK = 256


def passed_along(block, axis, distance):
    devices = range(lax.axis_size(axis))
    route = [(i - distance, i) for i in devices if i - distance in devices]
    return lax.ppermute(block, axis, route)


def owned_sum(partial_terms, axis):
    axis_len = lax.axis_size(axis)
    row_count, col_count = partial_terms.shape
    width = col_count // axis_len
    chunks = partial_terms.reshape(row_count, axis_len, width).transpose(1, 0, 2)
    return jnp.sum(lax.all_to_all(chunks, axis, 0, 0, tiled=False), axis=0)


def front_kernel(taps_ref, sig_ref, gy_ref, q_ref, k_ref, v_ref, kv_ref, gate_ref, xs_ref):
    rows = q_ref.shape[0]
    rim = sig_ref.shape[0] - rows
    lags = rim + 1
    xs_ref[pl.ds(0, rows + rim), :] = sig_ref[...].astype(jnp.float32)
    for branch, out_ref in enumerate((q_ref, k_ref, v_ref)):
        acc = None
        for offset in range(lags):
            term = taps_ref[pl.ds(branch * lags + offset, 1), :] * xs_ref[pl.ds(rim - offset, rows), :]
            acc = term if acc is None else acc + term
        out_ref[...] = acc.astype(jnp.bfloat16)
    kv_ref[...] = (k_ref[...].astype(jnp.float32) * v_ref[...].astype(jnp.float32)).astype(
        jnp.bfloat16
    )
    gate_ref[...] = (gy_ref[...].astype(jnp.float32) * q_ref[...].astype(jnp.float32)).astype(
        jnp.bfloat16
    )


def short_front(taps, signal_pad, grad_out):
    padded_rows, chan_count = signal_pad.shape
    rows = grad_out.shape[0]
    tap_rows = taps.shape[0]
    row_spec = pl.BlockSpec((rows, SHORT_BLOCK), lambda j: (0, j))
    shape = jax.ShapeDtypeStruct((rows, chan_count), jnp.bfloat16)
    return pl.pallas_call(
        front_kernel,
        grid=(chan_count // SHORT_BLOCK,),
        in_specs=[
            pl.BlockSpec((tap_rows, SHORT_BLOCK), lambda j: (0, j)),
            pl.BlockSpec((padded_rows, SHORT_BLOCK), lambda j: (0, j)),
            row_spec,
        ],
        out_specs=[row_spec] * 5,
        out_shape=[shape] * 5,
        scratch_shapes=[pltpu.VMEM((padded_rows + 8, SHORT_BLOCK), jnp.float32)],
    )(taps, signal_pad, grad_out)


def input_grad_kernel(taps_ref, grads_ref, rim_ref, ig_ref, gs_ref):
    branches, rows, lanes = grads_ref.shape
    rim = rim_ref.shape[1]
    lags = rim + 1
    for branch in range(branches):
        gs_ref[branch, pl.ds(0, rows), :] = grads_ref[branch].astype(jnp.float32)
        gs_ref[branch, pl.ds(rows, rim), :] = rim_ref[branch].astype(jnp.float32)
    acc = None
    for branch in range(branches):
        for offset in range(lags):
            term = taps_ref[pl.ds(branch * lags + offset, 1), :] * gs_ref[branch, pl.ds(offset, rows), :]
            acc = term if acc is None else acc + term
    ig_ref[...] = acc.astype(jnp.bfloat16)


def short_partial_kernel(sig_ref, grads_ref, sp_ref, xs_ref):
    branches, rows, lanes = grads_ref.shape
    rim = sig_ref.shape[0] - rows
    lags = rim + 1
    xs_ref[pl.ds(0, rows + rim), :] = sig_ref[...].astype(jnp.float32)
    for branch in range(branches):
        grads_f = grads_ref[branch].astype(jnp.float32)
        for offset in range(lags):
            prod = grads_f * xs_ref[pl.ds(rim - offset, rows), :]
            sp_ref[pl.ds(branch * lags + offset, 1), :] = jnp.sum(prod, axis=0, keepdims=True)


def short_partials(signal_pad, feature_grads):
    padded_rows, chan_count = signal_pad.shape
    branches, rows, _ = feature_grads.shape
    tap_rows = branches * (padded_rows - rows + 1)
    return pl.pallas_call(
        short_partial_kernel,
        grid=(chan_count // SHORT_BLOCK,),
        in_specs=[
            pl.BlockSpec((padded_rows, SHORT_BLOCK), lambda j: (0, j)),
            pl.BlockSpec((branches, rows, SHORT_BLOCK), lambda j: (0, 0, j)),
        ],
        out_specs=pl.BlockSpec((tap_rows, SHORT_BLOCK), lambda j: (0, j)),
        out_shape=jax.ShapeDtypeStruct((tap_rows, chan_count), jnp.float32),
        scratch_shapes=[pltpu.VMEM((padded_rows + 8, SHORT_BLOCK), jnp.float32)],
    )(signal_pad, feature_grads)


def input_grads(taps, feature_grads, feature_rim):
    branches, rows, chan_count = feature_grads.shape
    rim = feature_rim.shape[1]
    return pl.pallas_call(
        input_grad_kernel,
        grid=(chan_count // SHORT_BLOCK,),
        in_specs=[
            pl.BlockSpec((taps.shape[0], SHORT_BLOCK), lambda j: (0, j)),
            pl.BlockSpec((branches, rows, SHORT_BLOCK), lambda j: (0, 0, j)),
            pl.BlockSpec((branches, rim, SHORT_BLOCK), lambda j: (0, 0, j)),
        ],
        out_specs=pl.BlockSpec((rows, SHORT_BLOCK), lambda j: (0, j)),
        out_shape=jax.ShapeDtypeStruct((rows, chan_count), jnp.bfloat16),
        scratch_shapes=[pltpu.VMEM((branches, rows + rim + 2, SHORT_BLOCK), jnp.float32)],
    )(taps, feature_grads, feature_rim)


def medium_kernel(
    fwd_ref, bwd_ref, kv_rim_ref, prod_ref, gate_ref, gate_rim_ref, gy_ref, key_ref, value_ref,
    grads_ref, taps_ref, kv_s, gate_s, mixed_s, back_s,
):
    group_block, span = fwd_ref.shape
    rows = taps_ref.shape[1]
    seq_rows, lanes = gy_ref.shape
    block_count = seq_rows // rows
    rim = kv_rim_ref.shape[0]
    padded_rows = kv_s.shape[0]
    kv_s[pl.ds(0, rim), :] = kv_rim_ref[...].astype(jnp.float32)
    kv_s[pl.ds(rim, seq_rows), :] = prod_ref[...].astype(jnp.float32)
    kv_s[pl.ds(rim + seq_rows, padded_rows - rim - seq_rows), :] = jnp.zeros(
        (padded_rows - rim - seq_rows, lanes), jnp.float32
    )
    gate_s[pl.ds(0, seq_rows), :] = gate_ref[...].astype(jnp.float32)
    gate_s[pl.ds(seq_rows, rim), :] = gate_rim_ref[...].astype(jnp.float32)
    gate_s[pl.ds(rim + seq_rows, padded_rows - rim - seq_rows), :] = jnp.zeros(
        (padded_rows - rim - seq_rows, lanes), jnp.float32
    )
    kv_all = kv_s[...].astype(jnp.bfloat16)
    gate_all = gate_s[...].astype(jnp.bfloat16)
    row_id = lax.broadcasted_iota(jnp.int32, (padded_rows, padded_rows), 0)
    col_id = lax.broadcasted_iota(jnp.int32, (padded_rows, padded_rows), 1)
    reversal = (row_id + col_id == padded_rows - 1).astype(jnp.bfloat16)
    kv_flipped = jnp.dot(reversal, kv_all, preferred_element_type=jnp.float32).astype(jnp.bfloat16)
    group_width = lanes // group_block
    lane_group = lax.broadcasted_iota(jnp.int32, (1, lanes), 1) // group_width
    mixed_s[...] = jnp.zeros(mixed_s.shape, mixed_s.dtype)
    back_s[...] = jnp.zeros(back_s.shape, back_s.dtype)
    for group in range(group_block):
        in_group = lane_group == group
        fwd = jnp.broadcast_to(fwd_ref[pl.ds(group, 1), :], (rows, span))
        bwd = jnp.broadcast_to(bwd_ref[pl.ds(group, 1), :], (rows, span))
        fwd_band = pltpu.roll(fwd, 0, 1, stride=1, stride_axis=0).astype(jnp.bfloat16)
        bwd_band = pltpu.roll(bwd, 0, 1, stride=1, stride_axis=0).astype(jnp.bfloat16)
        cross = None
        for blk in range(block_count):
            start = blk * rows
            out_rows = pl.ds(start, rows)
            mixed = jnp.dot(fwd_band, kv_all[start : start + span], preferred_element_type=jnp.float32)
            mixed_s[out_rows, :] = jnp.where(in_group, mixed, mixed_s[out_rows, :])
            back = jnp.dot(bwd_band, gate_all[start : start + span], preferred_element_type=jnp.float32)
            back_s[out_rows, :] = jnp.where(in_group, back, back_s[out_rows, :])
            gate_rows = jnp.where(in_group, gate_all[start : start + rows], jnp.zeros((), jnp.bfloat16))
            flip_start = (block_count - 1 - blk) * rows
            part = lax.dot_general(
                gate_rows,
                kv_flipped[flip_start : flip_start + span],
                (((1,), (1,)), ((), ())),
                preferred_element_type=jnp.float32,
            )
            cross = part if cross is None else cross + part
        rolled = pltpu.roll(cross, 0, 1, stride=1, stride_axis=0)
        taps_ref[pl.ds(group, 1), :] = jnp.sum(rolled[:, span - rows :], axis=0, keepdims=True)
    back_all = back_s[...]
    grads_ref[0] = (gy_ref[...].astype(jnp.float32) * mixed_s[...]).astype(jnp.bfloat16)
    grads_ref[1] = (back_all * value_ref[...].astype(jnp.float32)).astype(jnp.bfloat16)
    grads_ref[2] = (back_all * key_ref[...].astype(jnp.float32)).astype(jnp.bfloat16)


def medium_terms(medium_taps, kv_rim, products, gate_grad, gate_rim, grad_out, key_in, value_in):
    tap_count, group_count = medium_taps.shape
    seq_rows, chan_count = products.shape
    group_width = chan_count // group_count
    row_block = tap_count
    span = row_block + tap_count
    padded_rows = seq_rows + tap_count
    group_block = LANE_BLOCK // group_width
    zero_taps = jnp.zeros((group_count, span - tap_count), jnp.float32)
    fwd_taps = jnp.concatenate([jnp.flip(medium_taps, 0).T.astype(jnp.float32), zero_taps], 1)
    bwd_taps = jnp.concatenate([medium_taps.T.astype(jnp.float32), zero_taps], 1)
    taps_spec = pl.BlockSpec((group_block, span), lambda j: (j, 0))
    rim_spec = pl.BlockSpec((kv_rim.shape[0], LANE_BLOCK), lambda j: (0, j))
    row_spec = pl.BlockSpec((seq_rows, LANE_BLOCK), lambda j: (0, j))
    grads, taps_grad = pl.pallas_call(
        medium_kernel,
        grid=(chan_count // LANE_BLOCK,),
        in_specs=[taps_spec, taps_spec, rim_spec, row_spec, row_spec, rim_spec, row_spec, row_spec, row_spec],
        out_specs=[
            pl.BlockSpec((3, seq_rows, LANE_BLOCK), lambda j: (0, 0, j)),
            pl.BlockSpec((group_block, tap_count), lambda j: (j, 0)),
        ],
        out_shape=[
            jax.ShapeDtypeStruct((3, seq_rows, chan_count), jnp.bfloat16),
            jax.ShapeDtypeStruct((group_count, tap_count), jnp.float32),
        ],
        scratch_shapes=[
            pltpu.VMEM((padded_rows, LANE_BLOCK), jnp.float32),
            pltpu.VMEM((padded_rows, LANE_BLOCK), jnp.float32),
            pltpu.VMEM((seq_rows, LANE_BLOCK), jnp.float32),
            pltpu.VMEM((seq_rows, LANE_BLOCK), jnp.float32),
        ],
    )(fwd_taps, bwd_taps, kv_rim, products, gate_grad, gate_rim, grad_out, key_in, value_in)
    return grads, taps_grad.T


def per_device(inputs, upstream, short_filter, medium_filter):
    signal = inputs[0]
    grad_out = upstream[0]
    seq_rows, chan_count = signal.shape
    tap_count = medium_filter.shape[1]
    group_count = medium_filter.shape[2]
    lag_count = short_filter.shape[1] // 3
    group_width = chan_count // group_count
    short_rim = lag_count - 1
    medium_rim = tap_count - 1
    chan_short = jnp.broadcast_to(
        short_filter[0].astype(jnp.float32).reshape(3, lag_count, group_count, 1),
        (3, lag_count, group_count, group_width),
    ).reshape(3, lag_count, chan_count)
    medium_taps = medium_filter[0]
    tap_table = chan_short.reshape(3 * lag_count, chan_count)
    signal_rim = passed_along(signal[seq_rows - short_rim :], "ctx", 1)
    signal_pad = jnp.concatenate([signal_rim, signal], 0)
    query_in, key_in, value_in, products, gate_grad = short_front(tap_table, signal_pad, grad_out)
    kv_rim, gate_rim = passed_along(products[seq_rows - medium_rim :], "ctx", 1), passed_along(
        gate_grad[:medium_rim], "ctx", -1
    )
    feature_grads, taps_grad = medium_terms(
        medium_taps, kv_rim, products, gate_grad, gate_rim, grad_out, key_in, value_in
    )
    feature_rim = passed_along(feature_grads[:, :short_rim], "ctx", -1)
    short_terms = short_partials(signal_pad, feature_grads)
    input_grad = input_grads(tap_table, feature_grads, feature_rim)
    short_grad = short_terms.reshape(3 * lag_count, group_count, group_width).sum(-1)
    short_count = short_grad.shape[0]
    both_part = owned_sum(jnp.concatenate([short_grad, taps_grad], 0), "ctx")
    short_part = both_part[None, :short_count]
    medium_part = both_part[None, short_count:]
    incoming = passed_along(input_grad[None], "section", -1)
    return (incoming, short_part, medium_part)


def solution(mesh):
    in_specs = (
        P("section", "ctx", "dp"),
        P("section", "ctx", "dp"),
        P("section", None, "dp"),
        P("section", None, "dp"),
    )
    out_specs = (
        P("section", "ctx", "dp"),
        P("section", None, ("dp", "ctx")),
        P("section", None, ("dp", "ctx")),
    )
    return jax.shard_map(
        per_device, mesh=mesh, in_specs=in_specs, out_specs=out_specs, check_vma=False
    )
```

```python
import jax
import jax.numpy as jnp
from jax import lax
from jax.experimental import pallas as pl
from jax.experimental.pallas import tpu as pltpu
from jax.sharding import PartitionSpec as P

LANE_BLOCK = 128
SHORT_BLOCK = 256


def passed_along(block, axis, distance):
    devices = range(lax.axis_size(axis))
    route = [(i - distance, i) for i in devices if i - distance in devices]
    return lax.ppermute(block, axis, route)


def owned_sum(partial_terms, axis):
    axis_len = lax.axis_size(axis)
    row_count, col_count = partial_terms.shape
    width = col_count // axis_len
    chunks = partial_terms.reshape(row_count, axis_len, width).transpose(1, 0, 2)
    return jnp.sum(lax.all_to_all(chunks, axis, 0, 0, tiled=False), axis=0)


def front_kernel(taps_ref, sig_ref, gy_ref, q_ref, k_ref, v_ref, kv_ref, gate_ref, xs_ref):
    rows = q_ref.shape[0]
    rim = sig_ref.shape[0] - rows
    lags = rim + 1
    xs_ref[pl.ds(0, rows + rim), :] = sig_ref[...].astype(jnp.float32)
    accs = [None, None, None]
    for offset in range(lags):
        window = xs_ref[pl.ds(rim - offset, rows), :]
        for branch in range(3):
            term = taps_ref[pl.ds(branch * lags + offset, 1), :] * window
            accs[branch] = term if accs[branch] is None else accs[branch] + term
    for acc, out_ref in zip(accs, (q_ref, k_ref, v_ref)):
        out_ref[...] = acc.astype(jnp.bfloat16)
    kv_ref[...] = (k_ref[...].astype(jnp.float32) * v_ref[...].astype(jnp.float32)).astype(
        jnp.bfloat16
    )
    gate_ref[...] = (gy_ref[...].astype(jnp.float32) * q_ref[...].astype(jnp.float32)).astype(
        jnp.bfloat16
    )


def short_front(taps, signal_pad, grad_out):
    padded_rows, chan_count = signal_pad.shape
    rows = grad_out.shape[0]
    tap_rows = taps.shape[0]
    row_spec = pl.BlockSpec((rows, SHORT_BLOCK), lambda j: (0, j))
    shape = jax.ShapeDtypeStruct((rows, chan_count), jnp.bfloat16)
    return pl.pallas_call(
        front_kernel,
        grid=(chan_count // SHORT_BLOCK,),
        in_specs=[
            pl.BlockSpec((tap_rows, SHORT_BLOCK), lambda j: (0, j)),
            pl.BlockSpec((padded_rows, SHORT_BLOCK), lambda j: (0, j)),
            row_spec,
        ],
        out_specs=[row_spec] * 5,
        out_shape=[shape] * 5,
        scratch_shapes=[pltpu.VMEM((padded_rows + 8, SHORT_BLOCK), jnp.float32)],
    )(taps, signal_pad, grad_out)


def input_grad_kernel(taps_ref, grads_ref, rim_ref, ig_ref, gs_ref):
    branches, rows, lanes = grads_ref.shape
    rim = rim_ref.shape[1]
    lags = rim + 1
    for branch in range(branches):
        gs_ref[branch, pl.ds(0, rows), :] = grads_ref[branch].astype(jnp.float32)
        gs_ref[branch, pl.ds(rows, rim), :] = rim_ref[branch].astype(jnp.float32)
    acc = None
    for branch in range(branches):
        for offset in range(lags):
            term = taps_ref[pl.ds(branch * lags + offset, 1), :] * gs_ref[branch, pl.ds(offset, rows), :]
            acc = term if acc is None else acc + term
    ig_ref[...] = acc.astype(jnp.bfloat16)


def short_partial_kernel(sig_ref, grads_ref, sp_ref, xs_ref):
    branches, rows, lanes = grads_ref.shape
    rim = sig_ref.shape[0] - rows
    lags = rim + 1
    xs_ref[pl.ds(0, rows + rim), :] = sig_ref[...].astype(jnp.float32)
    for branch in range(branches):
        grads_f = grads_ref[branch].astype(jnp.float32)
        for offset in range(lags):
            prod = grads_f * xs_ref[pl.ds(rim - offset, rows), :]
            sp_ref[pl.ds(branch * lags + offset, 1), :] = jnp.sum(prod, axis=0, keepdims=True)


def short_partials(signal_pad, feature_grads):
    padded_rows, chan_count = signal_pad.shape
    branches, rows, _ = feature_grads.shape
    tap_rows = branches * (padded_rows - rows + 1)
    return pl.pallas_call(
        short_partial_kernel,
        grid=(chan_count // SHORT_BLOCK,),
        in_specs=[
            pl.BlockSpec((padded_rows, SHORT_BLOCK), lambda j: (0, j)),
            pl.BlockSpec((branches, rows, SHORT_BLOCK), lambda j: (0, 0, j)),
        ],
        out_specs=pl.BlockSpec((tap_rows, SHORT_BLOCK), lambda j: (0, j)),
        out_shape=jax.ShapeDtypeStruct((tap_rows, chan_count), jnp.float32),
        scratch_shapes=[pltpu.VMEM((padded_rows + 8, SHORT_BLOCK), jnp.float32)],
    )(signal_pad, feature_grads)


def input_grads(taps, feature_grads, feature_rim):
    branches, rows, chan_count = feature_grads.shape
    rim = feature_rim.shape[1]
    return pl.pallas_call(
        input_grad_kernel,
        grid=(chan_count // SHORT_BLOCK,),
        in_specs=[
            pl.BlockSpec((taps.shape[0], SHORT_BLOCK), lambda j: (0, j)),
            pl.BlockSpec((branches, rows, SHORT_BLOCK), lambda j: (0, 0, j)),
            pl.BlockSpec((branches, rim, SHORT_BLOCK), lambda j: (0, 0, j)),
        ],
        out_specs=pl.BlockSpec((rows, SHORT_BLOCK), lambda j: (0, j)),
        out_shape=jax.ShapeDtypeStruct((rows, chan_count), jnp.bfloat16),
        scratch_shapes=[pltpu.VMEM((branches, rows + rim + 2, SHORT_BLOCK), jnp.float32)],
    )(taps, feature_grads, feature_rim)


def medium_kernel(
    fwd_ref, bwd_ref, kv_rim_ref, prod_ref, gate_ref, gate_rim_ref, gy_ref, key_ref, value_ref,
    grads_ref, taps_ref, kv_s, gate_s, mixed_s, back_s,
):
    group_block, span = fwd_ref.shape
    rows = taps_ref.shape[1]
    seq_rows, lanes = gy_ref.shape
    block_count = seq_rows // rows
    rim = kv_rim_ref.shape[0]
    padded_rows = kv_s.shape[0]
    kv_s[pl.ds(0, rim), :] = kv_rim_ref[...].astype(jnp.float32)
    kv_s[pl.ds(rim, seq_rows), :] = prod_ref[...].astype(jnp.float32)
    kv_s[pl.ds(rim + seq_rows, padded_rows - rim - seq_rows), :] = jnp.zeros(
        (padded_rows - rim - seq_rows, lanes), jnp.float32
    )
    gate_s[pl.ds(0, seq_rows), :] = gate_ref[...].astype(jnp.float32)
    gate_s[pl.ds(seq_rows, rim), :] = gate_rim_ref[...].astype(jnp.float32)
    gate_s[pl.ds(rim + seq_rows, padded_rows - rim - seq_rows), :] = jnp.zeros(
        (padded_rows - rim - seq_rows, lanes), jnp.float32
    )
    kv_all = kv_s[...].astype(jnp.bfloat16)
    gate_all = gate_s[...].astype(jnp.bfloat16)
    row_id = lax.broadcasted_iota(jnp.int32, (padded_rows, padded_rows), 0)
    col_id = lax.broadcasted_iota(jnp.int32, (padded_rows, padded_rows), 1)
    reversal = (row_id + col_id == padded_rows - 1).astype(jnp.bfloat16)
    kv_flipped = jnp.dot(reversal, kv_all, preferred_element_type=jnp.float32).astype(jnp.bfloat16)
    group_width = lanes // group_block
    lane_group = lax.broadcasted_iota(jnp.int32, (1, lanes), 1) // group_width
    mixed_s[...] = jnp.zeros(mixed_s.shape, mixed_s.dtype)
    back_s[...] = jnp.zeros(back_s.shape, back_s.dtype)
    for group in range(group_block):
        in_group = lane_group == group
        fwd = jnp.broadcast_to(fwd_ref[pl.ds(group, 1), :], (rows, span))
        bwd = jnp.broadcast_to(bwd_ref[pl.ds(group, 1), :], (rows, span))
        fwd_band = pltpu.roll(fwd, 0, 1, stride=1, stride_axis=0).astype(jnp.bfloat16)
        bwd_band = pltpu.roll(bwd, 0, 1, stride=1, stride_axis=0).astype(jnp.bfloat16)
        cross = None
        for blk in range(block_count):
            start = blk * rows
            out_rows = pl.ds(start, rows)
            mixed = jnp.dot(fwd_band, kv_all[start : start + span], preferred_element_type=jnp.float32)
            mixed_s[out_rows, :] = jnp.where(in_group, mixed, mixed_s[out_rows, :])
            back = jnp.dot(bwd_band, gate_all[start : start + span], preferred_element_type=jnp.float32)
            back_s[out_rows, :] = jnp.where(in_group, back, back_s[out_rows, :])
            gate_rows = jnp.where(in_group, gate_all[start : start + rows], jnp.zeros((), jnp.bfloat16))
            flip_start = (block_count - 1 - blk) * rows
            part = lax.dot_general(
                gate_rows,
                kv_flipped[flip_start : flip_start + span],
                (((1,), (1,)), ((), ())),
                preferred_element_type=jnp.float32,
            )
            cross = part if cross is None else cross + part
        rolled = pltpu.roll(cross, 0, 1, stride=1, stride_axis=0)
        taps_ref[pl.ds(group, 1), :] = jnp.sum(rolled[:, span - rows :], axis=0, keepdims=True)
    back_all = back_s[...]
    grads_ref[0] = (gy_ref[...].astype(jnp.float32) * mixed_s[...]).astype(jnp.bfloat16)
    grads_ref[1] = (back_all * value_ref[...].astype(jnp.float32)).astype(jnp.bfloat16)
    grads_ref[2] = (back_all * key_ref[...].astype(jnp.float32)).astype(jnp.bfloat16)


def medium_terms(medium_taps, kv_rim, products, gate_grad, gate_rim, grad_out, key_in, value_in):
    tap_count, group_count = medium_taps.shape
    seq_rows, chan_count = products.shape
    group_width = chan_count // group_count
    row_block = tap_count
    span = row_block + tap_count
    padded_rows = seq_rows + tap_count
    group_block = LANE_BLOCK // group_width
    zero_taps = jnp.zeros((group_count, span - tap_count), jnp.float32)
    fwd_taps = jnp.concatenate([jnp.flip(medium_taps, 0).T.astype(jnp.float32), zero_taps], 1)
    bwd_taps = jnp.concatenate([medium_taps.T.astype(jnp.float32), zero_taps], 1)
    taps_spec = pl.BlockSpec((group_block, span), lambda j: (j, 0))
    rim_spec = pl.BlockSpec((kv_rim.shape[0], LANE_BLOCK), lambda j: (0, j))
    row_spec = pl.BlockSpec((seq_rows, LANE_BLOCK), lambda j: (0, j))
    grads, taps_grad = pl.pallas_call(
        medium_kernel,
        grid=(chan_count // LANE_BLOCK,),
        in_specs=[taps_spec, taps_spec, rim_spec, row_spec, row_spec, rim_spec, row_spec, row_spec, row_spec],
        out_specs=[
            pl.BlockSpec((3, seq_rows, LANE_BLOCK), lambda j: (0, 0, j)),
            pl.BlockSpec((group_block, tap_count), lambda j: (j, 0)),
        ],
        out_shape=[
            jax.ShapeDtypeStruct((3, seq_rows, chan_count), jnp.bfloat16),
            jax.ShapeDtypeStruct((group_count, tap_count), jnp.float32),
        ],
        scratch_shapes=[
            pltpu.VMEM((padded_rows, LANE_BLOCK), jnp.float32),
            pltpu.VMEM((padded_rows, LANE_BLOCK), jnp.float32),
            pltpu.VMEM((seq_rows, LANE_BLOCK), jnp.float32),
            pltpu.VMEM((seq_rows, LANE_BLOCK), jnp.float32),
        ],
    )(fwd_taps, bwd_taps, kv_rim, products, gate_grad, gate_rim, grad_out, key_in, value_in)
    return grads, taps_grad.T


def per_device(inputs, upstream, short_filter, medium_filter):
    signal = inputs[0]
    grad_out = upstream[0]
    seq_rows, chan_count = signal.shape
    tap_count = medium_filter.shape[1]
    group_count = medium_filter.shape[2]
    lag_count = short_filter.shape[1] // 3
    group_width = chan_count // group_count
    short_rim = lag_count - 1
    medium_rim = tap_count - 1
    chan_short = jnp.broadcast_to(
        short_filter[0].astype(jnp.float32).reshape(3, lag_count, group_count, 1),
        (3, lag_count, group_count, group_width),
    ).reshape(3, lag_count, chan_count)
    medium_taps = medium_filter[0]
    tap_table = chan_short.reshape(3 * lag_count, chan_count)
    signal_rim = passed_along(signal[seq_rows - short_rim :], "ctx", 1)
    signal_pad = jnp.concatenate([signal_rim, signal], 0)
    query_in, key_in, value_in, products, gate_grad = short_front(tap_table, signal_pad, grad_out)
    kv_rim, gate_rim = passed_along(products[seq_rows - medium_rim :], "ctx", 1), passed_along(
        gate_grad[:medium_rim], "ctx", -1
    )
    feature_grads, taps_grad = medium_terms(
        medium_taps, kv_rim, products, gate_grad, gate_rim, grad_out, key_in, value_in
    )
    feature_rim = passed_along(feature_grads[:, :short_rim], "ctx", -1)
    short_terms = short_partials(signal_pad, feature_grads)
    input_grad = input_grads(tap_table, feature_grads, feature_rim)
    short_grad = short_terms.reshape(3 * lag_count, group_count, group_width).sum(-1)
    short_count = short_grad.shape[0]
    both_part = owned_sum(jnp.concatenate([short_grad, taps_grad], 0), "ctx")
    short_part = both_part[None, :short_count]
    medium_part = both_part[None, short_count:]
    incoming = passed_along(input_grad[None], "section", -1)
    return (incoming, short_part, medium_part)


def solution(mesh):
    in_specs = (
        P("section", "ctx", "dp"),
        P("section", "ctx", "dp"),
        P("section", None, "dp"),
        P("section", None, "dp"),
    )
    out_specs = (
        P("section", "ctx", "dp"),
        P("section", None, ("dp", "ctx")),
        P("section", None, ("dp", "ctx")),
    )
    return jax.shard_map(
        per_device, mesh=mesh, in_specs=in_specs, out_specs=out_specs, check_vma=False
    )
```

```python
import jax
import jax.numpy as jnp
from jax import lax
from jax.experimental import pallas as pl
from jax.experimental.pallas import tpu as pltpu
from jax.sharding import PartitionSpec as P

LANE_BLOCK = 128
SHORT_BLOCK = 256


def passed_along(block, axis, distance):
    devices = range(lax.axis_size(axis))
    route = [(i - distance, i) for i in devices if i - distance in devices]
    return lax.ppermute(block, axis, route)


def owned_sum(partial_terms, axis):
    axis_len = lax.axis_size(axis)
    row_count, col_count = partial_terms.shape
    width = col_count // axis_len
    chunks = partial_terms.reshape(row_count, axis_len, width).transpose(1, 0, 2)
    return jnp.sum(lax.all_to_all(chunks, axis, 0, 0, tiled=False), axis=0)


def front_kernel(taps_ref, sig_ref, gy_ref, q_ref, k_ref, v_ref, kv_ref, gate_ref, xs_ref):
    rows = q_ref.shape[0]
    rim = sig_ref.shape[0] - rows
    lags = rim + 1
    xs_ref[pl.ds(0, rows + rim), :] = sig_ref[...].astype(jnp.float32)
    accs = [None, None, None]
    for offset in range(lags):
        window = xs_ref[pl.ds(rim - offset, rows), :]
        for branch in range(3):
            term = taps_ref[pl.ds(branch * lags + offset, 1), :] * window
            accs[branch] = term if accs[branch] is None else accs[branch] + term
    for acc, out_ref in zip(accs, (q_ref, k_ref, v_ref)):
        out_ref[...] = acc.astype(jnp.bfloat16)
    kv_ref[...] = (k_ref[...].astype(jnp.float32) * v_ref[...].astype(jnp.float32)).astype(
        jnp.bfloat16
    )
    gate_ref[...] = (gy_ref[...].astype(jnp.float32) * q_ref[...].astype(jnp.float32)).astype(
        jnp.bfloat16
    )


def short_front(taps, signal_pad, grad_out):
    padded_rows, chan_count = signal_pad.shape
    rows = grad_out.shape[0]
    tap_rows = taps.shape[0]
    row_spec = pl.BlockSpec((rows, SHORT_BLOCK), lambda j: (0, j))
    shape = jax.ShapeDtypeStruct((rows, chan_count), jnp.bfloat16)
    return pl.pallas_call(
        front_kernel,
        grid=(chan_count // SHORT_BLOCK,),
        in_specs=[
            pl.BlockSpec((tap_rows, SHORT_BLOCK), lambda j: (0, j)),
            pl.BlockSpec((padded_rows, SHORT_BLOCK), lambda j: (0, j)),
            row_spec,
        ],
        out_specs=[row_spec] * 5,
        out_shape=[shape] * 5,
        scratch_shapes=[pltpu.VMEM((padded_rows + 8, SHORT_BLOCK), jnp.float32)],
    )(taps, signal_pad, grad_out)


def input_grad_kernel(taps_ref, grads_ref, rim_ref, ig_ref, gs_ref):
    branches, rows, lanes = grads_ref.shape
    rim = rim_ref.shape[1]
    lags = rim + 1
    for branch in range(branches):
        gs_ref[branch, pl.ds(0, rows), :] = grads_ref[branch].astype(jnp.float32)
        gs_ref[branch, pl.ds(rows, rim), :] = rim_ref[branch].astype(jnp.float32)
    acc = None
    for branch in range(branches):
        for offset in range(lags):
            term = taps_ref[pl.ds(branch * lags + offset, 1), :] * gs_ref[branch, pl.ds(offset, rows), :]
            acc = term if acc is None else acc + term
    ig_ref[...] = acc.astype(jnp.bfloat16)


def short_partial_kernel(sig_ref, grads_ref, sp_ref, xs_ref):
    branches, rows, lanes = grads_ref.shape
    rim = sig_ref.shape[0] - rows
    lags = rim + 1
    xs_ref[pl.ds(0, rows + rim), :] = sig_ref[...].astype(jnp.float32)
    for branch in range(branches):
        grads_f = grads_ref[branch].astype(jnp.float32)
        for offset in range(lags):
            prod = grads_f * xs_ref[pl.ds(rim - offset, rows), :]
            sp_ref[pl.ds(branch * lags + offset, 1), :] = jnp.sum(prod, axis=0, keepdims=True)


def short_partials(signal_pad, feature_grads):
    padded_rows, chan_count = signal_pad.shape
    branches, rows, _ = feature_grads.shape
    tap_rows = branches * (padded_rows - rows + 1)
    return pl.pallas_call(
        short_partial_kernel,
        grid=(chan_count // SHORT_BLOCK,),
        in_specs=[
            pl.BlockSpec((padded_rows, SHORT_BLOCK), lambda j: (0, j)),
            pl.BlockSpec((branches, rows, SHORT_BLOCK), lambda j: (0, 0, j)),
        ],
        out_specs=pl.BlockSpec((tap_rows, SHORT_BLOCK), lambda j: (0, j)),
        out_shape=jax.ShapeDtypeStruct((tap_rows, chan_count), jnp.float32),
        scratch_shapes=[pltpu.VMEM((padded_rows + 8, SHORT_BLOCK), jnp.float32)],
    )(signal_pad, feature_grads)


def input_grads(taps, feature_grads, feature_rim):
    branches, rows, chan_count = feature_grads.shape
    rim = feature_rim.shape[1]
    return pl.pallas_call(
        input_grad_kernel,
        grid=(chan_count // SHORT_BLOCK,),
        in_specs=[
            pl.BlockSpec((taps.shape[0], SHORT_BLOCK), lambda j: (0, j)),
            pl.BlockSpec((branches, rows, SHORT_BLOCK), lambda j: (0, 0, j)),
            pl.BlockSpec((branches, rim, SHORT_BLOCK), lambda j: (0, 0, j)),
        ],
        out_specs=pl.BlockSpec((rows, SHORT_BLOCK), lambda j: (0, j)),
        out_shape=jax.ShapeDtypeStruct((rows, chan_count), jnp.bfloat16),
        scratch_shapes=[pltpu.VMEM((branches, rows + rim + 2, SHORT_BLOCK), jnp.float32)],
    )(taps, feature_grads, feature_rim)


def medium_kernel(
    fwd_ref, bwd_ref, kv_rim_ref, prod_ref, gate_ref, gate_rim_ref, gy_ref, key_ref, value_ref,
    grads_ref, taps_ref, kv_s, gate_s, mixed_s, back_s,
):
    group_block, span = fwd_ref.shape
    rows = taps_ref.shape[1]
    seq_rows, lanes = gy_ref.shape
    block_count = seq_rows // rows
    rim = kv_rim_ref.shape[0]
    padded_rows = kv_s.shape[0]
    kv_s[pl.ds(0, rim), :] = kv_rim_ref[...].astype(jnp.float32)
    kv_s[pl.ds(rim, seq_rows), :] = prod_ref[...].astype(jnp.float32)
    kv_s[pl.ds(rim + seq_rows, padded_rows - rim - seq_rows), :] = jnp.zeros(
        (padded_rows - rim - seq_rows, lanes), jnp.float32
    )
    gate_s[pl.ds(0, seq_rows), :] = gate_ref[...].astype(jnp.float32)
    gate_s[pl.ds(seq_rows, rim), :] = gate_rim_ref[...].astype(jnp.float32)
    gate_s[pl.ds(rim + seq_rows, padded_rows - rim - seq_rows), :] = jnp.zeros(
        (padded_rows - rim - seq_rows, lanes), jnp.float32
    )
    kv_all = kv_s[...].astype(jnp.bfloat16)
    gate_all = gate_s[...].astype(jnp.bfloat16)
    row_id = lax.broadcasted_iota(jnp.int32, (padded_rows, padded_rows), 0)
    col_id = lax.broadcasted_iota(jnp.int32, (padded_rows, padded_rows), 1)
    reversal = (row_id + col_id == padded_rows - 1).astype(jnp.bfloat16)
    kv_flipped = jnp.dot(reversal, kv_all, preferred_element_type=jnp.float32).astype(jnp.bfloat16)
    group_width = lanes // group_block
    lane_group = lax.broadcasted_iota(jnp.int32, (1, lanes), 1) // group_width
    mixed_s[...] = jnp.zeros(mixed_s.shape, mixed_s.dtype)
    back_s[...] = jnp.zeros(back_s.shape, back_s.dtype)
    for group in range(group_block):
        in_group = lane_group == group
        fwd = jnp.broadcast_to(fwd_ref[pl.ds(group, 1), :], (rows, span))
        bwd = jnp.broadcast_to(bwd_ref[pl.ds(group, 1), :], (rows, span))
        fwd_band = pltpu.roll(fwd, 0, 1, stride=1, stride_axis=0).astype(jnp.bfloat16)
        bwd_band = pltpu.roll(bwd, 0, 1, stride=1, stride_axis=0).astype(jnp.bfloat16)
        starts = [blk * rows for blk in range(block_count)]
        kv_windows = jnp.concatenate([kv_all[st : st + span] for st in starts], axis=1)
        gate_windows = jnp.concatenate([gate_all[st : st + span] for st in starts], axis=1)
        mixed = jnp.dot(fwd_band, kv_windows, preferred_element_type=jnp.float32)
        back = jnp.dot(bwd_band, gate_windows, preferred_element_type=jnp.float32)
        for blk, st in enumerate(starts):
            out_rows = pl.ds(st, rows)
            lane_part = slice(blk * lanes, (blk + 1) * lanes)
            mixed_s[out_rows, :] = jnp.where(in_group, mixed[:, lane_part], mixed_s[out_rows, :])
            back_s[out_rows, :] = jnp.where(in_group, back[:, lane_part], back_s[out_rows, :])
        gate_rows = jnp.concatenate(
            [jnp.where(in_group, gate_all[st : st + rows], jnp.zeros((), jnp.bfloat16)) for st in starts],
            axis=1,
        )
        flips = [(block_count - 1 - blk) * rows for blk in range(block_count)]
        flipped = jnp.concatenate([kv_flipped[fs : fs + span] for fs in flips], axis=1)
        cross = lax.dot_general(
            gate_rows, flipped, (((1,), (1,)), ((), ())), preferred_element_type=jnp.float32
        )
        rolled = pltpu.roll(cross, 0, 1, stride=1, stride_axis=0)
        taps_ref[pl.ds(group, 1), :] = jnp.sum(rolled[:, span - rows :], axis=0, keepdims=True)
    back_all = back_s[...]
    grads_ref[0] = (gy_ref[...].astype(jnp.float32) * mixed_s[...]).astype(jnp.bfloat16)
    grads_ref[1] = (back_all * value_ref[...].astype(jnp.float32)).astype(jnp.bfloat16)
    grads_ref[2] = (back_all * key_ref[...].astype(jnp.float32)).astype(jnp.bfloat16)


def medium_terms(medium_taps, kv_rim, products, gate_grad, gate_rim, grad_out, key_in, value_in):
    tap_count, group_count = medium_taps.shape
    seq_rows, chan_count = products.shape
    group_width = chan_count // group_count
    row_block = tap_count
    span = row_block + tap_count
    padded_rows = seq_rows + tap_count
    group_block = LANE_BLOCK // group_width
    zero_taps = jnp.zeros((group_count, span - tap_count), jnp.float32)
    fwd_taps = jnp.concatenate([jnp.flip(medium_taps, 0).T.astype(jnp.float32), zero_taps], 1)
    bwd_taps = jnp.concatenate([medium_taps.T.astype(jnp.float32), zero_taps], 1)
    taps_spec = pl.BlockSpec((group_block, span), lambda j: (j, 0))
    rim_spec = pl.BlockSpec((kv_rim.shape[0], LANE_BLOCK), lambda j: (0, j))
    row_spec = pl.BlockSpec((seq_rows, LANE_BLOCK), lambda j: (0, j))
    grads, taps_grad = pl.pallas_call(
        medium_kernel,
        grid=(chan_count // LANE_BLOCK,),
        in_specs=[taps_spec, taps_spec, rim_spec, row_spec, row_spec, rim_spec, row_spec, row_spec, row_spec],
        out_specs=[
            pl.BlockSpec((3, seq_rows, LANE_BLOCK), lambda j: (0, 0, j)),
            pl.BlockSpec((group_block, tap_count), lambda j: (j, 0)),
        ],
        out_shape=[
            jax.ShapeDtypeStruct((3, seq_rows, chan_count), jnp.bfloat16),
            jax.ShapeDtypeStruct((group_count, tap_count), jnp.float32),
        ],
        scratch_shapes=[
            pltpu.VMEM((padded_rows, LANE_BLOCK), jnp.float32),
            pltpu.VMEM((padded_rows, LANE_BLOCK), jnp.float32),
            pltpu.VMEM((seq_rows, LANE_BLOCK), jnp.float32),
            pltpu.VMEM((seq_rows, LANE_BLOCK), jnp.float32),
        ],
    )(fwd_taps, bwd_taps, kv_rim, products, gate_grad, gate_rim, grad_out, key_in, value_in)
    return grads, taps_grad.T


def per_device(inputs, upstream, short_filter, medium_filter):
    signal = inputs[0]
    grad_out = upstream[0]
    seq_rows, chan_count = signal.shape
    tap_count = medium_filter.shape[1]
    group_count = medium_filter.shape[2]
    lag_count = short_filter.shape[1] // 3
    group_width = chan_count // group_count
    short_rim = lag_count - 1
    medium_rim = tap_count - 1
    chan_short = jnp.broadcast_to(
        short_filter[0].astype(jnp.float32).reshape(3, lag_count, group_count, 1),
        (3, lag_count, group_count, group_width),
    ).reshape(3, lag_count, chan_count)
    medium_taps = medium_filter[0]
    tap_table = chan_short.reshape(3 * lag_count, chan_count)
    signal_rim = passed_along(signal[seq_rows - short_rim :], "ctx", 1)
    signal_pad = jnp.concatenate([signal_rim, signal], 0)
    query_in, key_in, value_in, products, gate_grad = short_front(tap_table, signal_pad, grad_out)
    kv_rim, gate_rim = passed_along(products[seq_rows - medium_rim :], "ctx", 1), passed_along(
        gate_grad[:medium_rim], "ctx", -1
    )
    feature_grads, taps_grad = medium_terms(
        medium_taps, kv_rim, products, gate_grad, gate_rim, grad_out, key_in, value_in
    )
    feature_rim = passed_along(feature_grads[:, :short_rim], "ctx", -1)
    short_terms = short_partials(signal_pad, feature_grads)
    input_grad = input_grads(tap_table, feature_grads, feature_rim)
    short_grad = short_terms.reshape(3 * lag_count, group_count, group_width).sum(-1)
    short_count = short_grad.shape[0]
    both_part = owned_sum(jnp.concatenate([short_grad, taps_grad], 0), "ctx")
    short_part = both_part[None, :short_count]
    medium_part = both_part[None, short_count:]
    incoming = passed_along(input_grad[None], "section", -1)
    return (incoming, short_part, medium_part)


def solution(mesh):
    in_specs = (
        P("section", "ctx", "dp"),
        P("section", "ctx", "dp"),
        P("section", None, "dp"),
        P("section", None, "dp"),
    )
    out_specs = (
        P("section", "ctx", "dp"),
        P("section", None, ("dp", "ctx")),
        P("section", None, ("dp", "ctx")),
    )
    return jax.shard_map(
        per_device, mesh=mesh, in_specs=in_specs, out_specs=out_specs, check_vma=False
    )
```

```python
import jax
import jax.numpy as jnp
from jax import lax
from jax.experimental import pallas as pl
from jax.experimental.pallas import tpu as pltpu
from jax.sharding import PartitionSpec as P

LANE_BLOCK = 128
SHORT_BLOCK = 512


def passed_along(block, axis, distance):
    devices = range(lax.axis_size(axis))
    route = [(i - distance, i) for i in devices if i - distance in devices]
    return lax.ppermute(block, axis, route)


def owned_sum(partial_terms, axis):
    axis_len = lax.axis_size(axis)
    row_count, col_count = partial_terms.shape
    width = col_count // axis_len
    chunks = partial_terms.reshape(row_count, axis_len, width).transpose(1, 0, 2)
    return jnp.sum(lax.all_to_all(chunks, axis, 0, 0, tiled=False), axis=0)


def front_kernel(taps_ref, sig_ref, gy_ref, q_ref, k_ref, v_ref, kv_ref, gate_ref, xs_ref):
    rows = q_ref.shape[0]
    rim = sig_ref.shape[0] - rows
    lags = rim + 1
    xs_ref[pl.ds(0, rows + rim), :] = sig_ref[...].astype(jnp.float32)
    accs = [None, None, None]
    for offset in range(lags):
        window = xs_ref[pl.ds(rim - offset, rows), :]
        for branch in range(3):
            term = taps_ref[pl.ds(branch * lags + offset, 1), :] * window
            accs[branch] = term if accs[branch] is None else accs[branch] + term
    for acc, out_ref in zip(accs, (q_ref, k_ref, v_ref)):
        out_ref[...] = acc.astype(jnp.bfloat16)
    kv_ref[...] = (k_ref[...].astype(jnp.float32) * v_ref[...].astype(jnp.float32)).astype(
        jnp.bfloat16
    )
    gate_ref[...] = (gy_ref[...].astype(jnp.float32) * q_ref[...].astype(jnp.float32)).astype(
        jnp.bfloat16
    )


def short_front(taps, signal_pad, grad_out):
    padded_rows, chan_count = signal_pad.shape
    rows = grad_out.shape[0]
    tap_rows = taps.shape[0]
    row_spec = pl.BlockSpec((rows, SHORT_BLOCK), lambda j: (0, j))
    shape = jax.ShapeDtypeStruct((rows, chan_count), jnp.bfloat16)
    return pl.pallas_call(
        front_kernel,
        grid=(chan_count // SHORT_BLOCK,),
        in_specs=[
            pl.BlockSpec((tap_rows, SHORT_BLOCK), lambda j: (0, j)),
            pl.BlockSpec((padded_rows, SHORT_BLOCK), lambda j: (0, j)),
            row_spec,
        ],
        out_specs=[row_spec] * 5,
        out_shape=[shape] * 5,
        scratch_shapes=[pltpu.VMEM((padded_rows + 8, SHORT_BLOCK), jnp.float32)],
    )(taps, signal_pad, grad_out)


def input_grad_kernel(taps_ref, grads_ref, rim_ref, ig_ref, gs_ref):
    branches, rows, lanes = grads_ref.shape
    rim = rim_ref.shape[1]
    lags = rim + 1
    for branch in range(branches):
        gs_ref[branch, pl.ds(0, rows), :] = grads_ref[branch].astype(jnp.float32)
        gs_ref[branch, pl.ds(rows, rim), :] = rim_ref[branch].astype(jnp.float32)
    acc = None
    for branch in range(branches):
        for offset in range(lags):
            term = taps_ref[pl.ds(branch * lags + offset, 1), :] * gs_ref[branch, pl.ds(offset, rows), :]
            acc = term if acc is None else acc + term
    ig_ref[...] = acc.astype(jnp.bfloat16)


def short_partial_kernel(sig_ref, grads_ref, sp_ref, xs_ref):
    branches, rows, lanes = grads_ref.shape
    rim = sig_ref.shape[0] - rows
    lags = rim + 1
    xs_ref[pl.ds(0, rows + rim), :] = sig_ref[...].astype(jnp.float32)
    for branch in range(branches):
        grads_f = grads_ref[branch].astype(jnp.float32)
        for offset in range(lags):
            prod = grads_f * xs_ref[pl.ds(rim - offset, rows), :]
            sp_ref[pl.ds(branch * lags + offset, 1), :] = jnp.sum(prod, axis=0, keepdims=True)


def short_partials(signal_pad, feature_grads):
    padded_rows, chan_count = signal_pad.shape
    branches, rows, _ = feature_grads.shape
    tap_rows = branches * (padded_rows - rows + 1)
    return pl.pallas_call(
        short_partial_kernel,
        grid=(chan_count // SHORT_BLOCK,),
        in_specs=[
            pl.BlockSpec((padded_rows, SHORT_BLOCK), lambda j: (0, j)),
            pl.BlockSpec((branches, rows, SHORT_BLOCK), lambda j: (0, 0, j)),
        ],
        out_specs=pl.BlockSpec((tap_rows, SHORT_BLOCK), lambda j: (0, j)),
        out_shape=jax.ShapeDtypeStruct((tap_rows, chan_count), jnp.float32),
        scratch_shapes=[pltpu.VMEM((padded_rows + 8, SHORT_BLOCK), jnp.float32)],
    )(signal_pad, feature_grads)


def input_grads(taps, feature_grads, feature_rim):
    branches, rows, chan_count = feature_grads.shape
    rim = feature_rim.shape[1]
    return pl.pallas_call(
        input_grad_kernel,
        grid=(chan_count // SHORT_BLOCK,),
        in_specs=[
            pl.BlockSpec((taps.shape[0], SHORT_BLOCK), lambda j: (0, j)),
            pl.BlockSpec((branches, rows, SHORT_BLOCK), lambda j: (0, 0, j)),
            pl.BlockSpec((branches, rim, SHORT_BLOCK), lambda j: (0, 0, j)),
        ],
        out_specs=pl.BlockSpec((rows, SHORT_BLOCK), lambda j: (0, j)),
        out_shape=jax.ShapeDtypeStruct((rows, chan_count), jnp.bfloat16),
        scratch_shapes=[pltpu.VMEM((branches, rows + rim + 2, SHORT_BLOCK), jnp.float32)],
    )(taps, feature_grads, feature_rim)


def medium_kernel(
    fwd_ref, bwd_ref, kv_rim_ref, prod_ref, gate_ref, gate_rim_ref, gy_ref, key_ref, value_ref,
    grads_ref, taps_ref, kv_s, gate_s, mixed_s, back_s,
):
    group_block, span = fwd_ref.shape
    rows = taps_ref.shape[1]
    seq_rows, lanes = gy_ref.shape
    block_count = seq_rows // rows
    rim = kv_rim_ref.shape[0]
    padded_rows = kv_s.shape[0]
    kv_s[pl.ds(0, rim), :] = kv_rim_ref[...].astype(jnp.float32)
    kv_s[pl.ds(rim, seq_rows), :] = prod_ref[...].astype(jnp.float32)
    kv_s[pl.ds(rim + seq_rows, padded_rows - rim - seq_rows), :] = jnp.zeros(
        (padded_rows - rim - seq_rows, lanes), jnp.float32
    )
    gate_s[pl.ds(0, seq_rows), :] = gate_ref[...].astype(jnp.float32)
    gate_s[pl.ds(seq_rows, rim), :] = gate_rim_ref[...].astype(jnp.float32)
    gate_s[pl.ds(rim + seq_rows, padded_rows - rim - seq_rows), :] = jnp.zeros(
        (padded_rows - rim - seq_rows, lanes), jnp.float32
    )
    kv_all = kv_s[...].astype(jnp.bfloat16)
    gate_all = gate_s[...].astype(jnp.bfloat16)
    row_id = lax.broadcasted_iota(jnp.int32, (padded_rows, padded_rows), 0)
    col_id = lax.broadcasted_iota(jnp.int32, (padded_rows, padded_rows), 1)
    reversal = (row_id + col_id == padded_rows - 1).astype(jnp.bfloat16)
    kv_flipped = jnp.dot(reversal, kv_all, preferred_element_type=jnp.float32).astype(jnp.bfloat16)
    group_width = lanes // group_block
    lane_group = lax.broadcasted_iota(jnp.int32, (1, lanes), 1) // group_width
    mixed_s[...] = jnp.zeros(mixed_s.shape, mixed_s.dtype)
    back_s[...] = jnp.zeros(back_s.shape, back_s.dtype)
    for group in range(group_block):
        in_group = lane_group == group
        fwd = jnp.broadcast_to(fwd_ref[pl.ds(group, 1), :], (rows, span))
        bwd = jnp.broadcast_to(bwd_ref[pl.ds(group, 1), :], (rows, span))
        fwd_band = pltpu.roll(fwd, 0, 1, stride=1, stride_axis=0).astype(jnp.bfloat16)
        bwd_band = pltpu.roll(bwd, 0, 1, stride=1, stride_axis=0).astype(jnp.bfloat16)
        starts = [blk * rows for blk in range(block_count)]
        kv_windows = jnp.concatenate([kv_all[st : st + span] for st in starts], axis=1)
        gate_windows = jnp.concatenate([gate_all[st : st + span] for st in starts], axis=1)
        mixed = jnp.dot(fwd_band, kv_windows, preferred_element_type=jnp.float32)
        back = jnp.dot(bwd_band, gate_windows, preferred_element_type=jnp.float32)
        for blk, st in enumerate(starts):
            out_rows = pl.ds(st, rows)
            lane_part = slice(blk * lanes, (blk + 1) * lanes)
            mixed_s[out_rows, :] = jnp.where(in_group, mixed[:, lane_part], mixed_s[out_rows, :])
            back_s[out_rows, :] = jnp.where(in_group, back[:, lane_part], back_s[out_rows, :])
        gate_rows = jnp.concatenate(
            [jnp.where(in_group, gate_all[st : st + rows], jnp.zeros((), jnp.bfloat16)) for st in starts],
            axis=1,
        )
        flips = [(block_count - 1 - blk) * rows for blk in range(block_count)]
        flipped = jnp.concatenate([kv_flipped[fs : fs + span] for fs in flips], axis=1)
        cross = lax.dot_general(
            gate_rows, flipped, (((1,), (1,)), ((), ())), preferred_element_type=jnp.float32
        )
        rolled = pltpu.roll(cross, 0, 1, stride=1, stride_axis=0)
        taps_ref[pl.ds(group, 1), :] = jnp.sum(rolled[:, span - rows :], axis=0, keepdims=True)
    back_all = back_s[...]
    grads_ref[0] = (gy_ref[...].astype(jnp.float32) * mixed_s[...]).astype(jnp.bfloat16)
    grads_ref[1] = (back_all * value_ref[...].astype(jnp.float32)).astype(jnp.bfloat16)
    grads_ref[2] = (back_all * key_ref[...].astype(jnp.float32)).astype(jnp.bfloat16)


def medium_terms(medium_taps, kv_rim, products, gate_grad, gate_rim, grad_out, key_in, value_in):
    tap_count, group_count = medium_taps.shape
    seq_rows, chan_count = products.shape
    group_width = chan_count // group_count
    row_block = tap_count
    span = row_block + tap_count
    padded_rows = seq_rows + tap_count
    group_block = LANE_BLOCK // group_width
    zero_taps = jnp.zeros((group_count, span - tap_count), jnp.float32)
    fwd_taps = jnp.concatenate([jnp.flip(medium_taps, 0).T.astype(jnp.float32), zero_taps], 1)
    bwd_taps = jnp.concatenate([medium_taps.T.astype(jnp.float32), zero_taps], 1)
    taps_spec = pl.BlockSpec((group_block, span), lambda j: (j, 0))
    rim_spec = pl.BlockSpec((kv_rim.shape[0], LANE_BLOCK), lambda j: (0, j))
    row_spec = pl.BlockSpec((seq_rows, LANE_BLOCK), lambda j: (0, j))
    grads, taps_grad = pl.pallas_call(
        medium_kernel,
        grid=(chan_count // LANE_BLOCK,),
        in_specs=[taps_spec, taps_spec, rim_spec, row_spec, row_spec, rim_spec, row_spec, row_spec, row_spec],
        out_specs=[
            pl.BlockSpec((3, seq_rows, LANE_BLOCK), lambda j: (0, 0, j)),
            pl.BlockSpec((group_block, tap_count), lambda j: (j, 0)),
        ],
        out_shape=[
            jax.ShapeDtypeStruct((3, seq_rows, chan_count), jnp.bfloat16),
            jax.ShapeDtypeStruct((group_count, tap_count), jnp.float32),
        ],
        scratch_shapes=[
            pltpu.VMEM((padded_rows, LANE_BLOCK), jnp.float32),
            pltpu.VMEM((padded_rows, LANE_BLOCK), jnp.float32),
            pltpu.VMEM((seq_rows, LANE_BLOCK), jnp.float32),
            pltpu.VMEM((seq_rows, LANE_BLOCK), jnp.float32),
        ],
    )(fwd_taps, bwd_taps, kv_rim, products, gate_grad, gate_rim, grad_out, key_in, value_in)
    return grads, taps_grad.T


def per_device(inputs, upstream, short_filter, medium_filter):
    signal = inputs[0]
    grad_out = upstream[0]
    seq_rows, chan_count = signal.shape
    tap_count = medium_filter.shape[1]
    group_count = medium_filter.shape[2]
    lag_count = short_filter.shape[1] // 3
    group_width = chan_count // group_count
    short_rim = lag_count - 1
    medium_rim = tap_count - 1
    chan_short = jnp.broadcast_to(
        short_filter[0].astype(jnp.float32).reshape(3, lag_count, group_count, 1),
        (3, lag_count, group_count, group_width),
    ).reshape(3, lag_count, chan_count)
    medium_taps = medium_filter[0]
    tap_table = chan_short.reshape(3 * lag_count, chan_count)
    signal_rim = passed_along(signal[seq_rows - short_rim :], "ctx", 1)
    signal_pad = jnp.concatenate([signal_rim, signal], 0)
    query_in, key_in, value_in, products, gate_grad = short_front(tap_table, signal_pad, grad_out)
    kv_rim, gate_rim = passed_along(products[seq_rows - medium_rim :], "ctx", 1), passed_along(
        gate_grad[:medium_rim], "ctx", -1
    )
    feature_grads, taps_grad = medium_terms(
        medium_taps, kv_rim, products, gate_grad, gate_rim, grad_out, key_in, value_in
    )
    feature_rim = passed_along(feature_grads[:, :short_rim], "ctx", -1)
    short_terms = short_partials(signal_pad, feature_grads)
    input_grad = input_grads(tap_table, feature_grads, feature_rim)
    short_grad = short_terms.reshape(3 * lag_count, group_count, group_width).sum(-1)
    short_count = short_grad.shape[0]
    both_part = owned_sum(jnp.concatenate([short_grad, taps_grad], 0), "ctx")
    short_part = both_part[None, :short_count]
    medium_part = both_part[None, short_count:]
    incoming = passed_along(input_grad[None], "section", -1)
    return (incoming, short_part, medium_part)


def solution(mesh):
    in_specs = (
        P("section", "ctx", "dp"),
        P("section", "ctx", "dp"),
        P("section", None, "dp"),
        P("section", None, "dp"),
    )
    out_specs = (
        P("section", "ctx", "dp"),
        P("section", None, ("dp", "ctx")),
        P("section", None, ("dp", "ctx")),
    )
    return jax.shard_map(
        per_device, mesh=mesh, in_specs=in_specs, out_specs=out_specs, check_vma=False
    )
```
